32 devices in a mesh: groups: 2 (over y), ctx: 4 (over z), sub: 2 (over x), head: 2 (over core).
Axes of the slice: x: 2, y: 2, z: 4, core: 2. Of those that a mesh axis runs over, the one named last changes fastest.
Arguments:
- queries: bfloat16 [32, 10240, 128], P(('sub', 'head'), ('groups', 'ctx')), parts along dimension 1, may hold values from -6 to 6
- keys: bfloat16 [32, 10240, 128], P(('sub', 'head'), ('groups', 'ctx')), parts along dimension 1, may hold values from -6 to 6
- values: bfloat16 [32, 10240, 128], P(('sub', 'head'), ('groups', 'ctx')), parts along dimension 1, may hold values from -90 to 90
- out_grad: bfloat16 [32, 10240, 128], P(('sub', 'head'), ('groups', 'ctx')), parts along dimension 1, may hold values from -6 to 6
- norm_gain: float32 [32, 128], P(('sub', 'head')), may hold values from 0.25 to 1.75
- doc_ids: int32 [40], P(('groups', 'ctx')), parts along dimension 0, may hold values from 0 to 3, never falling along the last dimension, each value on 1 to 10 neighbouring positions
Outputs:
- grad_queries: bfloat16 [32, 10240, 128], P(('sub', 'head'), ('groups', 'ctx')), parts along dimension 1
- grad_keys: bfloat16 [32, 10240, 128], P(('sub', 'head'), ('groups', 'ctx')), parts along dimension 1
- grad_values: bfloat16 [32, 10240, 128], P(('sub', 'head'), ('groups', 'ctx')), parts along dimension 1
The draws below stay inside these ranges and needn't reach their ends.
There are 2 independent parts, one for each index of `groups`. The reference program is written for one: setup_inputs(seed, part) draws one part's arguments, and reference() takes and returns one part's arrays. A program takes and returns all parts, laid end to end along the dimension named above; an argument that names none is the same for every part. Nothing has to cross between parts.
Inputs may be any that keep to these rules, and one draw needn't show every extreme that they name: `doc_ids`: never falls; each of its 4 values labels 1 to 10 consecutive blocks, one value exactly 10.
All inputs are finite; a program needn't handle non-finite values.
Results may differ from the reference program's by a relative error of at most 0.0058.
Values sent between devices are 32-bit elements; how exact they have to be, the bound alone decides.
No kernel may reach another device: no remote copies, remote signals or barrier semaphores. Data moves between devices by JAX's collectives and lax.ppermute only.
A program may use at most 128 MiB of HBM per device.

```python
import math
import jax
import jax.numpy as jnp
import numpy as np
from jax import lax

DH = 128
HEADS = 32
BLOCK = 256
TOKENS = 5120
NB = 20


def draw_queries(key, part):
    sample_key = jax.random.fold_in(key, 0)
    sample = jnp.clip(jax.random.normal(sample_key, (HEADS, TOKENS, DH), jnp.float32), -4.0, 4.0)
    return sample.astype(jnp.bfloat16)


def draw_values(key, part):
    sample_key, column_key = jax.random.split(key, 2)
    head_pos = jnp.arange(HEADS, dtype=jnp.float32)[:, None, None] / (HEADS - 1)
    column = jnp.exp(jax.random.uniform(column_key, (HEADS, 1, DH), jnp.float32, 0.0, math.log(10.0))) / 4.0
    rising = jnp.exp(head_pos * math.log(3.0))
    sample = jnp.clip(jax.random.normal(sample_key, (HEADS, TOKENS, DH), jnp.float32), -4.0, 4.0)
    return (sample * rising * column).astype(jnp.bfloat16)


def levels(key, extent, cuts, least, top_value):
    gain = 1.0
    for axis_at, shards_of in cuts:
        heights = jax.random.uniform(jax.random.fold_in(jax.random.fold_in(key, 6), axis_at), (shards_of,), jnp.float32, least / len(cuts), top_value / len(cuts))
        gain = gain * jnp.repeat(jnp.exp(heights), extent[axis_at] // shards_of).reshape((-1,) + (1,) * (len(extent) - 1 - axis_at))
    return gain


def split_up(amount, total, most, lean):
    loads = [(1 << 20) // math.isqrt(standing ** lean) + 1 for standing in range(2, amount + 1)]
    surplus, holding = total - most - (amount - 1), [1] * (amount - 1)
    while surplus > 0:
        candidates = [i for i in range(amount - 1) if holding[i] < most]
        pool, left = sum([loads[i] for i in candidates]), surplus
        for i in candidates:
            addition = min(most - holding[i], max(1, left * loads[i] // pool), surplus)
            holding[i] = holding[i] + addition
            surplus = surplus - addition
    return np.array([most] + holding)


def uneven_parts(own_key, count, total, limit, lean):
    if count == 2:
        one = jax.random.randint(own_key, (), max(1, total - limit), min(limit, total - 1) + 1)
        return jnp.stack([one, total - one])
    tallies = jnp.asarray(split_up(count, total, limit, lean), jnp.int32)
    couples = (count - 1) // 2
    donor, taker = tallies[1:1 + 2 * couples:2], tallies[2:2 + 2 * couples:2]
    room = jnp.minimum(donor - 1, limit - taker)
    moved = jax.random.randint(jax.random.fold_in(own_key, 1), (couples,), 0, 1 << 20) % (room + 1)
    tallies = tallies.at[1:1 + 2 * couples:2].set(donor - moved).at[2:2 + 2 * couples:2].set(taker + moved)
    return tallies[jax.random.permutation(jax.random.fold_in(own_key, 2), count)]


def normal_values(stream_key, extent, width, reach, pieces=(), kind=jnp.bfloat16):
    result = width * jax.random.normal(stream_key, extent, jnp.float32)
    if pieces:
        result = result * levels(stream_key, extent, pieces, -0.22, 0.18)
    return jnp.clip(result, -reach, reach).astype(kind)


def setup_inputs(seed: int = 0, part: int = 0) -> dict:
    seeds = jax.random.split(jax.random.key(seed), 7)
    own_keys = jax.random.split(jax.random.fold_in(seeds[6], part), 7)
    queries = draw_queries(jax.random.fold_in(jax.random.fold_in(seeds[6], part), 71), part)
    keys = normal_values(own_keys[1], (HEADS, TOKENS, DH), 1.0, 6.0, ((0, 4), (1, 4)))
    values = draw_values(jax.random.fold_in(jax.random.fold_in(seeds[6], part), 71), part)
    out_grad = normal_values(own_keys[3], (HEADS, TOKENS, DH), 1.0, 6.0, ((0, 4), (1, 4)))
    norm_gain = jnp.clip(1.0 + 0.15 * jax.random.normal(seeds[4], (HEADS, DH), jnp.float32), 0.25, 1.75)
    doc_ids = jnp.searchsorted(jnp.cumsum(uneven_parts(own_keys[5], 4, NB, NB // 2, 0)), jnp.arange(NB), side="right").astype(jnp.int32)
    return dict(queries=queries, keys=keys, values=values, out_grad=out_grad, norm_gain=norm_gain, doc_ids=doc_ids)


def reference(queries, keys, values, out_grad, norm_gain, doc_ids):
    row_ids = jnp.arange(BLOCK)
    causal = row_ids[:, None] >= row_ids[None, :]
    block_ids = jnp.arange(NB)
    same_doc = doc_ids[:, None] == doc_ids[None, :]
    earlier_mask = (same_doc & (block_ids[None, :] < block_ids[:, None])).astype(jnp.float32)
    later_mask = (same_doc & (block_ids[None, :] > block_ids[:, None])).astype(jnp.float32)
    block_shape = (NB, BLOCK, DH)
    highest_precision = lax.Precision.HIGHEST

    def forward_parts(q_head, k_head, v_head):
        query_blocks = q_head.reshape(block_shape).astype(jnp.float32)
        key_blocks = k_head.reshape(block_shape).astype(jnp.float32)
        value_blocks = v_head.reshape(block_shape).astype(jnp.float32)
        scores = jnp.einsum('nid,njd->nij', query_blocks, key_blocks, precision=highest_precision)
        block_probs = lax.optimization_barrier(jnp.where(causal, scores, 0.0).astype(jnp.bfloat16)).astype(jnp.float32)
        key_value_block = jnp.einsum('vhr,vha->vra', key_blocks, value_blocks, precision=highest_precision)
        prior_sum = jnp.einsum('bc,cde->bde', earlier_mask, key_value_block, precision=highest_precision)
        preceding_states = lax.optimization_barrier(prior_sum.astype(jnp.bfloat16)).astype(jnp.float32)
        return (query_blocks, key_blocks, value_blocks, block_probs, preceding_states)

    def forward_head(operands):
        query_blocks, key_blocks, value_blocks, block_probs, preceding_states = forward_parts(*operands)
        intra_part = jnp.einsum('nij,njd->nid', block_probs, value_blocks, precision=highest_precision)
        cross_block_part = jnp.einsum('sml,sly->smy', query_blocks, preceding_states, precision=highest_precision)
        return (intra_part + cross_block_part).reshape(TOKENS, DH)
    raw_attn = lax.map(forward_head, (queries, keys, values))
    root_mean = jnp.sqrt(lax.optimization_barrier(jnp.mean(raw_attn * raw_attn, axis=(0, 2))) + 1e-06)
    scaled = norm_gain[:, None, :].astype(jnp.float32) * out_grad.astype(jnp.float32)
    inner_mean = lax.optimization_barrier(jnp.mean(scaled * raw_attn, axis=(0, 2)))
    factor = inner_mean / (root_mean * root_mean)
    d_attn = ((scaled - raw_attn * factor[None, :, None]) / root_mean[None, :, None]).astype(jnp.bfloat16)

    def backward_head(operands):
        q_head, k_head, v_head, d_head = operands
        query_blocks, key_blocks, value_blocks, block_probs, preceding_states = forward_parts(q_head, k_head, v_head)
        output_grad_blocks = d_head.reshape(block_shape).astype(jnp.float32)
        grad_scores = jnp.einsum('nid,njd->nij', output_grad_blocks, value_blocks, precision=highest_precision)
        grad_probs = lax.optimization_barrier(jnp.where(causal, grad_scores, 0.0).astype(jnp.bfloat16)).astype(jnp.float32)
        query_grad_block = jnp.einsum('vhr,vha->vra', query_blocks, output_grad_blocks, precision=highest_precision)
        later_sum = jnp.einsum('bc,cde->bde', later_mask, query_grad_block, precision=highest_precision)
        following_states = lax.optimization_barrier(later_sum.astype(jnp.bfloat16)).astype(jnp.float32)
        query_gradient = jnp.einsum('nij,njd->nid', grad_probs, key_blocks, precision=highest_precision)
        query_gradient = query_gradient + jnp.einsum('jzs,jys->jzy', output_grad_blocks, preceding_states, precision=highest_precision)
        key_gradient = jnp.einsum('nij,nid->njd', grad_probs, query_blocks, precision=highest_precision)
        key_gradient = key_gradient + jnp.einsum('jzs,jys->jzy', value_blocks, following_states, precision=highest_precision)
        value_gradient = jnp.einsum('nij,nid->njd', block_probs, output_grad_blocks, precision=highest_precision)
        value_gradient = value_gradient + jnp.einsum('sml,sly->smy', key_blocks, following_states, precision=highest_precision)
        return (query_gradient.reshape(TOKENS, DH).astype(jnp.bfloat16), key_gradient.reshape(TOKENS, DH).astype(jnp.bfloat16), value_gradient.reshape(TOKENS, DH).astype(jnp.bfloat16))
    grad_queries, grad_keys, grad_values = lax.map(backward_head, (queries, keys, values, d_attn))
    return (grad_queries, grad_keys, grad_values)
```

```python
import jax
import jax.numpy as jnp
from jax import lax
from jax.sharding import PartitionSpec as P


def segmented_scan(doc, state, axis, reverse):
    peers = lax.axis_size(axis)
    index = lax.axis_index(axis)
    none_doc = jnp.float32(-1.0)

    def shift(value, step):
        if reverse:
            pairs = [(j, j - step) for j in range(step, peers)]
        else:
            pairs = [(j, j + step) for j in range(peers - step)]
        return lax.ppermute(value, axis, pairs)

    def combine(near_doc, near_state, far_doc, far_state):
        joined = (near_doc == far_doc).astype(jnp.float32)
        return near_doc, near_state + joined * far_state

    if peers == 1:
        return none_doc, jnp.zeros_like(state)
    got_doc, got_state = shift((doc, state), 1)
    valid = (index >= 1) if not reverse else (index <= peers - 2)
    ex_doc = jnp.where(valid, got_doc, none_doc)
    ex_state = jnp.where(valid, got_state, 0.0)
    in_doc, in_state = combine(doc, state, ex_doc, ex_state)
    covered = 1
    while covered < peers - 1:
        step = covered + 1
        got_doc, got_state = shift((in_doc, in_state), step)
        valid = (index >= step) if not reverse else (index <= peers - 1 - step)
        got_doc = jnp.where(valid, got_doc, none_doc)
        got_state = jnp.where(valid, got_state, 0.0)
        ex_doc, ex_state = combine(ex_doc, ex_state, got_doc, got_state)
        covered = covered + step
        if covered < peers - 1:
            in_doc, in_state = combine(in_doc, in_state, got_doc, got_state)
    return ex_doc, ex_state


def on_device(queries, keys, values, out_grad, norm_gain, doc_ids):
    head_count, tok_count, head_width = queries.shape
    block_count = doc_ids.shape[0]
    block_len = tok_count // block_count
    block_shape = (head_count, block_count, block_len, head_width)
    highest_precision = lax.Precision.HIGHEST
    query_blocks = queries.reshape(block_shape)
    key_blocks = keys.reshape(block_shape)
    value_blocks = values.reshape(block_shape)
    row_ids = lax.broadcasted_iota(jnp.int32, (block_len, block_len), 0)
    col_ids = lax.broadcasted_iota(jnp.int32, (block_len, block_len), 1)
    causal = row_ids >= col_ids
    doc_values = doc_ids.astype(jnp.float32)
    block_pos = jnp.arange(block_count, dtype=jnp.int32)
    same_doc = doc_values[:, None] == doc_values[None, :]
    earlier_mask = (same_doc & (block_pos[None, :] < block_pos[:, None])).astype(jnp.float32)
    later_mask = (same_doc & (block_pos[None, :] > block_pos[:, None])).astype(jnp.float32)
    key_value_block = jnp.einsum(
        "hnid,hnie->hnde", key_blocks, value_blocks, preferred_element_type=jnp.float32
    )
    last_match = (doc_values == doc_values[-1]).astype(jnp.float32)
    device_kv = jnp.einsum("c,hcde->hde", last_match, key_value_block, precision=highest_precision)
    prior_doc, prior_state = segmented_scan(doc_values[-1], device_kv, "ctx", False)
    scores = jnp.einsum(
        "hnid,hnjd->hnij", query_blocks, key_blocks, preferred_element_type=jnp.float32
    )
    block_probs = jnp.where(causal, scores, 0.0).astype(jnp.bfloat16)
    intra_part = jnp.einsum(
        "hnij,hnjd->hnid", block_probs, value_blocks, preferred_element_type=jnp.float32
    )
    local_prefix = jnp.einsum(
        "bc,hcde->hbde", earlier_mask, key_value_block, precision=highest_precision
    )
    prior_match = (doc_values == prior_doc).astype(jnp.float32)
    entering = prior_match[None, :, None, None] * prior_state[:, None, :, :]
    preceding_states = (local_prefix + entering).astype(jnp.bfloat16)
    cross_block_part = jnp.einsum(
        "hnid,hnde->hnie", query_blocks, preceding_states, preferred_element_type=jnp.float32
    )
    raw_attn = (intra_part + cross_block_part).reshape(head_count, tok_count, head_width)
    feature_count = head_count * head_width * lax.axis_size(("sub", "head"))
    scaled = norm_gain[:, None, :] * out_grad.astype(jnp.float32)
    local_sums = jnp.stack(
        [jnp.sum(raw_attn * raw_attn, axis=(0, 2)), jnp.sum(scaled * raw_attn, axis=(0, 2))]
    )
    total_sums = lax.psum(local_sums, ("sub", "head"))
    root_mean = jnp.sqrt(total_sums[0] / feature_count + 1e-06)
    inner_mean = total_sums[1] / feature_count
    factor = inner_mean / (root_mean * root_mean)
    d_attn = (
        (scaled - raw_attn * factor[None, :, None]) / root_mean[None, :, None]
    ).astype(jnp.bfloat16)
    output_grad_blocks = d_attn.reshape(block_shape)
    query_grad_block = jnp.einsum(
        "hnid,hnie->hnde", query_blocks, output_grad_blocks, preferred_element_type=jnp.float32
    )
    first_match = (doc_values == doc_values[0]).astype(jnp.float32)
    device_qd = jnp.einsum(
        "c,hcde->hde", first_match, query_grad_block, precision=highest_precision
    )
    next_doc, next_state = segmented_scan(doc_values[0], device_qd, "ctx", True)
    grad_scores = jnp.einsum(
        "hnid,hnjd->hnij", output_grad_blocks, value_blocks, preferred_element_type=jnp.float32
    )
    grad_probs = jnp.where(causal, grad_scores, 0.0).astype(jnp.bfloat16)
    query_gradient = jnp.einsum(
        "hnij,hnjd->hnid", grad_probs, key_blocks, preferred_element_type=jnp.float32
    )
    key_gradient = jnp.einsum(
        "hnij,hnid->hnjd", grad_probs, query_blocks, preferred_element_type=jnp.float32
    )
    value_gradient = jnp.einsum(
        "hnij,hnid->hnjd", block_probs, output_grad_blocks, preferred_element_type=jnp.float32
    )
    local_suffix = jnp.einsum(
        "bc,hcde->hbde", later_mask, query_grad_block, precision=highest_precision
    )
    next_match = (doc_values == next_doc).astype(jnp.float32)
    leaving = next_match[None, :, None, None] * next_state[:, None, :, :]
    following_states = (local_suffix + leaving).astype(jnp.bfloat16)
    query_gradient = query_gradient + jnp.einsum(
        "hnie,hnde->hnid", output_grad_blocks, preceding_states, preferred_element_type=jnp.float32
    )
    key_gradient = key_gradient + jnp.einsum(
        "hnie,hnde->hnid", value_blocks, following_states, preferred_element_type=jnp.float32
    )
    value_gradient = value_gradient + jnp.einsum(
        "hnid,hnde->hnie", key_blocks, following_states, preferred_element_type=jnp.float32
    )
    out_shape = (head_count, tok_count, head_width)
    return (
        query_gradient.reshape(out_shape).astype(jnp.bfloat16),
        key_gradient.reshape(out_shape).astype(jnp.bfloat16),
        value_gradient.reshape(out_shape).astype(jnp.bfloat16),
    )


def solution(mesh):
    return jax.shard_map(
        on_device,
        mesh=mesh,
        in_specs=(
            P(("sub", "head"), ("groups", "ctx"), None),
            P(("sub", "head"), ("groups", "ctx"), None),
            P(("sub", "head"), ("groups", "ctx"), None),
            P(("sub", "head"), ("groups", "ctx"), None),
            P(("sub", "head"), None),
            P(("groups", "ctx")),
        ),
        out_specs=(
            P(("sub", "head"), ("groups", "ctx"), None),
            P(("sub", "head"), ("groups", "ctx"), None),
            P(("sub", "head"), ("groups", "ctx"), None),
        ),
        check_vma=False,
    )
```

```python
import functools

import jax
import jax.numpy as jnp
from jax import lax
from jax.experimental import pallas as pl
from jax.sharding import PartitionSpec as P

_ROWS_MINOR = (((1,), (1,)), ((), ()))
_ROWS_MAJOR = (((0,), (0,)), ((), ()))


def segmented_scan(doc, state, axis, reverse):
    peers = lax.axis_size(axis)
    index = lax.axis_index(axis)
    none_doc = jnp.float32(-1.0)
    pad = jnp.broadcast_to(doc, (state.shape[0], 8, state.shape[2])).astype(jnp.float32)

    def shift(value_doc, value_state, step):
        if reverse:
            pairs = [(j, j - step) for j in range(step, peers)]
        else:
            pairs = [(j, j + step) for j in range(peers - step)]
        row = jnp.broadcast_to(value_doc, pad.shape)
        got = lax.ppermute(jnp.concatenate([value_state, row], axis=1), axis, pairs)
        valid = (index <= peers - 1 - step) if reverse else (index >= step)
        got_doc = jnp.where(valid, got[0, state.shape[1], 0], none_doc)
        got_state = jnp.where(valid, got[:, : state.shape[1]], 0.0)
        return got_doc, got_state

    def combine(near_doc, near_state, far_doc, far_state):
        joined = (near_doc == far_doc).astype(jnp.float32)
        return near_doc, near_state + joined * far_state

    if peers == 1:
        return none_doc, jnp.zeros_like(state)
    ex_doc, ex_state = shift(doc, state, 1)
    in_doc, in_state = combine(doc, state, ex_doc, ex_state)
    covered = 1
    while covered < peers - 1:
        step = covered + 1
        got_doc, got_state = shift(in_doc, in_state, step)
        ex_doc, ex_state = combine(ex_doc, ex_state, got_doc, got_state)
        covered = covered + step
        if covered < peers - 1:
            in_doc, in_state = combine(in_doc, in_state, got_doc, got_state)
    return ex_doc, ex_state


def _causal(block_len):
    row_ids = lax.broadcasted_iota(jnp.int32, (block_len, block_len), 0)
    col_ids = lax.broadcasted_iota(jnp.int32, (block_len, block_len), 1)
    return row_ids >= col_ids


def forward_kernel(block_len, q_ref, k_ref, v_ref, o_ref):
    causal = _causal(block_len)
    for n in range(q_ref.shape[1] // block_len):
        rows = pl.ds(n * block_len, block_len)
        q, k, v = q_ref[0, rows, :], k_ref[0, rows, :], v_ref[0, rows, :]
        scores = lax.dot_general(q, k, _ROWS_MINOR, preferred_element_type=jnp.float32)
        probs = jnp.where(causal, scores, 0.0).astype(jnp.bfloat16)
        o_ref[0, rows, :] = jnp.dot(probs, v, preferred_element_type=jnp.float32)


def backward_kernel(block_len, q_ref, k_ref, v_ref, d_ref, s_ref, dq_ref, dk_ref, dv_ref):
    causal = _causal(block_len)
    for n in range(q_ref.shape[1] // block_len):
        rows = pl.ds(n * block_len, block_len)
        q, k, v = q_ref[0, rows, :], k_ref[0, rows, :], v_ref[0, rows, :]
        d = d_ref[0, rows, :]
        scores = lax.dot_general(q, k, _ROWS_MINOR, preferred_element_type=jnp.float32)
        probs = jnp.where(causal, scores, 0.0).astype(jnp.bfloat16)
        grad_scores = lax.dot_general(d, v, _ROWS_MINOR, preferred_element_type=jnp.float32)
        grad_probs = jnp.where(causal, grad_scores, 0.0).astype(jnp.bfloat16)
        dq = jnp.dot(grad_probs, k, preferred_element_type=jnp.float32)
        dq = dq + lax.dot_general(d, s_ref[0, n], _ROWS_MINOR, preferred_element_type=jnp.float32)
        dq_ref[0, rows, :] = dq.astype(dq_ref.dtype)
        dk_ref[0, rows, :] = lax.dot_general(
            grad_probs, q, _ROWS_MAJOR, preferred_element_type=jnp.float32
        )
        dv_ref[0, rows, :] = lax.dot_general(
            probs, d, _ROWS_MAJOR, preferred_element_type=jnp.float32
        )


def per_head_call(kernel, inputs, out_dtypes, flops):
    head_count, tok_count, head_width = inputs[0].shape

    def spec(shape):
        return pl.BlockSpec((1,) + shape[1:], lambda h: (h,) + (0,) * (len(shape) - 1))

    in_bytes = sum(x.size * x.dtype.itemsize for x in inputs)
    out_bytes = sum(head_count * tok_count * head_width * jnp.dtype(t).itemsize for t in out_dtypes)
    return pl.pallas_call(
        kernel,
        grid=(head_count,),
        in_specs=[spec(x.shape) for x in inputs],
        out_specs=[spec(inputs[0].shape) for _ in out_dtypes],
        out_shape=[jax.ShapeDtypeStruct(inputs[0].shape, t) for t in out_dtypes],
        cost_estimate=pl.CostEstimate(
            flops=flops, transcendentals=0, bytes_accessed=in_bytes + out_bytes
        ),
    )(*inputs)


def on_device(queries, keys, values, out_grad, norm_gain, doc_ids):
    head_count, tok_count, head_width = queries.shape
    block_count = doc_ids.shape[0]
    block_len = tok_count // block_count
    block_shape = (head_count, block_count, block_len, head_width)
    highest_precision = lax.Precision.HIGHEST
    query_blocks = queries.reshape(block_shape)
    key_blocks = keys.reshape(block_shape)
    value_blocks = values.reshape(block_shape)
    doc_values = doc_ids.astype(jnp.float32)
    block_pos = jnp.arange(block_count, dtype=jnp.int32)
    same_doc = doc_values[:, None] == doc_values[None, :]
    earlier_mask = (same_doc & (block_pos[None, :] < block_pos[:, None])).astype(jnp.float32)
    later_mask = (same_doc & (block_pos[None, :] > block_pos[:, None])).astype(jnp.float32)
    pair_flops = 2 * head_count * block_count * block_len * block_len * head_width
    key_value_block = jnp.einsum(
        "hnid,hnie->hnde", key_blocks, value_blocks, preferred_element_type=jnp.float32
    )
    last_match = (doc_values == doc_values[-1]).astype(jnp.float32)
    device_kv = jnp.einsum("c,hcde->hde", last_match, key_value_block, precision=highest_precision)
    prior_doc, prior_state = segmented_scan(doc_values[-1], device_kv, "ctx", False)
    (intra_part,) = per_head_call(
        functools.partial(forward_kernel, block_len),
        [queries, keys, values],
        [jnp.float32],
        2 * pair_flops,
    )
    local_prefix = jnp.einsum(
        "bc,hcde->hbde", earlier_mask, key_value_block, precision=highest_precision
    )
    prior_match = (doc_values == prior_doc).astype(jnp.float32)
    entering = prior_match[None, :, None, None] * prior_state[:, None, :, :]
    preceding_states = (local_prefix + entering).astype(jnp.bfloat16)
    cross_block_part = jnp.einsum(
        "hnid,hnde->hnie", query_blocks, preceding_states, preferred_element_type=jnp.float32
    )
    raw_attn = intra_part + cross_block_part.reshape(head_count, tok_count, head_width)
    feature_count = head_count * head_width * lax.axis_size(("sub", "head"))
    scaled = norm_gain[:, None, :] * out_grad.astype(jnp.float32)
    local_sums = jnp.stack(
        [jnp.sum(raw_attn * raw_attn, axis=(0, 2)), jnp.sum(scaled * raw_attn, axis=(0, 2))]
    )
    total_sums = lax.psum(local_sums, ("sub", "head"))
    root_mean = jnp.sqrt(total_sums[0] / feature_count + 1e-06)
    inner_mean = total_sums[1] / feature_count
    factor = inner_mean / (root_mean * root_mean)
    d_attn = (
        (scaled - raw_attn * factor[None, :, None]) / root_mean[None, :, None]
    ).astype(jnp.bfloat16)
    output_grad_blocks = d_attn.reshape(block_shape)
    query_grad_block = jnp.einsum(
        "hnid,hnie->hnde", query_blocks, output_grad_blocks, preferred_element_type=jnp.float32
    )
    first_match = (doc_values == doc_values[0]).astype(jnp.float32)
    device_qd = jnp.einsum(
        "c,hcde->hde", first_match, query_grad_block, precision=highest_precision
    )
    next_doc, next_state = segmented_scan(doc_values[0], device_qd, "ctx", True)
    query_gradient, key_intra, value_intra = per_head_call(
        functools.partial(backward_kernel, block_len),
        [queries, keys, values, d_attn, preceding_states],
        [jnp.bfloat16, jnp.float32, jnp.float32],
        5 * pair_flops,
    )
    local_suffix = jnp.einsum(
        "bc,hcde->hbde", later_mask, query_grad_block, precision=highest_precision
    )
    next_match = (doc_values == next_doc).astype(jnp.float32)
    leaving = next_match[None, :, None, None] * next_state[:, None, :, :]
    following_states = (local_suffix + leaving).astype(jnp.bfloat16)
    key_cross = jnp.einsum(
        "hnie,hnde->hnid", value_blocks, following_states, preferred_element_type=jnp.float32
    )
    value_cross = jnp.einsum(
        "hnid,hnde->hnie", key_blocks, following_states, preferred_element_type=jnp.float32
    )
    out_shape = (head_count, tok_count, head_width)
    return (
        query_gradient,
        (key_intra + key_cross.reshape(out_shape)).astype(jnp.bfloat16),
        (value_intra + value_cross.reshape(out_shape)).astype(jnp.bfloat16),
    )


def solution(mesh):
    return jax.shard_map(
        on_device,
        mesh=mesh,
        in_specs=(
            P(("sub", "head"), ("groups", "ctx"), None),
            P(("sub", "head"), ("groups", "ctx"), None),
            P(("sub", "head"), ("groups", "ctx"), None),
            P(("sub", "head"), ("groups", "ctx"), None),
            P(("sub", "head"), None),
            P(("groups", "ctx")),
        ),
        out_specs=(
            P(("sub", "head"), ("groups", "ctx"), None),
            P(("sub", "head"), ("groups", "ctx"), None),
            P(("sub", "head"), ("groups", "ctx"), None),
        ),
        check_vma=False,
    )
```

```python
import functools

import jax
import jax.numpy as jnp
from jax import lax
from jax.experimental import pallas as pl
from jax.sharding import PartitionSpec as P

_ROWS_MINOR = (((1,), (1,)), ((), ()))
_ROWS_MAJOR = (((0,), (0,)), ((), ()))


def segmented_scan(doc, state, axis, reverse, cover):
    peers = lax.axis_size(axis)
    index = lax.axis_index(axis)
    none_doc = jnp.float32(-1.0)
    pad = jnp.broadcast_to(doc, (state.shape[0], 8, state.shape[2])).astype(jnp.float32)

    def shift(value_doc, value_state, step):
        if reverse:
            pairs = [(j, j - step) for j in range(step, peers)]
        else:
            pairs = [(j, j + step) for j in range(peers - step)]
        row = jnp.broadcast_to(value_doc, pad.shape)
        got = lax.ppermute(jnp.concatenate([value_state, row], axis=1), axis, pairs)
        valid = (index <= peers - 1 - step) if reverse else (index >= step)
        got_doc = jnp.where(valid, got[0, state.shape[1], 0], none_doc)
        got_state = jnp.where(valid, got[:, : state.shape[1]], 0.0)
        return got_doc, got_state

    def combine(near_doc, near_state, far_doc, far_state):
        joined = (near_doc == far_doc).astype(jnp.float32)
        return near_doc, near_state + joined * far_state

    if peers == 1:
        return none_doc, jnp.zeros_like(state), cover()
    got_doc, got_state = shift(doc, state, 1)
    covered_value = cover()
    ex_doc, ex_state, covered_value = lax.optimization_barrier((got_doc, got_state, covered_value))
    in_doc, in_state = combine(doc, state, ex_doc, ex_state)
    covered = 1
    while covered < peers - 1:
        step = covered + 1
        got_doc, got_state = shift(in_doc, in_state, step)
        ex_doc, ex_state = combine(ex_doc, ex_state, got_doc, got_state)
        covered = covered + step
        if covered < peers - 1:
            in_doc, in_state = combine(in_doc, in_state, got_doc, got_state)
    return ex_doc, ex_state, covered_value


def _causal(block_len):
    row_ids = lax.broadcasted_iota(jnp.int32, (block_len, block_len), 0)
    col_ids = lax.broadcasted_iota(jnp.int32, (block_len, block_len), 1)
    return row_ids >= col_ids


def forward_kernel(block_len, q_ref, k_ref, v_ref, o_ref):
    causal = _causal(block_len)
    for n in range(q_ref.shape[1] // block_len):
        rows = pl.ds(n * block_len, block_len)
        q, k, v = q_ref[0, rows, :], k_ref[0, rows, :], v_ref[0, rows, :]
        scores = lax.dot_general(q, k, _ROWS_MINOR, preferred_element_type=jnp.float32)
        probs = jnp.where(causal, scores, 0.0).astype(jnp.bfloat16)
        o_ref[0, rows, :] = jnp.dot(probs, v, preferred_element_type=jnp.float32)


def backward_kernel(block_len, q_ref, k_ref, v_ref, d_ref, s_ref, dq_ref, dk_ref, dv_ref):
    causal = _causal(block_len)
    for n in range(q_ref.shape[1] // block_len):
        rows = pl.ds(n * block_len, block_len)
        q, k, v = q_ref[0, rows, :], k_ref[0, rows, :], v_ref[0, rows, :]
        d = d_ref[0, rows, :]
        scores = lax.dot_general(q, k, _ROWS_MINOR, preferred_element_type=jnp.float32)
        probs = jnp.where(causal, scores, 0.0).astype(jnp.bfloat16)
        grad_scores = lax.dot_general(d, v, _ROWS_MINOR, preferred_element_type=jnp.float32)
        grad_probs = jnp.where(causal, grad_scores, 0.0).astype(jnp.bfloat16)
        dq = jnp.dot(grad_probs, k, preferred_element_type=jnp.float32)
        dq = dq + lax.dot_general(d, s_ref[0, n], _ROWS_MINOR, preferred_element_type=jnp.float32)
        dq_ref[0, rows, :] = dq.astype(dq_ref.dtype)
        dk_ref[0, rows, :] = lax.dot_general(
            grad_probs, q, _ROWS_MAJOR, preferred_element_type=jnp.float32
        )
        dv_ref[0, rows, :] = lax.dot_general(
            probs, d, _ROWS_MAJOR, preferred_element_type=jnp.float32
        )


def forward_finish_kernel(block_len, i_ref, q_ref, s_ref, o_ref):
    for n in range(q_ref.shape[1] // block_len):
        rows = pl.ds(n * block_len, block_len)
        o_ref[0, rows, :] = i_ref[0, rows, :] + jnp.dot(
            q_ref[0, rows, :], s_ref[0, n], preferred_element_type=jnp.float32
        )


def backward_finish_kernel(block_len, ik_ref, iv_ref, k_ref, v_ref, s_ref, dk_ref, dv_ref):
    for n in range(k_ref.shape[1] // block_len):
        rows = pl.ds(n * block_len, block_len)
        state = s_ref[0, n]
        dk = ik_ref[0, rows, :] + lax.dot_general(
            v_ref[0, rows, :], state, _ROWS_MINOR, preferred_element_type=jnp.float32
        )
        dv = iv_ref[0, rows, :] + jnp.dot(
            k_ref[0, rows, :], state, preferred_element_type=jnp.float32
        )
        dk_ref[0, rows, :] = dk.astype(dk_ref.dtype)
        dv_ref[0, rows, :] = dv.astype(dv_ref.dtype)


def per_head_call(kernel, inputs, out_dtypes, flops):
    head_count, tok_count, head_width = inputs[0].shape

    def spec(shape):
        return pl.BlockSpec((1,) + shape[1:], lambda h: (h,) + (0,) * (len(shape) - 1))

    in_bytes = sum(x.size * x.dtype.itemsize for x in inputs)
    out_bytes = sum(head_count * tok_count * head_width * jnp.dtype(t).itemsize for t in out_dtypes)
    return pl.pallas_call(
        kernel,
        grid=(head_count,),
        in_specs=[spec(x.shape) for x in inputs],
        out_specs=[spec(inputs[0].shape) for _ in out_dtypes],
        out_shape=[jax.ShapeDtypeStruct(inputs[0].shape, t) for t in out_dtypes],
        cost_estimate=pl.CostEstimate(
            flops=flops, transcendentals=0, bytes_accessed=in_bytes + out_bytes
        ),
    )(*inputs)


def on_device(queries, keys, values, out_grad, norm_gain, doc_ids):
    head_count, tok_count, head_width = queries.shape
    block_count = doc_ids.shape[0]
    block_len = tok_count // block_count
    block_shape = (head_count, block_count, block_len, head_width)
    highest_precision = lax.Precision.HIGHEST
    query_blocks = queries.reshape(block_shape)
    key_blocks = keys.reshape(block_shape)
    value_blocks = values.reshape(block_shape)
    doc_values = doc_ids.astype(jnp.float32)
    block_pos = jnp.arange(block_count, dtype=jnp.int32)
    same_doc = doc_values[:, None] == doc_values[None, :]
    earlier_mask = (same_doc & (block_pos[None, :] < block_pos[:, None])).astype(jnp.float32)
    later_mask = (same_doc & (block_pos[None, :] > block_pos[:, None])).astype(jnp.float32)
    pair_flops = 2 * head_count * block_count * block_len * block_len * head_width
    key_value_block = jnp.einsum(
        "hnid,hnie->hnde", key_blocks, value_blocks, preferred_element_type=jnp.float32
    )
    last_match = (doc_values == doc_values[-1]).astype(jnp.float32)
    device_kv = jnp.einsum("c,hcde->hde", last_match, key_value_block, precision=highest_precision)
    prior_doc, prior_state, intra_part = segmented_scan(
        doc_values[-1],
        device_kv,
        "ctx",
        False,
        lambda: per_head_call(
            functools.partial(forward_kernel, block_len),
            [queries, keys, values],
            [jnp.float32],
            2 * pair_flops,
        )[0],
    )
    local_prefix = jnp.einsum(
        "bc,hcde->hbde", earlier_mask, key_value_block, precision=highest_precision
    )
    prior_match = (doc_values == prior_doc).astype(jnp.float32)
    entering = prior_match[None, :, None, None] * prior_state[:, None, :, :]
    preceding_states = (local_prefix + entering).astype(jnp.bfloat16)
    (raw_attn,) = per_head_call(
        functools.partial(forward_finish_kernel, block_len),
        [intra_part, queries, preceding_states],
        [jnp.float32],
        pair_flops // 2,
    )
    feature_count = head_count * head_width * lax.axis_size(("sub", "head"))
    scaled = norm_gain[:, None, :] * out_grad.astype(jnp.float32)
    local_sums = jnp.stack(
        [jnp.sum(raw_attn * raw_attn, axis=(0, 2)), jnp.sum(scaled * raw_attn, axis=(0, 2))]
    )
    total_sums = lax.psum(local_sums, ("sub", "head"))
    root_mean = jnp.sqrt(total_sums[0] / feature_count + 1e-06)
    inner_mean = total_sums[1] / feature_count
    factor = inner_mean / (root_mean * root_mean)
    d_attn = (
        (scaled - raw_attn * factor[None, :, None]) / root_mean[None, :, None]
    ).astype(jnp.bfloat16)
    output_grad_blocks = d_attn.reshape(block_shape)
    query_grad_block = jnp.einsum(
        "hnid,hnie->hnde", query_blocks, output_grad_blocks, preferred_element_type=jnp.float32
    )
    first_match = (doc_values == doc_values[0]).astype(jnp.float32)
    device_qd = jnp.einsum(
        "c,hcde->hde", first_match, query_grad_block, precision=highest_precision
    )
    next_doc, next_state, (query_gradient, key_intra, value_intra) = segmented_scan(
        doc_values[0],
        device_qd,
        "ctx",
        True,
        lambda: per_head_call(
            functools.partial(backward_kernel, block_len),
            [queries, keys, values, d_attn, preceding_states],
            [jnp.bfloat16, jnp.float32, jnp.float32],
            5 * pair_flops,
        ),
    )
    local_suffix = jnp.einsum(
        "bc,hcde->hbde", later_mask, query_grad_block, precision=highest_precision
    )
    next_match = (doc_values == next_doc).astype(jnp.float32)
    leaving = next_match[None, :, None, None] * next_state[:, None, :, :]
    following_states = (local_suffix + leaving).astype(jnp.bfloat16)
    key_gradient, value_gradient = per_head_call(
        functools.partial(backward_finish_kernel, block_len),
        [key_intra, value_intra, keys, values, following_states],
        [jnp.bfloat16, jnp.bfloat16],
        pair_flops,
    )
    return query_gradient, key_gradient, value_gradient


def solution(mesh):
    return jax.shard_map(
        on_device,
        mesh=mesh,
        in_specs=(
            P(("sub", "head"), ("groups", "ctx"), None),
            P(("sub", "head"), ("groups", "ctx"), None),
            P(("sub", "head"), ("groups", "ctx"), None),
            P(("sub", "head"), ("groups", "ctx"), None),
            P(("sub", "head"), None),
            P(("groups", "ctx")),
        ),
        out_specs=(
            P(("sub", "head"), ("groups", "ctx"), None),
            P(("sub", "head"), ("groups", "ctx"), None),
            P(("sub", "head"), ("groups", "ctx"), None),
        ),
        check_vma=False,
    )
```

```python
import functools
import math

import jax
import jax.numpy as jnp
from jax import lax
from jax.experimental import pallas as pl
from jax.sharding import PartitionSpec as P

_ROWS_MINOR = (((1,), (1,)), ((), ()))
_ROWS_MAJOR = (((0,), (0,)), ((), ()))


def segmented_scan(doc, state, axis, reverse, cover):
    peers = lax.axis_size(axis)
    index = lax.axis_index(axis)
    none_doc = jnp.float32(-1.0)
    pad = jnp.broadcast_to(doc, (state.shape[0], 8, state.shape[2])).astype(jnp.float32)

    def shift(value_doc, value_state, step):
        if reverse:
            pairs = [(j, j - step) for j in range(step, peers)]
        else:
            pairs = [(j, j + step) for j in range(peers - step)]
        row = jnp.broadcast_to(value_doc, pad.shape)
        got = lax.ppermute(jnp.concatenate([value_state, row], axis=1), axis, pairs)
        valid = (index <= peers - 1 - step) if reverse else (index >= step)
        got_doc = jnp.where(valid, got[0, state.shape[1], 0], none_doc)
        got_state = jnp.where(valid, got[:, : state.shape[1]], 0.0)
        return got_doc, got_state

    def combine(near_doc, near_state, far_doc, far_state):
        joined = (near_doc == far_doc).astype(jnp.float32)
        return near_doc, near_state + joined * far_state

    if peers == 1:
        return none_doc, jnp.zeros_like(state), cover()
    got_doc, got_state = shift(doc, state, 1)
    covered_value = cover()
    ex_doc, ex_state, covered_value = lax.optimization_barrier((got_doc, got_state, covered_value))
    in_doc, in_state = combine(doc, state, ex_doc, ex_state)
    covered = 1
    while covered < peers - 1:
        step = covered + 1
        got_doc, got_state = shift(in_doc, in_state, step)
        ex_doc, ex_state = combine(ex_doc, ex_state, got_doc, got_state)
        covered = covered + step
        if covered < peers - 1:
            in_doc, in_state = combine(in_doc, in_state, got_doc, got_state)
    return ex_doc, ex_state, covered_value


def _causal(block_len):
    row_ids = lax.broadcasted_iota(jnp.int32, (block_len, block_len), 0)
    col_ids = lax.broadcasted_iota(jnp.int32, (block_len, block_len), 1)
    return row_ids >= col_ids


def _raw_block(causal, q, k, v, state):
    scores = lax.dot_general(q, k, _ROWS_MINOR, preferred_element_type=jnp.float32)
    probs = jnp.where(causal, scores, 0.0).astype(jnp.bfloat16)
    raw = jnp.dot(probs, v, preferred_element_type=jnp.float32)
    return raw + jnp.dot(q, state, preferred_element_type=jnp.float32)


def forward_kernel(block_len, q_ref, k_ref, v_ref, g_ref, n_ref, s_ref, o_ref):
    causal = _causal(block_len)

    @pl.when(pl.program_id(0) == 0)
    def _():
        o_ref[...] = jnp.zeros_like(o_ref)

    for n in range(q_ref.shape[1] // block_len):
        rows = pl.ds(n * block_len, block_len)
        q, k, v = q_ref[0, rows, :], k_ref[0, rows, :], v_ref[0, rows, :]
        raw = _raw_block(causal, q, k, v, s_ref[0, n])
        scaled = n_ref[0] * g_ref[0, rows, :].astype(jnp.float32)
        o_ref[rows, 0:1] += jnp.sum(raw * raw, axis=1, keepdims=True)
        o_ref[rows, 1:2] += jnp.sum(scaled * raw, axis=1, keepdims=True)


def grad_kernel(block_len, q_ref, k_ref, v_ref, g_ref, n_ref, s_ref, c_ref, d_ref, qd_ref):
    causal = _causal(block_len)
    for n in range(q_ref.shape[1] // block_len):
        rows = pl.ds(n * block_len, block_len)
        q, k, v = q_ref[0, rows, :], k_ref[0, rows, :], v_ref[0, rows, :]
        raw = _raw_block(causal, q, k, v, s_ref[0, n])
        scaled = n_ref[0] * g_ref[0, rows, :].astype(jnp.float32)
        root_mean = c_ref[rows, 0:1]
        factor = c_ref[rows, 1:2]
        d = ((scaled - raw * factor) / root_mean).astype(jnp.bfloat16)
        d_ref[0, rows, :] = d
        qd_ref[0, n] = lax.dot_general(q, d, _ROWS_MAJOR, preferred_element_type=jnp.float32)


def query_grad_kernel(block_len, k_ref, v_ref, d_ref, s_ref, dq_ref):
    causal = _causal(block_len)
    for n in range(k_ref.shape[1] // block_len):
        rows = pl.ds(n * block_len, block_len)
        k, v, d = k_ref[0, rows, :], v_ref[0, rows, :], d_ref[0, rows, :]
        grad_scores = lax.dot_general(d, v, _ROWS_MINOR, preferred_element_type=jnp.float32)
        grad_probs = jnp.where(causal, grad_scores, 0.0).astype(jnp.bfloat16)
        dq = jnp.dot(grad_probs, k, preferred_element_type=jnp.float32)
        dq = dq + lax.dot_general(d, s_ref[0, n], _ROWS_MINOR, preferred_element_type=jnp.float32)
        dq_ref[0, rows, :] = dq.astype(dq_ref.dtype)


def key_value_grad_kernel(block_len, q_ref, k_ref, v_ref, d_ref, s_ref, dk_ref, dv_ref):
    causal = _causal(block_len)
    for n in range(q_ref.shape[1] // block_len):
        rows = pl.ds(n * block_len, block_len)
        q, k, v = q_ref[0, rows, :], k_ref[0, rows, :], v_ref[0, rows, :]
        d = d_ref[0, rows, :]
        state = s_ref[0, n]
        scores = lax.dot_general(q, k, _ROWS_MINOR, preferred_element_type=jnp.float32)
        probs = jnp.where(causal, scores, 0.0).astype(jnp.bfloat16)
        grad_scores = lax.dot_general(d, v, _ROWS_MINOR, preferred_element_type=jnp.float32)
        grad_probs = jnp.where(causal, grad_scores, 0.0).astype(jnp.bfloat16)
        dk = lax.dot_general(grad_probs, q, _ROWS_MAJOR, preferred_element_type=jnp.float32)
        dk = dk + lax.dot_general(v, state, _ROWS_MINOR, preferred_element_type=jnp.float32)
        dv = lax.dot_general(probs, d, _ROWS_MAJOR, preferred_element_type=jnp.float32)
        dv = dv + jnp.dot(k, state, preferred_element_type=jnp.float32)
        dk_ref[0, rows, :] = dk.astype(dk_ref.dtype)
        dv_ref[0, rows, :] = dv.astype(dv_ref.dtype)


def per_head_call(kernel, inputs, outputs, flops):
    def spec(shape, per_head):
        if per_head:
            return pl.BlockSpec((1,) + shape[1:], lambda h: (h,) + (0,) * (len(shape) - 1))
        return pl.BlockSpec(shape, lambda h: (0,) * len(shape))

    head_count = inputs[0][0].shape[0]
    in_bytes = sum(x.size * x.dtype.itemsize for x, _ in inputs)
    out_bytes = sum(math.prod(o.shape) * o.dtype.itemsize for o, _ in outputs)
    return pl.pallas_call(
        kernel,
        grid=(head_count,),
        in_specs=[spec(x.shape, h) for x, h in inputs],
        out_specs=[spec(o.shape, h) for o, h in outputs],
        out_shape=[o for o, _ in outputs],
        cost_estimate=pl.CostEstimate(
            flops=flops, transcendentals=0, bytes_accessed=in_bytes + out_bytes
        ),
    )(*[x for x, _ in inputs])


def on_device(queries, keys, values, out_grad, norm_gain, doc_ids):
    head_count, tok_count, head_width = queries.shape
    block_count = doc_ids.shape[0]
    block_len = tok_count // block_count
    block_shape = (head_count, block_count, block_len, head_width)
    highest_precision = lax.Precision.HIGHEST
    key_blocks = keys.reshape(block_shape)
    value_blocks = values.reshape(block_shape)
    gain = norm_gain.reshape(head_count, 1, head_width)
    doc_values = doc_ids.astype(jnp.float32)
    block_pos = jnp.arange(block_count, dtype=jnp.int32)
    same_doc = doc_values[:, None] == doc_values[None, :]
    earlier_mask = (same_doc & (block_pos[None, :] < block_pos[:, None])).astype(jnp.float32)
    later_mask = (same_doc & (block_pos[None, :] > block_pos[:, None])).astype(jnp.float32)
    pair_flops = 2 * head_count * block_count * block_len * block_len * head_width
    full = jax.ShapeDtypeStruct(queries.shape, jnp.bfloat16)
    state_shape = (head_count, block_count, head_width, head_width)
    key_value_block = jnp.einsum(
        "hnid,hnie->hnde", key_blocks, value_blocks, preferred_element_type=jnp.float32
    )
    last_match = (doc_values == doc_values[-1]).astype(jnp.float32)
    device_kv = jnp.einsum("c,hcde->hde", last_match, key_value_block, precision=highest_precision)
    local_prefix = jnp.einsum(
        "bc,hcde->hbde", earlier_mask, key_value_block, precision=highest_precision
    )
    prior_doc, prior_state, _ = segmented_scan(
        doc_values[-1], device_kv, "ctx", False, lambda: jnp.float32(0.0)
    )
    prior_match = (doc_values == prior_doc).astype(jnp.float32)
    entering = prior_match[None, :, None, None] * prior_state[:, None, :, :]
    preceding_states = (local_prefix + entering).astype(jnp.bfloat16)
    (local_sums,) = per_head_call(
        functools.partial(forward_kernel, block_len),
        [(queries, True), (keys, True), (values, True), (out_grad, True), (gain, True),
         (preceding_states, True)],
        [(jax.ShapeDtypeStruct((tok_count, 2), jnp.float32), False)],
        5 * pair_flops // 2,
    )
    feature_count = head_count * head_width * lax.axis_size(("sub", "head"))
    total_sums = lax.psum(local_sums, ("sub", "head"))
    root_mean = jnp.sqrt(total_sums[:, 0] / feature_count + 1e-06)
    inner_mean = total_sums[:, 1] / feature_count
    factor = inner_mean / (root_mean * root_mean)
    coefs = jnp.stack([root_mean, factor], axis=1)
    d_attn, query_grad_block = per_head_call(
        functools.partial(grad_kernel, block_len),
        [(queries, True), (keys, True), (values, True), (out_grad, True), (gain, True),
         (preceding_states, True), (coefs, False)],
        [(full, True), (jax.ShapeDtypeStruct(state_shape, jnp.float32), True)],
        3 * pair_flops,
    )
    first_match = (doc_values == doc_values[0]).astype(jnp.float32)
    device_qd = jnp.einsum(
        "c,hcde->hde", first_match, query_grad_block, precision=highest_precision
    )
    next_doc, next_state, (query_gradient,) = segmented_scan(
        doc_values[0],
        device_qd,
        "ctx",
        True,
        lambda: per_head_call(
            functools.partial(query_grad_kernel, block_len),
            [(keys, True), (values, True), (d_attn, True), (preceding_states, True)],
            [(full, True)],
            5 * pair_flops // 2,
        ),
    )
    local_suffix = jnp.einsum(
        "bc,hcde->hbde", later_mask, query_grad_block, precision=highest_precision
    )
    next_match = (doc_values == next_doc).astype(jnp.float32)
    leaving = next_match[None, :, None, None] * next_state[:, None, :, :]
    following_states = (local_suffix + leaving).astype(jnp.bfloat16)
    key_gradient, value_gradient = per_head_call(
        functools.partial(key_value_grad_kernel, block_len),
        [(queries, True), (keys, True), (values, True), (d_attn, True),
         (following_states, True)],
        [(full, True), (full, True)],
        5 * pair_flops,
    )
    return query_gradient, key_gradient, value_gradient


def solution(mesh):
    return jax.shard_map(
        on_device,
        mesh=mesh,
        in_specs=(
            P(("sub", "head"), ("groups", "ctx"), None),
            P(("sub", "head"), ("groups", "ctx"), None),
            P(("sub", "head"), ("groups", "ctx"), None),
            P(("sub", "head"), ("groups", "ctx"), None),
            P(("sub", "head"), None),
            P(("groups", "ctx")),
        ),
        out_specs=(
            P(("sub", "head"), ("groups", "ctx"), None),
            P(("sub", "head"), ("groups", "ctx"), None),
            P(("sub", "head"), ("groups", "ctx"), None),
        ),
        check_vma=False,
    )
```

```python
import functools
import math

import jax
import jax.numpy as jnp
from jax import lax
from jax.experimental import pallas as pl
from jax.sharding import PartitionSpec as P

_ROWS_MINOR = (((1,), (1,)), ((), ()))
_ROWS_MAJOR = (((0,), (0,)), ((), ()))


def segmented_scan(doc, state, axis, reverse, reach, cover):
    peers = lax.axis_size(axis)
    index = lax.axis_index(axis)
    none_doc = jnp.float32(-1.0)
    rows = state.shape[1]
    reach = min(reach, peers - 1)

    def pack(value_doc, value_state):
        row = jnp.broadcast_to(value_doc, (state.shape[0], 8, state.shape[2]))
        return jnp.concatenate([value_state, row.astype(jnp.float32)], axis=1)

    def shift(packed, step):
        if reverse:
            pairs = [(j, j - step) for j in range(step, peers)]
        else:
            pairs = [(j, j + step) for j in range(peers - step)]
        return lax.ppermute(packed, axis, pairs), step

    def unpack(got):
        got, step = got
        valid = (index <= peers - 1 - step) if reverse else (index >= step)
        got_doc = jnp.where(valid, got[0, rows, 0], none_doc)
        got_state = jnp.where(valid, got[:, :rows], 0.0)
        return got_doc, got_state

    def combine(near_doc, near_state, far_doc, far_state):
        joined = (near_doc == far_doc).astype(jnp.float32)
        return near_doc, near_state + joined * far_state

    if reach < 1:
        return none_doc, jnp.zeros_like(state), cover()
    packed = pack(doc, state)
    if reach <= 2:
        arrivals = [shift(packed, step) for step in range(1, reach + 1)]
        covered_value = cover()
        arrivals, covered_value = lax.optimization_barrier((arrivals, covered_value))
        ex_doc, ex_state = unpack(arrivals[0])
        for got in arrivals[1:]:
            ex_doc, ex_state = combine(ex_doc, ex_state, *unpack(got))
        return ex_doc, ex_state, covered_value
    got = shift(packed, 1)
    covered_value = cover()
    got, covered_value = lax.optimization_barrier((got, covered_value))
    ex_doc, ex_state = unpack(got)
    in_doc, in_state = combine(doc, state, ex_doc, ex_state)
    covered = 1
    while covered < reach:
        step = covered + 1
        got_doc, got_state = unpack(shift(pack(in_doc, in_state), step))
        ex_doc, ex_state = combine(ex_doc, ex_state, got_doc, got_state)
        covered = covered + step
        if covered < reach:
            in_doc, in_state = combine(in_doc, in_state, got_doc, got_state)
    return ex_doc, ex_state, covered_value


def _causal(block_len):
    row_ids = lax.broadcasted_iota(jnp.int32, (block_len, block_len), 0)
    col_ids = lax.broadcasted_iota(jnp.int32, (block_len, block_len), 1)
    return row_ids >= col_ids


def _raw_block(causal, q, k, v, state):
    scores = lax.dot_general(q, k, _ROWS_MINOR, preferred_element_type=jnp.float32)
    probs = jnp.where(causal, scores, 0.0).astype(jnp.bfloat16)
    raw = jnp.dot(probs, v, preferred_element_type=jnp.float32)
    return raw + jnp.dot(q, state, preferred_element_type=jnp.float32)


def intra_kernel(block_len, q_ref, k_ref, v_ref, o_ref):
    causal = _causal(block_len)
    for n in range(q_ref.shape[1] // block_len):
        rows = pl.ds(n * block_len, block_len)
        q, k, v = q_ref[0, rows, :], k_ref[0, rows, :], v_ref[0, rows, :]
        scores = lax.dot_general(q, k, _ROWS_MINOR, preferred_element_type=jnp.float32)
        probs = jnp.where(causal, scores, 0.0).astype(jnp.bfloat16)
        o_ref[0, rows, :] = jnp.dot(probs, v, preferred_element_type=jnp.float32)


def forward_kernel(block_len, i_ref, q_ref, g_ref, n_ref, s_ref, o_ref):
    @pl.when(pl.program_id(0) == 0)
    def _():
        o_ref[...] = jnp.zeros_like(o_ref)

    for n in range(q_ref.shape[1] // block_len):
        rows = pl.ds(n * block_len, block_len)
        raw = i_ref[0, rows, :] + jnp.dot(
            q_ref[0, rows, :], s_ref[0, n], preferred_element_type=jnp.float32
        )
        scaled = n_ref[0] * g_ref[0, rows, :].astype(jnp.float32)
        o_ref[rows, 0:1] += jnp.sum(raw * raw, axis=1, keepdims=True)
        o_ref[rows, 1:2] += jnp.sum(scaled * raw, axis=1, keepdims=True)


def grad_kernel(block_len, q_ref, k_ref, v_ref, g_ref, n_ref, s_ref, c_ref, d_ref, qd_ref):
    causal = _causal(block_len)
    for n in range(q_ref.shape[1] // block_len):
        rows = pl.ds(n * block_len, block_len)
        q, k, v = q_ref[0, rows, :], k_ref[0, rows, :], v_ref[0, rows, :]
        raw = _raw_block(causal, q, k, v, s_ref[0, n])
        scaled = n_ref[0] * g_ref[0, rows, :].astype(jnp.float32)
        root_mean = c_ref[rows, 0:1]
        factor = c_ref[rows, 1:2]
        d = ((scaled - raw * factor) / root_mean).astype(jnp.bfloat16)
        d_ref[0, rows, :] = d
        qd_ref[0, n] = lax.dot_general(q, d, _ROWS_MAJOR, preferred_element_type=jnp.float32)


def query_grad_kernel(block_len, q_ref, k_ref, v_ref, d_ref, s_ref, dq_ref, dk_ref, dv_ref):
    causal = _causal(block_len)
    for n in range(k_ref.shape[1] // block_len):
        rows = pl.ds(n * block_len, block_len)
        q, k, v = q_ref[0, rows, :], k_ref[0, rows, :], v_ref[0, rows, :]
        d = d_ref[0, rows, :]
        scores = lax.dot_general(q, k, _ROWS_MINOR, preferred_element_type=jnp.float32)
        probs = jnp.where(causal, scores, 0.0).astype(jnp.bfloat16)
        grad_scores = lax.dot_general(d, v, _ROWS_MINOR, preferred_element_type=jnp.float32)
        grad_probs = jnp.where(causal, grad_scores, 0.0).astype(jnp.bfloat16)
        dq = jnp.dot(grad_probs, k, preferred_element_type=jnp.float32)
        dq = dq + lax.dot_general(d, s_ref[0, n], _ROWS_MINOR, preferred_element_type=jnp.float32)
        dq_ref[0, rows, :] = dq.astype(dq_ref.dtype)
        dk_ref[0, rows, :] = lax.dot_general(
            grad_probs, q, _ROWS_MAJOR, preferred_element_type=jnp.float32
        )
        dv_ref[0, rows, :] = lax.dot_general(
            probs, d, _ROWS_MAJOR, preferred_element_type=jnp.float32
        )


def key_value_grad_kernel(block_len, ik_ref, iv_ref, k_ref, v_ref, s_ref, dk_ref, dv_ref):
    for n in range(k_ref.shape[1] // block_len):
        rows = pl.ds(n * block_len, block_len)
        state = s_ref[0, n]
        dk = ik_ref[0, rows, :] + lax.dot_general(
            v_ref[0, rows, :], state, _ROWS_MINOR, preferred_element_type=jnp.float32
        )
        dv = iv_ref[0, rows, :] + jnp.dot(
            k_ref[0, rows, :], state, preferred_element_type=jnp.float32
        )
        dk_ref[0, rows, :] = dk.astype(dk_ref.dtype)
        dv_ref[0, rows, :] = dv.astype(dv_ref.dtype)


def per_head_call(kernel, inputs, outputs, flops):
    def spec(shape, per_head):
        if per_head:
            return pl.BlockSpec((1,) + shape[1:], lambda h: (h,) + (0,) * (len(shape) - 1))
        return pl.BlockSpec(shape, lambda h: (0,) * len(shape))

    head_count = inputs[0][0].shape[0]
    in_bytes = sum(x.size * x.dtype.itemsize for x, _ in inputs)
    out_bytes = sum(math.prod(o.shape) * o.dtype.itemsize for o, _ in outputs)
    return pl.pallas_call(
        kernel,
        grid=(head_count,),
        in_specs=[spec(x.shape, h) for x, h in inputs],
        out_specs=[spec(o.shape, h) for o, h in outputs],
        out_shape=[o for o, _ in outputs],
        cost_estimate=pl.CostEstimate(
            flops=flops, transcendentals=0, bytes_accessed=in_bytes + out_bytes
        ),
    )(*[x for x, _ in inputs])


def on_device(queries, keys, values, out_grad, norm_gain, doc_ids):
    head_count, tok_count, head_width = queries.shape
    block_count = doc_ids.shape[0]
    block_len = tok_count // block_count
    block_shape = (head_count, block_count, block_len, head_width)
    highest_precision = lax.Precision.HIGHEST
    key_blocks = keys.reshape(block_shape)
    value_blocks = values.reshape(block_shape)
    gain = norm_gain.reshape(head_count, 1, head_width)
    doc_values = doc_ids.astype(jnp.float32)
    block_pos = jnp.arange(block_count, dtype=jnp.int32)
    same_doc = doc_values[:, None] == doc_values[None, :]
    earlier_mask = (same_doc & (block_pos[None, :] < block_pos[:, None])).astype(jnp.float32)
    later_mask = (same_doc & (block_pos[None, :] > block_pos[:, None])).astype(jnp.float32)
    pair_flops = 2 * head_count * block_count * block_len * block_len * head_width
    full = jax.ShapeDtypeStruct(queries.shape, jnp.bfloat16)
    state_shape = (head_count, block_count, head_width, head_width)
    key_value_block = jnp.einsum(
        "hnid,hnie->hnde", key_blocks, value_blocks, preferred_element_type=jnp.float32
    )
    last_match = (doc_values == doc_values[-1]).astype(jnp.float32)
    device_kv = jnp.einsum("c,hcde->hde", last_match, key_value_block, precision=highest_precision)
    local_prefix = jnp.einsum(
        "bc,hcde->hbde", earlier_mask, key_value_block, precision=highest_precision
    )
    ctx_size = lax.axis_size("ctx")
    longest_doc = ctx_size * block_count // 2
    reach = (longest_doc - 2) // block_count + 1
    intra_shape = jax.ShapeDtypeStruct(queries.shape, jnp.float32)
    prior_doc, prior_state, intra_part = segmented_scan(
        doc_values[-1],
        device_kv,
        "ctx",
        False,
        reach,
        lambda: per_head_call(
            functools.partial(intra_kernel, block_len),
            [(queries, True), (keys, True), (values, True)],
            [(intra_shape, True)],
            2 * pair_flops,
        )[0],
    )
    prior_match = (doc_values == prior_doc).astype(jnp.float32)
    entering = prior_match[None, :, None, None] * prior_state[:, None, :, :]
    preceding_states = (local_prefix + entering).astype(jnp.bfloat16)
    (local_sums,) = per_head_call(
        functools.partial(forward_kernel, block_len),
        [(intra_part, True), (queries, True), (out_grad, True), (gain, True),
         (preceding_states, True)],
        [(jax.ShapeDtypeStruct((tok_count, 2), jnp.float32), False)],
        pair_flops // 2,
    )
    feature_count = head_count * head_width * lax.axis_size(("sub", "head"))
    total_sums = lax.psum(local_sums, ("sub", "head"))
    root_mean = jnp.sqrt(total_sums[:, 0] / feature_count + 1e-06)
    inner_mean = total_sums[:, 1] / feature_count
    factor = inner_mean / (root_mean * root_mean)
    coefs = jnp.stack([root_mean, factor], axis=1)
    d_attn, query_grad_block = per_head_call(
        functools.partial(grad_kernel, block_len),
        [(queries, True), (keys, True), (values, True), (out_grad, True), (gain, True),
         (preceding_states, True), (coefs, False)],
        [(full, True), (jax.ShapeDtypeStruct(state_shape, jnp.float32), True)],
        3 * pair_flops,
    )
    first_match = (doc_values == doc_values[0]).astype(jnp.float32)
    device_qd = jnp.einsum(
        "c,hcde->hde", first_match, query_grad_block, precision=highest_precision
    )
    next_doc, next_state, (query_gradient, key_intra, value_intra) = segmented_scan(
        doc_values[0],
        device_qd,
        "ctx",
        True,
        reach,
        lambda: per_head_call(
            functools.partial(query_grad_kernel, block_len),
            [(queries, True), (keys, True), (values, True), (d_attn, True),
             (preceding_states, True)],
            [(full, True), (intra_shape, True), (intra_shape, True)],
            5 * pair_flops,
        ),
    )
    local_suffix = jnp.einsum(
        "bc,hcde->hbde", later_mask, query_grad_block, precision=highest_precision
    )
    next_match = (doc_values == next_doc).astype(jnp.float32)
    leaving = next_match[None, :, None, None] * next_state[:, None, :, :]
    following_states = (local_suffix + leaving).astype(jnp.bfloat16)
    key_gradient, value_gradient = per_head_call(
        functools.partial(key_value_grad_kernel, block_len),
        [(key_intra, True), (value_intra, True), (keys, True), (values, True),
         (following_states, True)],
        [(full, True), (full, True)],
        pair_flops,
    )
    return query_gradient, key_gradient, value_gradient


def solution(mesh):
    return jax.shard_map(
        on_device,
        mesh=mesh,
        in_specs=(
            P(("sub", "head"), ("groups", "ctx"), None),
            P(("sub", "head"), ("groups", "ctx"), None),
            P(("sub", "head"), ("groups", "ctx"), None),
            P(("sub", "head"), ("groups", "ctx"), None),
            P(("sub", "head"), None),
            P(("groups", "ctx")),
        ),
        out_specs=(
            P(("sub", "head"), ("groups", "ctx"), None),
            P(("sub", "head"), ("groups", "ctx"), None),
            P(("sub", "head"), ("groups", "ctx"), None),
        ),
        check_vma=False,
    )
```

```python
import functools
import math

import jax
import jax.numpy as jnp
from jax import lax
from jax.experimental import pallas as pl
from jax.sharding import PartitionSpec as P

_ROWS_MINOR = (((1,), (1,)), ((), ()))
_ROWS_MAJOR = (((0,), (0,)), ((), ()))


def segmented_scan(doc, state, axis, reverse, reach, cover):
    peers = lax.axis_size(axis)
    index = lax.axis_index(axis)
    none_doc = jnp.float32(-1.0)
    rows = state.shape[1]
    reach = min(reach, peers - 1)

    def pack(value_doc, value_state):
        row = jnp.broadcast_to(value_doc, (state.shape[0], 8, state.shape[2]))
        return jnp.concatenate([value_state, row.astype(jnp.float32)], axis=1)

    def shift(packed, step):
        if reverse:
            pairs = [(j, j - step) for j in range(step, peers)]
        else:
            pairs = [(j, j + step) for j in range(peers - step)]
        return lax.ppermute(packed, axis, pairs), step

    def unpack(got):
        got, step = got
        valid = (index <= peers - 1 - step) if reverse else (index >= step)
        got_doc = jnp.where(valid, got[0, rows, 0], none_doc)
        got_state = jnp.where(valid, got[:, :rows], 0.0)
        return got_doc, got_state

    def combine(near_doc, near_state, far_doc, far_state):
        joined = (near_doc == far_doc).astype(jnp.float32)
        return near_doc, near_state + joined * far_state

    if reach < 1:
        return none_doc, jnp.zeros_like(state), cover()
    packed = pack(doc, state)
    if reach <= 2:
        got = shift(packed, 1)
        covered_value = cover()
        got, covered_value = lax.optimization_barrier((got, covered_value))
        ex_doc, ex_state = unpack(got)
        if reach == 2:
            in_doc, in_state = combine(doc, state, ex_doc, ex_state)
            ex_doc, ex_state = unpack(shift(pack(in_doc, in_state), 1))
        return ex_doc, ex_state, covered_value
    got = shift(packed, 1)
    covered_value = cover()
    got, covered_value = lax.optimization_barrier((got, covered_value))
    ex_doc, ex_state = unpack(got)
    in_doc, in_state = combine(doc, state, ex_doc, ex_state)
    covered = 1
    while covered < reach:
        step = covered + 1
        got_doc, got_state = unpack(shift(pack(in_doc, in_state), step))
        ex_doc, ex_state = combine(ex_doc, ex_state, got_doc, got_state)
        covered = covered + step
        if covered < reach:
            in_doc, in_state = combine(in_doc, in_state, got_doc, got_state)
    return ex_doc, ex_state, covered_value


def _causal(block_len):
    row_ids = lax.broadcasted_iota(jnp.int32, (block_len, block_len), 0)
    col_ids = lax.broadcasted_iota(jnp.int32, (block_len, block_len), 1)
    return row_ids >= col_ids


def _raw_block(causal, q, k, v, state):
    scores = lax.dot_general(q, k, _ROWS_MINOR, preferred_element_type=jnp.float32)
    probs = jnp.where(causal, scores, 0.0).astype(jnp.bfloat16)
    raw = jnp.dot(probs, v, preferred_element_type=jnp.float32)
    return raw + jnp.dot(q, state, preferred_element_type=jnp.float32)


def intra_kernel(block_len, q_ref, k_ref, v_ref, o_ref):
    causal = _causal(block_len)
    for n in range(q_ref.shape[1] // block_len):
        rows = pl.ds(n * block_len, block_len)
        q, k, v = q_ref[0, rows, :], k_ref[0, rows, :], v_ref[0, rows, :]
        scores = lax.dot_general(q, k, _ROWS_MINOR, preferred_element_type=jnp.float32)
        probs = jnp.where(causal, scores, 0.0).astype(jnp.bfloat16)
        o_ref[0, rows, :] = jnp.dot(probs, v, preferred_element_type=jnp.float32)


def forward_kernel(block_len, i_ref, q_ref, g_ref, n_ref, s_ref, o_ref):
    @pl.when(pl.program_id(0) == 0)
    def _():
        o_ref[...] = jnp.zeros_like(o_ref)

    for n in range(q_ref.shape[1] // block_len):
        rows = pl.ds(n * block_len, block_len)
        raw = i_ref[0, rows, :] + jnp.dot(
            q_ref[0, rows, :], s_ref[0, n], preferred_element_type=jnp.float32
        )
        scaled = n_ref[0] * g_ref[0, rows, :].astype(jnp.float32)
        o_ref[rows, 0:1] += jnp.sum(raw * raw, axis=1, keepdims=True)
        o_ref[rows, 1:2] += jnp.sum(scaled * raw, axis=1, keepdims=True)


def grad_kernel(block_len, q_ref, k_ref, v_ref, g_ref, n_ref, s_ref, c_ref, d_ref, qd_ref):
    causal = _causal(block_len)
    for n in range(q_ref.shape[1] // block_len):
        rows = pl.ds(n * block_len, block_len)
        q, k, v = q_ref[0, rows, :], k_ref[0, rows, :], v_ref[0, rows, :]
        raw = _raw_block(causal, q, k, v, s_ref[0, n])
        scaled = n_ref[0] * g_ref[0, rows, :].astype(jnp.float32)
        root_mean = c_ref[rows, 0:1]
        factor = c_ref[rows, 1:2]
        d = ((scaled - raw * factor) / root_mean).astype(jnp.bfloat16)
        d_ref[0, rows, :] = d
        qd_ref[0, n] = lax.dot_general(q, d, _ROWS_MAJOR, preferred_element_type=jnp.float32)


def query_grad_kernel(block_len, q_ref, k_ref, v_ref, d_ref, s_ref, dq_ref, dk_ref, dv_ref):
    causal = _causal(block_len)
    for n in range(k_ref.shape[1] // block_len):
        rows = pl.ds(n * block_len, block_len)
        q, k, v = q_ref[0, rows, :], k_ref[0, rows, :], v_ref[0, rows, :]
        d = d_ref[0, rows, :]
        scores = lax.dot_general(q, k, _ROWS_MINOR, preferred_element_type=jnp.float32)
        probs = jnp.where(causal, scores, 0.0).astype(jnp.bfloat16)
        grad_scores = lax.dot_general(d, v, _ROWS_MINOR, preferred_element_type=jnp.float32)
        grad_probs = jnp.where(causal, grad_scores, 0.0).astype(jnp.bfloat16)
        dq = jnp.dot(grad_probs, k, preferred_element_type=jnp.float32)
        dq = dq + lax.dot_general(d, s_ref[0, n], _ROWS_MINOR, preferred_element_type=jnp.float32)
        dq_ref[0, rows, :] = dq.astype(dq_ref.dtype)
        dk_ref[0, rows, :] = lax.dot_general(
            grad_probs, q, _ROWS_MAJOR, preferred_element_type=jnp.float32
        )
        dv_ref[0, rows, :] = lax.dot_general(
            probs, d, _ROWS_MAJOR, preferred_element_type=jnp.float32
        )


def key_value_grad_kernel(block_len, ik_ref, iv_ref, k_ref, v_ref, s_ref, dk_ref, dv_ref):
    for n in range(k_ref.shape[1] // block_len):
        rows = pl.ds(n * block_len, block_len)
        state = s_ref[0, n]
        dk = ik_ref[0, rows, :] + lax.dot_general(
            v_ref[0, rows, :], state, _ROWS_MINOR, preferred_element_type=jnp.float32
        )
        dv = iv_ref[0, rows, :] + jnp.dot(
            k_ref[0, rows, :], state, preferred_element_type=jnp.float32
        )
        dk_ref[0, rows, :] = dk.astype(dk_ref.dtype)
        dv_ref[0, rows, :] = dv.astype(dv_ref.dtype)


def per_head_call(kernel, inputs, outputs, flops):
    def spec(shape, per_head):
        if per_head:
            return pl.BlockSpec((1,) + shape[1:], lambda h: (h,) + (0,) * (len(shape) - 1))
        return pl.BlockSpec(shape, lambda h: (0,) * len(shape))

    head_count = inputs[0][0].shape[0]
    in_bytes = sum(x.size * x.dtype.itemsize for x, _ in inputs)
    out_bytes = sum(math.prod(o.shape) * o.dtype.itemsize for o, _ in outputs)
    return pl.pallas_call(
        kernel,
        grid=(head_count,),
        in_specs=[spec(x.shape, h) for x, h in inputs],
        out_specs=[spec(o.shape, h) for o, h in outputs],
        out_shape=[o for o, _ in outputs],
        cost_estimate=pl.CostEstimate(
            flops=flops, transcendentals=0, bytes_accessed=in_bytes + out_bytes
        ),
    )(*[x for x, _ in inputs])


def on_device(queries, keys, values, out_grad, norm_gain, doc_ids):
    head_count, tok_count, head_width = queries.shape
    block_count = doc_ids.shape[0]
    block_len = tok_count // block_count
    block_shape = (head_count, block_count, block_len, head_width)
    highest_precision = lax.Precision.HIGHEST
    key_blocks = keys.reshape(block_shape)
    value_blocks = values.reshape(block_shape)
    gain = norm_gain.reshape(head_count, 1, head_width)
    doc_values = doc_ids.astype(jnp.float32)
    block_pos = jnp.arange(block_count, dtype=jnp.int32)
    same_doc = doc_values[:, None] == doc_values[None, :]
    earlier_mask = (same_doc & (block_pos[None, :] < block_pos[:, None])).astype(jnp.float32)
    later_mask = (same_doc & (block_pos[None, :] > block_pos[:, None])).astype(jnp.float32)
    pair_flops = 2 * head_count * block_count * block_len * block_len * head_width
    full = jax.ShapeDtypeStruct(queries.shape, jnp.bfloat16)
    state_shape = (head_count, block_count, head_width, head_width)
    key_value_block = jnp.einsum(
        "hnid,hnie->hnde", key_blocks, value_blocks, preferred_element_type=jnp.float32
    )
    last_match = (doc_values == doc_values[-1]).astype(jnp.float32)
    device_kv = jnp.einsum("c,hcde->hde", last_match, key_value_block, precision=highest_precision)
    local_prefix = jnp.einsum(
        "bc,hcde->hbde", earlier_mask, key_value_block, precision=highest_precision
    )
    ctx_size = lax.axis_size("ctx")
    longest_doc = ctx_size * block_count // 2
    reach = (longest_doc - 2) // block_count + 1
    intra_shape = jax.ShapeDtypeStruct(queries.shape, jnp.float32)
    prior_doc, prior_state, intra_part = segmented_scan(
        doc_values[-1],
        device_kv,
        "ctx",
        False,
        reach,
        lambda: per_head_call(
            functools.partial(intra_kernel, block_len),
            [(queries, True), (keys, True), (values, True)],
            [(intra_shape, True)],
            2 * pair_flops,
        )[0],
    )
    prior_match = (doc_values == prior_doc).astype(jnp.float32)
    entering = prior_match[None, :, None, None] * prior_state[:, None, :, :]
    preceding_states = (local_prefix + entering).astype(jnp.bfloat16)
    (local_sums,) = per_head_call(
        functools.partial(forward_kernel, block_len),
        [(intra_part, True), (queries, True), (out_grad, True), (gain, True),
         (preceding_states, True)],
        [(jax.ShapeDtypeStruct((tok_count, 2), jnp.float32), False)],
        pair_flops // 2,
    )
    feature_count = head_count * head_width * lax.axis_size(("sub", "head"))
    total_sums = lax.psum(local_sums.T, ("sub", "head"))
    root_mean = jnp.sqrt(total_sums[0] / feature_count + 1e-06)
    inner_mean = total_sums[1] / feature_count
    factor = inner_mean / (root_mean * root_mean)
    coefs = jnp.stack([root_mean, factor], axis=1)
    d_attn, query_grad_block = per_head_call(
        functools.partial(grad_kernel, block_len),
        [(queries, True), (keys, True), (values, True), (out_grad, True), (gain, True),
         (preceding_states, True), (coefs, False)],
        [(full, True), (jax.ShapeDtypeStruct(state_shape, jnp.float32), True)],
        3 * pair_flops,
    )
    first_match = (doc_values == doc_values[0]).astype(jnp.float32)
    device_qd = jnp.einsum(
        "c,hcde->hde", first_match, query_grad_block, precision=highest_precision
    )
    next_doc, next_state, (query_gradient, key_intra, value_intra) = segmented_scan(
        doc_values[0],
        device_qd,
        "ctx",
        True,
        reach,
        lambda: per_head_call(
            functools.partial(query_grad_kernel, block_len),
            [(queries, True), (keys, True), (values, True), (d_attn, True),
             (preceding_states, True)],
            [(full, True), (intra_shape, True), (intra_shape, True)],
            5 * pair_flops,
        ),
    )
    local_suffix = jnp.einsum(
        "bc,hcde->hbde", later_mask, query_grad_block, precision=highest_precision
    )
    next_match = (doc_values == next_doc).astype(jnp.float32)
    leaving = next_match[None, :, None, None] * next_state[:, None, :, :]
    following_states = (local_suffix + leaving).astype(jnp.bfloat16)
    key_gradient, value_gradient = per_head_call(
        functools.partial(key_value_grad_kernel, block_len),
        [(key_intra, True), (value_intra, True), (keys, True), (values, True),
         (following_states, True)],
        [(full, True), (full, True)],
        pair_flops,
    )
    return query_gradient, key_gradient, value_gradient


def solution(mesh):
    return jax.shard_map(
        on_device,
        mesh=mesh,
        in_specs=(
            P(("sub", "head"), ("groups", "ctx"), None),
            P(("sub", "head"), ("groups", "ctx"), None),
            P(("sub", "head"), ("groups", "ctx"), None),
            P(("sub", "head"), ("groups", "ctx"), None),
            P(("sub", "head"), None),
            P(("groups", "ctx")),
        ),
        out_specs=(
            P(("sub", "head"), ("groups", "ctx"), None),
            P(("sub", "head"), ("groups", "ctx"), None),
            P(("sub", "head"), ("groups", "ctx"), None),
        ),
        check_vma=False,
    )
```

```python
import functools
import math

import jax
import jax.numpy as jnp
from jax import lax
from jax.experimental import pallas as pl
from jax.sharding import PartitionSpec as P

_ROWS_MINOR = (((1,), (1,)), ((), ()))
_ROWS_MAJOR = (((0,), (0,)), ((), ()))


def segmented_scan(doc, state, axis, reverse, reach, cover):
    peers = lax.axis_size(axis)
    index = lax.axis_index(axis)
    none_doc = jnp.float32(-1.0)
    rows = state.shape[1]
    reach = min(reach, peers - 1)

    def pack(value_doc, value_state):
        row = jnp.broadcast_to(value_doc, (state.shape[0], 8, state.shape[2]))
        return jnp.concatenate([value_state, row.astype(jnp.float32)], axis=1)

    def shift(packed, step):
        if reverse:
            pairs = [(j, j - step) for j in range(step, peers)]
        else:
            pairs = [(j, j + step) for j in range(peers - step)]
        return lax.ppermute(packed, axis, pairs), step

    def unpack(got):
        got, step = got
        valid = (index <= peers - 1 - step) if reverse else (index >= step)
        got_doc = jnp.where(valid, got[0, rows, 0], none_doc)
        got_state = jnp.where(valid, got[:, :rows], 0.0)
        return got_doc, got_state

    def combine(near_doc, near_state, far_doc, far_state):
        joined = (near_doc == far_doc).astype(jnp.float32)
        return near_doc, near_state + joined * far_state

    if reach < 1:
        return none_doc, jnp.zeros_like(state), cover()
    packed = pack(doc, state)
    if reach <= 2:
        got = shift(packed, 1)
        covered_value = cover()
        got, covered_value = lax.optimization_barrier((got, covered_value))
        ex_doc, ex_state = unpack(got)
        if reach == 2:
            in_doc, in_state = combine(doc, state, ex_doc, ex_state)
            ex_doc, ex_state = unpack(shift(pack(in_doc, in_state), 1))
        return ex_doc, ex_state, covered_value
    got = shift(packed, 1)
    covered_value = cover()
    got, covered_value = lax.optimization_barrier((got, covered_value))
    ex_doc, ex_state = unpack(got)
    in_doc, in_state = combine(doc, state, ex_doc, ex_state)
    covered = 1
    while covered < reach:
        step = covered + 1
        got_doc, got_state = unpack(shift(pack(in_doc, in_state), step))
        ex_doc, ex_state = combine(ex_doc, ex_state, got_doc, got_state)
        covered = covered + step
        if covered < reach:
            in_doc, in_state = combine(in_doc, in_state, got_doc, got_state)
    return ex_doc, ex_state, covered_value


def masked_block_sum(mask, blocks):
    total = mask[0] * blocks[:, 0]
    for c in range(1, blocks.shape[1]):
        total = total + mask[c] * blocks[:, c]
    return total


def masked_block_sums(mask, blocks):
    return jnp.stack([masked_block_sum(mask[b], blocks) for b in range(mask.shape[0])], axis=1)


def _causal(block_len):
    row_ids = lax.broadcasted_iota(jnp.int32, (block_len, block_len), 0)
    col_ids = lax.broadcasted_iota(jnp.int32, (block_len, block_len), 1)
    return row_ids >= col_ids


def _raw_block(causal, q, k, v, state):
    scores = lax.dot_general(q, k, _ROWS_MINOR, preferred_element_type=jnp.float32)
    probs = jnp.where(causal, scores, 0.0).astype(jnp.bfloat16)
    raw = jnp.dot(probs, v, preferred_element_type=jnp.float32)
    return raw + jnp.dot(q, state, preferred_element_type=jnp.float32)


def intra_kernel(block_len, q_ref, k_ref, v_ref, o_ref):
    causal = _causal(block_len)
    for n in range(q_ref.shape[1] // block_len):
        rows = pl.ds(n * block_len, block_len)
        q, k, v = q_ref[0, rows, :], k_ref[0, rows, :], v_ref[0, rows, :]
        scores = lax.dot_general(q, k, _ROWS_MINOR, preferred_element_type=jnp.float32)
        probs = jnp.where(causal, scores, 0.0).astype(jnp.bfloat16)
        o_ref[0, rows, :] = jnp.dot(probs, v, preferred_element_type=jnp.float32)


def forward_kernel(block_len, i_ref, q_ref, g_ref, n_ref, s_ref, o_ref):
    @pl.when(pl.program_id(0) == 0)
    def _():
        o_ref[...] = jnp.zeros_like(o_ref)

    for n in range(q_ref.shape[1] // block_len):
        rows = pl.ds(n * block_len, block_len)
        raw = i_ref[0, rows, :] + jnp.dot(
            q_ref[0, rows, :], s_ref[0, n], preferred_element_type=jnp.float32
        )
        scaled = n_ref[0] * g_ref[0, rows, :].astype(jnp.float32)
        o_ref[rows, 0:1] += jnp.sum(raw * raw, axis=1, keepdims=True)
        o_ref[rows, 1:2] += jnp.sum(scaled * raw, axis=1, keepdims=True)


def grad_kernel(block_len, q_ref, k_ref, v_ref, g_ref, n_ref, s_ref, c_ref, d_ref, qd_ref):
    causal = _causal(block_len)
    for n in range(q_ref.shape[1] // block_len):
        rows = pl.ds(n * block_len, block_len)
        q, k, v = q_ref[0, rows, :], k_ref[0, rows, :], v_ref[0, rows, :]
        raw = _raw_block(causal, q, k, v, s_ref[0, n])
        scaled = n_ref[0] * g_ref[0, rows, :].astype(jnp.float32)
        root_mean = c_ref[rows, 0:1]
        factor = c_ref[rows, 1:2]
        d = ((scaled - raw * factor) / root_mean).astype(jnp.bfloat16)
        d_ref[0, rows, :] = d
        qd_ref[0, n] = lax.dot_general(q, d, _ROWS_MAJOR, preferred_element_type=jnp.float32)


def query_grad_kernel(block_len, q_ref, k_ref, v_ref, d_ref, s_ref, dq_ref, dk_ref, dv_ref):
    causal = _causal(block_len)
    for n in range(k_ref.shape[1] // block_len):
        rows = pl.ds(n * block_len, block_len)
        q, k, v = q_ref[0, rows, :], k_ref[0, rows, :], v_ref[0, rows, :]
        d = d_ref[0, rows, :]
        scores = lax.dot_general(q, k, _ROWS_MINOR, preferred_element_type=jnp.float32)
        probs = jnp.where(causal, scores, 0.0).astype(jnp.bfloat16)
        grad_scores = lax.dot_general(d, v, _ROWS_MINOR, preferred_element_type=jnp.float32)
        grad_probs = jnp.where(causal, grad_scores, 0.0).astype(jnp.bfloat16)
        dq = jnp.dot(grad_probs, k, preferred_element_type=jnp.float32)
        dq = dq + lax.dot_general(d, s_ref[0, n], _ROWS_MINOR, preferred_element_type=jnp.float32)
        dq_ref[0, rows, :] = dq.astype(dq_ref.dtype)
        dk_ref[0, rows, :] = lax.dot_general(
            grad_probs, q, _ROWS_MAJOR, preferred_element_type=jnp.float32
        )
        dv_ref[0, rows, :] = lax.dot_general(
            probs, d, _ROWS_MAJOR, preferred_element_type=jnp.float32
        )


def key_value_grad_kernel(block_len, ik_ref, iv_ref, k_ref, v_ref, s_ref, dk_ref, dv_ref):
    for n in range(k_ref.shape[1] // block_len):
        rows = pl.ds(n * block_len, block_len)
        state = s_ref[0, n]
        dk = ik_ref[0, rows, :] + lax.dot_general(
            v_ref[0, rows, :], state, _ROWS_MINOR, preferred_element_type=jnp.float32
        )
        dv = iv_ref[0, rows, :] + jnp.dot(
            k_ref[0, rows, :], state, preferred_element_type=jnp.float32
        )
        dk_ref[0, rows, :] = dk.astype(dk_ref.dtype)
        dv_ref[0, rows, :] = dv.astype(dv_ref.dtype)


def per_head_call(kernel, inputs, outputs, flops):
    def spec(shape, per_head):
        if per_head:
            return pl.BlockSpec((1,) + shape[1:], lambda h: (h,) + (0,) * (len(shape) - 1))
        return pl.BlockSpec(shape, lambda h: (0,) * len(shape))

    head_count = inputs[0][0].shape[0]
    in_bytes = sum(x.size * x.dtype.itemsize for x, _ in inputs)
    out_bytes = sum(math.prod(o.shape) * o.dtype.itemsize for o, _ in outputs)
    return pl.pallas_call(
        kernel,
        grid=(head_count,),
        in_specs=[spec(x.shape, h) for x, h in inputs],
        out_specs=[spec(o.shape, h) for o, h in outputs],
        out_shape=[o for o, _ in outputs],
        cost_estimate=pl.CostEstimate(
            flops=flops, transcendentals=0, bytes_accessed=in_bytes + out_bytes
        ),
    )(*[x for x, _ in inputs])


def on_device(queries, keys, values, out_grad, norm_gain, doc_ids):
    head_count, tok_count, head_width = queries.shape
    block_count = doc_ids.shape[0]
    block_len = tok_count // block_count
    block_shape = (head_count, block_count, block_len, head_width)
    key_blocks = keys.reshape(block_shape)
    value_blocks = values.reshape(block_shape)
    gain = norm_gain.reshape(head_count, 1, head_width)
    doc_values = doc_ids.astype(jnp.float32)
    block_pos = jnp.arange(block_count, dtype=jnp.int32)
    same_doc = doc_values[:, None] == doc_values[None, :]
    earlier_mask = (same_doc & (block_pos[None, :] < block_pos[:, None])).astype(jnp.float32)
    later_mask = (same_doc & (block_pos[None, :] > block_pos[:, None])).astype(jnp.float32)
    pair_flops = 2 * head_count * block_count * block_len * block_len * head_width
    full = jax.ShapeDtypeStruct(queries.shape, jnp.bfloat16)
    state_shape = (head_count, block_count, head_width, head_width)
    key_value_block = jnp.einsum(
        "hnid,hnie->hnde", key_blocks, value_blocks, preferred_element_type=jnp.float32
    )
    last_match = (doc_values == doc_values[-1]).astype(jnp.float32)
    device_kv = masked_block_sum(last_match, key_value_block)
    local_prefix = masked_block_sums(earlier_mask, key_value_block)
    ctx_size = lax.axis_size("ctx")
    longest_doc = ctx_size * block_count // 2
    reach = (longest_doc - 2) // block_count + 1
    intra_shape = jax.ShapeDtypeStruct(queries.shape, jnp.float32)
    prior_doc, prior_state, intra_part = segmented_scan(
        doc_values[-1],
        device_kv,
        "ctx",
        False,
        reach,
        lambda: per_head_call(
            functools.partial(intra_kernel, block_len),
            [(queries, True), (keys, True), (values, True)],
            [(intra_shape, True)],
            2 * pair_flops,
        )[0],
    )
    prior_match = (doc_values == prior_doc).astype(jnp.float32)
    entering = prior_match[None, :, None, None] * prior_state[:, None, :, :]
    preceding_states = (local_prefix + entering).astype(jnp.bfloat16)
    (local_sums,) = per_head_call(
        functools.partial(forward_kernel, block_len),
        [(intra_part, True), (queries, True), (out_grad, True), (gain, True),
         (preceding_states, True)],
        [(jax.ShapeDtypeStruct((tok_count, 2), jnp.float32), False)],
        pair_flops // 2,
    )
    feature_count = head_count * head_width * lax.axis_size(("sub", "head"))
    total_sums = lax.psum(local_sums.T.reshape(2 * tok_count), ("sub", "head"))
    root_mean = jnp.sqrt(total_sums[:tok_count] / feature_count + 1e-06)
    inner_mean = total_sums[tok_count:] / feature_count
    factor = inner_mean / (root_mean * root_mean)
    coefs = jnp.stack([root_mean, factor], axis=1)
    d_attn, query_grad_block = per_head_call(
        functools.partial(grad_kernel, block_len),
        [(queries, True), (keys, True), (values, True), (out_grad, True), (gain, True),
         (preceding_states, True), (coefs, False)],
        [(full, True), (jax.ShapeDtypeStruct(state_shape, jnp.float32), True)],
        3 * pair_flops,
    )
    first_match = (doc_values == doc_values[0]).astype(jnp.float32)
    device_qd = masked_block_sum(first_match, query_grad_block)
    next_doc, next_state, (query_gradient, key_intra, value_intra) = segmented_scan(
        doc_values[0],
        device_qd,
        "ctx",
        True,
        reach,
        lambda: per_head_call(
            functools.partial(query_grad_kernel, block_len),
            [(queries, True), (keys, True), (values, True), (d_attn, True),
             (preceding_states, True)],
            [(full, True), (intra_shape, True), (intra_shape, True)],
            5 * pair_flops,
        ),
    )
    local_suffix = masked_block_sums(later_mask, query_grad_block)
    next_match = (doc_values == next_doc).astype(jnp.float32)
    leaving = next_match[None, :, None, None] * next_state[:, None, :, :]
    following_states = (local_suffix + leaving).astype(jnp.bfloat16)
    key_gradient, value_gradient = per_head_call(
        functools.partial(key_value_grad_kernel, block_len),
        [(key_intra, True), (value_intra, True), (keys, True), (values, True),
         (following_states, True)],
        [(full, True), (full, True)],
        pair_flops,
    )
    return query_gradient, key_gradient, value_gradient


def solution(mesh):
    return jax.shard_map(
        on_device,
        mesh=mesh,
        in_specs=(
            P(("sub", "head"), ("groups", "ctx"), None),
            P(("sub", "head"), ("groups", "ctx"), None),
            P(("sub", "head"), ("groups", "ctx"), None),
            P(("sub", "head"), ("groups", "ctx"), None),
            P(("sub", "head"), None),
            P(("groups", "ctx")),
        ),
        out_specs=(
            P(("sub", "head"), ("groups", "ctx"), None),
            P(("sub", "head"), ("groups", "ctx"), None),
            P(("sub", "head"), ("groups", "ctx"), None),
        ),
        check_vma=False,
    )
```

```python
import functools
import math

import jax
import jax.numpy as jnp
from jax import lax
from jax.experimental import pallas as pl
from jax.sharding import PartitionSpec as P

_ROWS_MINOR = (((1,), (1,)), ((), ()))
_ROWS_MAJOR = (((0,), (0,)), ((), ()))


def _causal(block_len):
    row_ids = lax.broadcasted_iota(jnp.int32, (block_len, block_len), 0)
    col_ids = lax.broadcasted_iota(jnp.int32, (block_len, block_len), 1)
    return row_ids >= col_ids


def _sum_blocks(mask_ref, first_row, parts):
    total = mask_ref[first_row : first_row + 1, :] * parts[0]
    for c in range(1, len(parts)):
        total = total + mask_ref[first_row + c : first_row + c + 1, :] * parts[c]
    return total


def _carried(state_ref, doc_ref, n, carry_ref):
    width = carry_ref.shape[2]
    joined = doc_ref[n : n + 1, :] == carry_ref[0, width : width + 1, :]
    total = state_ref[0, n] + jnp.where(joined, carry_ref[0, :width, :], 0.0)
    return total.astype(jnp.bfloat16)


def state_kernel(block_len, k_ref, v_ref, pair_ref, end_ref, row_ref, prefix_ref, pay_ref):
    count = k_ref.shape[1] // block_len
    width = k_ref.shape[2]
    parts = []
    for n in range(count):
        rows = pl.ds(n * block_len, block_len)
        parts.append(
            lax.dot_general(
                k_ref[0, rows, :], v_ref[0, rows, :], _ROWS_MAJOR,
                preferred_element_type=jnp.float32,
            )
        )
    for b in range(count):
        prefix_ref[0, b] = _sum_blocks(pair_ref, b * count, parts)
    pay_ref[0, :width, :] = _sum_blocks(end_ref, 0, parts)
    pay_ref[0, width:, :] = row_ref[...]


def combine_kernel(near_ref, far_ref, o_ref):
    width = near_ref.shape[2]
    joined = near_ref[0, width : width + 1, :] == far_ref[0, width : width + 1, :]
    o_ref[0, :width, :] = near_ref[0, :width, :] + jnp.where(
        joined, far_ref[0, :width, :], 0.0
    )
    o_ref[0, width:, :] = near_ref[0, width:, :]


def intra_kernel(block_len, q_ref, k_ref, v_ref, o_ref):
    causal = _causal(block_len)
    for n in range(q_ref.shape[1] // block_len):
        rows = pl.ds(n * block_len, block_len)
        q, k, v = q_ref[0, rows, :], k_ref[0, rows, :], v_ref[0, rows, :]
        scores = lax.dot_general(q, k, _ROWS_MINOR, preferred_element_type=jnp.float32)
        probs = jnp.where(causal, scores, 0.0).astype(jnp.bfloat16)
        o_ref[0, rows, :] = jnp.dot(probs, v, preferred_element_type=jnp.float32)


def forward_kernel(
    block_len, i_ref, q_ref, g_ref, n_ref, prefix_ref, carry_ref, doc_ref, o_ref, s_ref
):
    @pl.when(pl.program_id(0) == 0)
    def _():
        o_ref[...] = jnp.zeros_like(o_ref)

    for n in range(q_ref.shape[1] // block_len):
        rows = pl.ds(n * block_len, block_len)
        state = _carried(prefix_ref, doc_ref, n, carry_ref)
        s_ref[0, n] = state
        raw = i_ref[0, rows, :] + jnp.dot(
            q_ref[0, rows, :], state, preferred_element_type=jnp.float32
        )
        scaled = n_ref[0] * g_ref[0, rows, :].astype(jnp.float32)
        o_ref[rows, 0:1] += jnp.sum(raw * raw, axis=1, keepdims=True)
        o_ref[rows, 1:2] += jnp.sum(scaled * raw, axis=1, keepdims=True)


def grad_kernel(
    block_len, q_ref, k_ref, v_ref, g_ref, n_ref, s_ref, c_ref, pair_ref, end_ref, row_ref,
    d_ref, suffix_ref, pay_ref,
):
    causal = _causal(block_len)
    count = q_ref.shape[1] // block_len
    width = q_ref.shape[2]
    parts = []
    for n in range(count):
        rows = pl.ds(n * block_len, block_len)
        q, k, v = q_ref[0, rows, :], k_ref[0, rows, :], v_ref[0, rows, :]
        scores = lax.dot_general(q, k, _ROWS_MINOR, preferred_element_type=jnp.float32)
        probs = jnp.where(causal, scores, 0.0).astype(jnp.bfloat16)
        raw = jnp.dot(probs, v, preferred_element_type=jnp.float32)
        raw = raw + jnp.dot(q, s_ref[0, n], preferred_element_type=jnp.float32)
        scaled = n_ref[0] * g_ref[0, rows, :].astype(jnp.float32)
        root_mean = c_ref[rows, 0:1]
        factor = c_ref[rows, 1:2]
        d = ((scaled - raw * factor) / root_mean).astype(jnp.bfloat16)
        d_ref[0, rows, :] = d
        parts.append(lax.dot_general(q, d, _ROWS_MAJOR, preferred_element_type=jnp.float32))
    for b in range(count):
        suffix_ref[0, b] = _sum_blocks(pair_ref, b * count, parts)
    pay_ref[0, :width, :] = _sum_blocks(end_ref, 0, parts)
    pay_ref[0, width:, :] = row_ref[...]


def query_grad_kernel(block_len, q_ref, k_ref, v_ref, d_ref, s_ref, dq_ref, dk_ref, dv_ref):
    causal = _causal(block_len)
    for n in range(k_ref.shape[1] // block_len):
        rows = pl.ds(n * block_len, block_len)
        q, k, v = q_ref[0, rows, :], k_ref[0, rows, :], v_ref[0, rows, :]
        d = d_ref[0, rows, :]
        scores = lax.dot_general(q, k, _ROWS_MINOR, preferred_element_type=jnp.float32)
        probs = jnp.where(causal, scores, 0.0).astype(jnp.bfloat16)
        grad_scores = lax.dot_general(d, v, _ROWS_MINOR, preferred_element_type=jnp.float32)
        grad_probs = jnp.where(causal, grad_scores, 0.0).astype(jnp.bfloat16)
        dq = jnp.dot(grad_probs, k, preferred_element_type=jnp.float32)
        dq = dq + lax.dot_general(d, s_ref[0, n], _ROWS_MINOR, preferred_element_type=jnp.float32)
        dq_ref[0, rows, :] = dq.astype(dq_ref.dtype)
        dk_ref[0, rows, :] = lax.dot_general(
            grad_probs, q, _ROWS_MAJOR, preferred_element_type=jnp.float32
        )
        dv_ref[0, rows, :] = lax.dot_general(
            probs, d, _ROWS_MAJOR, preferred_element_type=jnp.float32
        )


def key_value_grad_kernel(
    block_len, ik_ref, iv_ref, k_ref, v_ref, suffix_ref, carry_ref, doc_ref, dk_ref, dv_ref
):
    for n in range(k_ref.shape[1] // block_len):
        rows = pl.ds(n * block_len, block_len)
        state = _carried(suffix_ref, doc_ref, n, carry_ref)
        dk = ik_ref[0, rows, :] + lax.dot_general(
            v_ref[0, rows, :], state, _ROWS_MINOR, preferred_element_type=jnp.float32
        )
        dv = iv_ref[0, rows, :] + jnp.dot(
            k_ref[0, rows, :], state, preferred_element_type=jnp.float32
        )
        dk_ref[0, rows, :] = dk.astype(dk_ref.dtype)
        dv_ref[0, rows, :] = dv.astype(dv_ref.dtype)


def per_head_call(kernel, inputs, outputs, flops):
    def spec(shape, per_head):
        if per_head:
            return pl.BlockSpec((1,) + shape[1:], lambda h: (h,) + (0,) * (len(shape) - 1))
        return pl.BlockSpec(shape, lambda h: (0,) * len(shape))

    head_count = inputs[0][0].shape[0]
    in_bytes = sum(x.size * x.dtype.itemsize for x, _ in inputs)
    out_bytes = sum(math.prod(o.shape) * o.dtype.itemsize for o, _ in outputs)
    return pl.pallas_call(
        kernel,
        grid=(head_count,),
        in_specs=[spec(x.shape, h) for x, h in inputs],
        out_specs=[spec(o.shape, h) for o, h in outputs],
        out_shape=[o for o, _ in outputs],
        cost_estimate=pl.CostEstimate(
            flops=flops, transcendentals=0, bytes_accessed=in_bytes + out_bytes
        ),
    )(*[x for x, _ in inputs])


def combine(near, far):
    return per_head_call(
        combine_kernel, [(near, True), (far, True)], [(near, True)], 2 * near.size
    )[0]


def carry(payload, axis, reverse, reach, cover):
    peers = lax.axis_size(axis)
    reach = min(reach, peers - 1)

    def shift(value, step):
        if reverse:
            pairs = [(j, j - step) for j in range(step, peers)]
        else:
            pairs = [(j, j + step) for j in range(peers - step)]
        return lax.ppermute(value, axis, pairs)

    if reach < 1:
        return jnp.zeros_like(payload), cover()
    got = shift(payload, 1)
    covered_value = cover()
    got, covered_value = lax.optimization_barrier((got, covered_value))
    if reach <= 2:
        if reach == 2:
            got = shift(combine(payload, got), 1)
        return got, covered_value
    earlier, inclusive = got, combine(payload, got)
    covered = 1
    while covered < reach:
        step = covered + 1
        got = shift(inclusive, step)
        earlier = combine(earlier, got)
        covered = covered + step
        if covered < reach:
            inclusive = combine(inclusive, got)
    return earlier, covered_value


def on_device(queries, keys, values, out_grad, norm_gain, doc_ids):
    head_count, tok_count, head_width = queries.shape
    block_count = doc_ids.shape[0]
    block_len = tok_count // block_count
    gain = norm_gain.reshape(head_count, 1, head_width)
    doc_values = doc_ids.astype(jnp.float32)
    block_pos = jnp.arange(block_count, dtype=jnp.int32)
    same_doc = doc_values[:, None] == doc_values[None, :]
    earlier_mask = (same_doc & (block_pos[None, :] < block_pos[:, None])).astype(jnp.float32)
    later_mask = (same_doc & (block_pos[None, :] > block_pos[:, None])).astype(jnp.float32)
    last_match = (doc_values == doc_values[-1]).astype(jnp.float32)
    first_match = (doc_values == doc_values[0]).astype(jnp.float32)

    def lanes(table, rows):
        return jnp.broadcast_to(table.reshape(rows, 1), (rows, head_width))

    earlier_rows = lanes(earlier_mask, block_count * block_count)
    later_rows = lanes(later_mask, block_count * block_count)
    last_rows = lanes(last_match, block_count)
    first_rows = lanes(first_match, block_count)
    doc_rows = lanes(doc_values + 1.0, block_count)
    last_doc_rows = jnp.broadcast_to(doc_values[-1] + 1.0, (8, head_width))
    first_doc_rows = jnp.broadcast_to(doc_values[0] + 1.0, (8, head_width))

    pair_flops = 2 * head_count * block_count * block_len * block_len * head_width
    full = jax.ShapeDtypeStruct(queries.shape, jnp.bfloat16)
    wide = jax.ShapeDtypeStruct(queries.shape, jnp.float32)
    states = jax.ShapeDtypeStruct((head_count, block_count, head_width, head_width), jnp.float32)
    payload = jax.ShapeDtypeStruct((head_count, head_width + 8, head_width), jnp.float32)
    ctx_size = lax.axis_size("ctx")
    longest_doc = ctx_size * block_count // 2
    reach = (longest_doc - 2) // block_count + 1

    local_prefix, kv_payload = per_head_call(
        functools.partial(state_kernel, block_len),
        [(keys, True), (values, True), (earlier_rows, False), (last_rows, False),
         (last_doc_rows, False)],
        [(states, True), (payload, True)],
        pair_flops // 2,
    )
    prior, intra_part = carry(
        kv_payload,
        "ctx",
        False,
        reach,
        lambda: per_head_call(
            functools.partial(intra_kernel, block_len),
            [(queries, True), (keys, True), (values, True)],
            [(wide, True)],
            2 * pair_flops,
        )[0],
    )
    local_sums, preceding_states = per_head_call(
        functools.partial(forward_kernel, block_len),
        [(intra_part, True), (queries, True), (out_grad, True), (gain, True),
         (local_prefix, True), (prior, True), (doc_rows, False)],
        [(jax.ShapeDtypeStruct((tok_count, 2), jnp.float32), False),
         (jax.ShapeDtypeStruct(states.shape, jnp.bfloat16), True)],
        pair_flops // 2,
    )
    feature_count = head_count * head_width * lax.axis_size(("sub", "head"))
    total_sums = lax.psum(local_sums.T.reshape(2 * tok_count), ("sub", "head"))
    root_mean = jnp.sqrt(total_sums[:tok_count] / feature_count + 1e-06)
    inner_mean = total_sums[tok_count:] / feature_count
    factor = inner_mean / (root_mean * root_mean)
    coefs = jnp.stack([root_mean, factor], axis=1)
    d_attn, local_suffix, qd_payload = per_head_call(
        functools.partial(grad_kernel, block_len),
        [(queries, True), (keys, True), (values, True), (out_grad, True), (gain, True),
         (preceding_states, True), (coefs, False), (later_rows, False), (first_rows, False),
         (first_doc_rows, False)],
        [(full, True), (states, True), (payload, True)],
        3 * pair_flops,
    )
    following, (query_gradient, key_intra, value_intra) = carry(
        qd_payload,
        "ctx",
        True,
        reach,
        lambda: per_head_call(
            functools.partial(query_grad_kernel, block_len),
            [(queries, True), (keys, True), (values, True), (d_attn, True),
             (preceding_states, True)],
            [(full, True), (wide, True), (wide, True)],
            5 * pair_flops,
        ),
    )
    key_gradient, value_gradient = per_head_call(
        functools.partial(key_value_grad_kernel, block_len),
        [(key_intra, True), (value_intra, True), (keys, True), (values, True),
         (local_suffix, True), (following, True), (doc_rows, False)],
        [(full, True), (full, True)],
        pair_flops,
    )
    return query_gradient, key_gradient, value_gradient


def solution(mesh):
    return jax.shard_map(
        on_device,
        mesh=mesh,
        in_specs=(
            P(("sub", "head"), ("groups", "ctx"), None),
            P(("sub", "head"), ("groups", "ctx"), None),
            P(("sub", "head"), ("groups", "ctx"), None),
            P(("sub", "head"), ("groups", "ctx"), None),
            P(("sub", "head"), None),
            P(("groups", "ctx")),
        ),
        out_specs=(
            P(("sub", "head"), ("groups", "ctx"), None),
            P(("sub", "head"), ("groups", "ctx"), None),
            P(("sub", "head"), ("groups", "ctx"), None),
        ),
        check_vma=False,
    )
```

```python
import functools
import math

import jax
import jax.numpy as jnp
from jax import lax
from jax.experimental import pallas as pl
from jax.sharding import PartitionSpec as P

_ROWS_MINOR = (((1,), (1,)), ((), ()))
_ROWS_MAJOR = (((0,), (0,)), ((), ()))


def _causal(block_len):
    row_ids = lax.broadcasted_iota(jnp.int32, (block_len, block_len), 0)
    col_ids = lax.broadcasted_iota(jnp.int32, (block_len, block_len), 1)
    return row_ids >= col_ids


def _sum_blocks(mask_ref, first_row, parts):
    total = mask_ref[first_row : first_row + 1, :] * parts[0]
    for c in range(1, len(parts)):
        total = total + mask_ref[first_row + c : first_row + c + 1, :] * parts[c]
    return total


def _carried(state_ref, doc_ref, n, carry_ref):
    width = carry_ref.shape[2]
    joined = doc_ref[n : n + 1, :] == carry_ref[0, width : width + 1, :]
    total = state_ref[0, n] + jnp.where(joined, carry_ref[0, :width, :], 0.0)
    return total.astype(jnp.bfloat16)


def state_kernel(block_len, k_ref, v_ref, pair_ref, end_ref, row_ref, prefix_ref, pay_ref):
    count = k_ref.shape[1] // block_len
    width = k_ref.shape[2]
    parts = []
    for n in range(count):
        rows = pl.ds(n * block_len, block_len)
        parts.append(
            lax.dot_general(
                k_ref[0, rows, :], v_ref[0, rows, :], _ROWS_MAJOR,
                preferred_element_type=jnp.float32,
            )
        )
    for b in range(count):
        prefix_ref[0, b] = _sum_blocks(pair_ref, b * count, parts)
    pay_ref[0, :width, :] = _sum_blocks(end_ref, 0, parts)
    pay_ref[0, width:, :] = row_ref[...]


def combine_kernel(near_ref, far_ref, o_ref):
    width = near_ref.shape[2]
    for h in range(near_ref.shape[0]):
        joined = near_ref[h, width : width + 1, :] == far_ref[h, width : width + 1, :]
        o_ref[h, :width, :] = near_ref[h, :width, :] + jnp.where(
            joined, far_ref[h, :width, :], 0.0
        )
        o_ref[h, width:, :] = near_ref[h, width:, :]


def intra_kernel(block_len, q_ref, k_ref, v_ref, o_ref):
    causal = _causal(block_len)
    for n in range(q_ref.shape[1] // block_len):
        rows = pl.ds(n * block_len, block_len)
        q, k, v = q_ref[0, rows, :], k_ref[0, rows, :], v_ref[0, rows, :]
        scores = lax.dot_general(q, k, _ROWS_MINOR, preferred_element_type=jnp.float32)
        probs = jnp.where(causal, scores, 0.0).astype(jnp.bfloat16)
        o_ref[0, rows, :] = jnp.dot(probs, v, preferred_element_type=jnp.float32)


def forward_kernel(
    block_len, i_ref, q_ref, g_ref, n_ref, prefix_ref, carry_ref, doc_ref, o_ref, s_ref
):
    @pl.when(pl.program_id(0) == 0)
    def _():
        o_ref[...] = jnp.zeros_like(o_ref)

    for n in range(q_ref.shape[1] // block_len):
        rows = pl.ds(n * block_len, block_len)
        state = _carried(prefix_ref, doc_ref, n, carry_ref)
        s_ref[0, n] = state
        raw = i_ref[0, rows, :] + jnp.dot(
            q_ref[0, rows, :], state, preferred_element_type=jnp.float32
        )
        scaled = n_ref[0] * g_ref[0, rows, :].astype(jnp.float32)
        o_ref[rows, 0:1] += jnp.sum(raw * raw, axis=1, keepdims=True)
        o_ref[rows, 1:2] += jnp.sum(scaled * raw, axis=1, keepdims=True)


def grad_kernel(
    block_len, q_ref, k_ref, v_ref, g_ref, n_ref, s_ref, c_ref, pair_ref, end_ref, row_ref,
    d_ref, suffix_ref, pay_ref,
):
    causal = _causal(block_len)
    count = q_ref.shape[1] // block_len
    width = q_ref.shape[2]
    parts = []
    for n in range(count):
        rows = pl.ds(n * block_len, block_len)
        q, k, v = q_ref[0, rows, :], k_ref[0, rows, :], v_ref[0, rows, :]
        scores = lax.dot_general(q, k, _ROWS_MINOR, preferred_element_type=jnp.float32)
        probs = jnp.where(causal, scores, 0.0).astype(jnp.bfloat16)
        raw = jnp.dot(probs, v, preferred_element_type=jnp.float32)
        raw = raw + jnp.dot(q, s_ref[0, n], preferred_element_type=jnp.float32)
        scaled = n_ref[0] * g_ref[0, rows, :].astype(jnp.float32)
        root_mean = c_ref[rows, 0:1]
        factor = c_ref[rows, 1:2]
        d = ((scaled - raw * factor) / root_mean).astype(jnp.bfloat16)
        d_ref[0, rows, :] = d
        parts.append(lax.dot_general(q, d, _ROWS_MAJOR, preferred_element_type=jnp.float32))
    for b in range(count):
        suffix_ref[0, b] = _sum_blocks(pair_ref, b * count, parts)
    pay_ref[0, :width, :] = _sum_blocks(end_ref, 0, parts)
    pay_ref[0, width:, :] = row_ref[...]


def query_grad_kernel(block_len, q_ref, k_ref, v_ref, d_ref, s_ref, dq_ref, dk_ref, dv_ref):
    causal = _causal(block_len)
    for n in range(k_ref.shape[1] // block_len):
        rows = pl.ds(n * block_len, block_len)
        q, k, v = q_ref[0, rows, :], k_ref[0, rows, :], v_ref[0, rows, :]
        d = d_ref[0, rows, :]
        scores = lax.dot_general(q, k, _ROWS_MINOR, preferred_element_type=jnp.float32)
        probs = jnp.where(causal, scores, 0.0).astype(jnp.bfloat16)
        grad_scores = lax.dot_general(d, v, _ROWS_MINOR, preferred_element_type=jnp.float32)
        grad_probs = jnp.where(causal, grad_scores, 0.0).astype(jnp.bfloat16)
        dq = jnp.dot(grad_probs, k, preferred_element_type=jnp.float32)
        dq = dq + lax.dot_general(d, s_ref[0, n], _ROWS_MINOR, preferred_element_type=jnp.float32)
        dq_ref[0, rows, :] = dq.astype(dq_ref.dtype)
        dk_ref[0, rows, :] = lax.dot_general(
            grad_probs, q, _ROWS_MAJOR, preferred_element_type=jnp.float32
        )
        dv_ref[0, rows, :] = lax.dot_general(
            probs, d, _ROWS_MAJOR, preferred_element_type=jnp.float32
        )


def key_value_grad_kernel(
    block_len, ik_ref, iv_ref, k_ref, v_ref, suffix_ref, carry_ref, doc_ref, dk_ref, dv_ref
):
    for n in range(k_ref.shape[1] // block_len):
        rows = pl.ds(n * block_len, block_len)
        state = _carried(suffix_ref, doc_ref, n, carry_ref)
        dk = ik_ref[0, rows, :] + lax.dot_general(
            v_ref[0, rows, :], state, _ROWS_MINOR, preferred_element_type=jnp.float32
        )
        dv = iv_ref[0, rows, :] + jnp.dot(
            k_ref[0, rows, :], state, preferred_element_type=jnp.float32
        )
        dk_ref[0, rows, :] = dk.astype(dk_ref.dtype)
        dv_ref[0, rows, :] = dv.astype(dv_ref.dtype)


def per_head_call(kernel, inputs, outputs, flops):
    def spec(shape, per_head):
        if per_head:
            return pl.BlockSpec((1,) + shape[1:], lambda h: (h,) + (0,) * (len(shape) - 1))
        return pl.BlockSpec(shape, lambda h: (0,) * len(shape))

    head_count = inputs[0][0].shape[0]
    in_bytes = sum(x.size * x.dtype.itemsize for x, _ in inputs)
    out_bytes = sum(math.prod(o.shape) * o.dtype.itemsize for o, _ in outputs)
    return pl.pallas_call(
        kernel,
        grid=(head_count,),
        in_specs=[spec(x.shape, h) for x, h in inputs],
        out_specs=[spec(o.shape, h) for o, h in outputs],
        out_shape=[o for o, _ in outputs],
        cost_estimate=pl.CostEstimate(
            flops=flops, transcendentals=0, bytes_accessed=in_bytes + out_bytes
        ),
    )(*[x for x, _ in inputs])


def combine(near, far):
    return pl.pallas_call(
        combine_kernel,
        out_shape=jax.ShapeDtypeStruct(near.shape, near.dtype),
        cost_estimate=pl.CostEstimate(
            flops=2 * near.size, transcendentals=0, bytes_accessed=3 * near.size * 4
        ),
    )(near, far)


def carry(payload, axis, reverse, reach, cover):
    peers = lax.axis_size(axis)
    reach = min(reach, peers - 1)

    def shift(value, step):
        if reverse:
            pairs = [(j, j - step) for j in range(step, peers)]
        else:
            pairs = [(j, j + step) for j in range(peers - step)]
        return lax.ppermute(value, axis, pairs)

    if reach < 1:
        return jnp.zeros_like(payload), cover()
    got = shift(payload, 1)
    covered_value = cover()
    got, covered_value = lax.optimization_barrier((got, covered_value))
    if reach <= 2:
        if reach == 2:
            got = shift(combine(payload, got), 1)
        return got, covered_value
    earlier, inclusive = got, combine(payload, got)
    covered = 1
    while covered < reach:
        step = covered + 1
        got = shift(inclusive, step)
        earlier = combine(earlier, got)
        covered = covered + step
        if covered < reach:
            inclusive = combine(inclusive, got)
    return earlier, covered_value


def on_device(queries, keys, values, out_grad, norm_gain, doc_ids):
    head_count, tok_count, head_width = queries.shape
    block_count = doc_ids.shape[0]
    block_len = tok_count // block_count
    gain = norm_gain.reshape(head_count, 1, head_width)
    doc_values = doc_ids.astype(jnp.float32)
    block_pos = jnp.arange(block_count, dtype=jnp.int32)
    same_doc = doc_values[:, None] == doc_values[None, :]
    earlier_mask = (same_doc & (block_pos[None, :] < block_pos[:, None])).astype(jnp.float32)
    later_mask = (same_doc & (block_pos[None, :] > block_pos[:, None])).astype(jnp.float32)
    last_match = (doc_values == doc_values[-1]).astype(jnp.float32)
    first_match = (doc_values == doc_values[0]).astype(jnp.float32)

    def lanes(table, rows):
        return jnp.broadcast_to(table.reshape(rows, 1), (rows, head_width))

    earlier_rows = lanes(earlier_mask, block_count * block_count)
    later_rows = lanes(later_mask, block_count * block_count)
    last_rows = lanes(last_match, block_count)
    first_rows = lanes(first_match, block_count)
    doc_rows = lanes(doc_values + 1.0, block_count)
    last_doc_rows = jnp.broadcast_to(doc_values[-1] + 1.0, (8, head_width))
    first_doc_rows = jnp.broadcast_to(doc_values[0] + 1.0, (8, head_width))

    pair_flops = 2 * head_count * block_count * block_len * block_len * head_width
    full = jax.ShapeDtypeStruct(queries.shape, jnp.bfloat16)
    wide = jax.ShapeDtypeStruct(queries.shape, jnp.float32)
    states = jax.ShapeDtypeStruct((head_count, block_count, head_width, head_width), jnp.float32)
    payload = jax.ShapeDtypeStruct((head_count, head_width + 8, head_width), jnp.float32)
    ctx_size = lax.axis_size("ctx")
    longest_doc = ctx_size * block_count // 2
    reach = (longest_doc - 2) // block_count + 1

    local_prefix, kv_payload = per_head_call(
        functools.partial(state_kernel, block_len),
        [(keys, True), (values, True), (earlier_rows, False), (last_rows, False),
         (last_doc_rows, False)],
        [(states, True), (payload, True)],
        pair_flops // 2,
    )
    prior, intra_part = carry(
        kv_payload,
        "ctx",
        False,
        reach,
        lambda: per_head_call(
            functools.partial(intra_kernel, block_len),
            [(queries, True), (keys, True), (values, True)],
            [(wide, True)],
            2 * pair_flops,
        )[0],
    )
    local_sums, preceding_states = per_head_call(
        functools.partial(forward_kernel, block_len),
        [(intra_part, True), (queries, True), (out_grad, True), (gain, True),
         (local_prefix, True), (prior, True), (doc_rows, False)],
        [(jax.ShapeDtypeStruct((tok_count, 2), jnp.float32), False),
         (jax.ShapeDtypeStruct(states.shape, jnp.bfloat16), True)],
        pair_flops // 2,
    )
    feature_count = head_count * head_width * lax.axis_size(("sub", "head"))
    total_sums = local_sums.T.reshape(2 * tok_count)
    for axis in ("head", "sub"):
        if lax.axis_size(axis) == 2:
            total_sums = total_sums + lax.ppermute(total_sums, axis, [(0, 1), (1, 0)])
        elif lax.axis_size(axis) > 2:
            total_sums = lax.psum(total_sums, axis)
    root_mean = jnp.sqrt(total_sums[:tok_count] / feature_count + 1e-06)
    inner_mean = total_sums[tok_count:] / feature_count
    factor = inner_mean / (root_mean * root_mean)
    coefs = jnp.stack([root_mean, factor], axis=1)
    d_attn, local_suffix, qd_payload = per_head_call(
        functools.partial(grad_kernel, block_len),
        [(queries, True), (keys, True), (values, True), (out_grad, True), (gain, True),
         (preceding_states, True), (coefs, False), (later_rows, False), (first_rows, False),
         (first_doc_rows, False)],
        [(full, True), (states, True), (payload, True)],
        3 * pair_flops,
    )
    following, (query_gradient, key_intra, value_intra) = carry(
        qd_payload,
        "ctx",
        True,
        reach,
        lambda: per_head_call(
            functools.partial(query_grad_kernel, block_len),
            [(queries, True), (keys, True), (values, True), (d_attn, True),
             (preceding_states, True)],
            [(full, True), (wide, True), (wide, True)],
            5 * pair_flops,
        ),
    )
    key_gradient, value_gradient = per_head_call(
        functools.partial(key_value_grad_kernel, block_len),
        [(key_intra, True), (value_intra, True), (keys, True), (values, True),
         (local_suffix, True), (following, True), (doc_rows, False)],
        [(full, True), (full, True)],
        pair_flops,
    )
    return query_gradient, key_gradient, value_gradient


def solution(mesh):
    return jax.shard_map(
        on_device,
        mesh=mesh,
        in_specs=(
            P(("sub", "head"), ("groups", "ctx"), None),
            P(("sub", "head"), ("groups", "ctx"), None),
            P(("sub", "head"), ("groups", "ctx"), None),
            P(("sub", "head"), ("groups", "ctx"), None),
            P(("sub", "head"), None),
            P(("groups", "ctx")),
        ),
        out_specs=(
            P(("sub", "head"), ("groups", "ctx"), None),
            P(("sub", "head"), ("groups", "ctx"), None),
            P(("sub", "head"), ("groups", "ctx"), None),
        ),
        check_vma=False,
    )
```

```python
import functools
import math

import jax
import jax.numpy as jnp
from jax import lax
from jax.experimental import pallas as pl
from jax.sharding import PartitionSpec as P

_ROWS_MINOR = (((1,), (1,)), ((), ()))
_ROWS_MAJOR = (((0,), (0,)), ((), ()))


def _causal(block_len):
    row_ids = lax.broadcasted_iota(jnp.int32, (block_len, block_len), 0)
    col_ids = lax.broadcasted_iota(jnp.int32, (block_len, block_len), 1)
    return row_ids >= col_ids


def _sum_blocks(mask_ref, first_row, parts):
    total = mask_ref[first_row : first_row + 1, :] * parts[0]
    for c in range(1, len(parts)):
        total = total + mask_ref[first_row + c : first_row + c + 1, :] * parts[c]
    return total


def _carried(state_ref, doc_ref, n, carry_ref):
    width = carry_ref.shape[2]
    joined = doc_ref[n : n + 1, :] == carry_ref[0, width : width + 1, :]
    total = state_ref[0, n] + jnp.where(joined, carry_ref[0, :width, :], 0.0)
    return total.astype(jnp.bfloat16)


def state_kernel(block_len, k_ref, v_ref, pair_ref, end_ref, row_ref, prefix_ref, pay_ref):
    count = k_ref.shape[1] // block_len
    width = k_ref.shape[2]
    parts = []
    for n in range(count):
        rows = pl.ds(n * block_len, block_len)
        parts.append(
            lax.dot_general(
                k_ref[0, rows, :], v_ref[0, rows, :], _ROWS_MAJOR,
                preferred_element_type=jnp.float32,
            )
        )
    for b in range(count):
        prefix_ref[0, b] = _sum_blocks(pair_ref, b * count, parts)
    pay_ref[0, :width, :] = _sum_blocks(end_ref, 0, parts)
    pay_ref[0, width:, :] = row_ref[...]


def combine_kernel(near_ref, far_ref, o_ref):
    width = near_ref.shape[2]
    for h in range(near_ref.shape[0]):
        joined = near_ref[h, width : width + 1, :] == far_ref[h, width : width + 1, :]
        o_ref[h, :width, :] = near_ref[h, :width, :] + jnp.where(
            joined, far_ref[h, :width, :], 0.0
        )
        o_ref[h, width:, :] = near_ref[h, width:, :]


def intra_kernel(block_len, q_ref, k_ref, v_ref, o_ref):
    causal = _causal(block_len)
    for n in range(q_ref.shape[1] // block_len):
        rows = pl.ds(n * block_len, block_len)
        q, k, v = q_ref[0, rows, :], k_ref[0, rows, :], v_ref[0, rows, :]
        scores = lax.dot_general(q, k, _ROWS_MINOR, preferred_element_type=jnp.float32)
        probs = jnp.where(causal, scores, 0.0).astype(jnp.bfloat16)
        o_ref[0, rows, :] = jnp.dot(probs, v, preferred_element_type=jnp.float32)


def forward_kernel(
    block_len, i_ref, q_ref, g_ref, n_ref, prefix_ref, carry_ref, doc_ref, o_ref, s_ref, r_ref
):
    @pl.when(pl.program_id(0) == 0)
    def _():
        o_ref[...] = jnp.zeros_like(o_ref)

    for n in range(q_ref.shape[1] // block_len):
        rows = pl.ds(n * block_len, block_len)
        state = _carried(prefix_ref, doc_ref, n, carry_ref)
        s_ref[0, n] = state
        raw = i_ref[0, rows, :] + jnp.dot(
            q_ref[0, rows, :], state, preferred_element_type=jnp.float32
        )
        r_ref[0, rows, :] = raw
        scaled = n_ref[0] * g_ref[0, rows, :].astype(jnp.float32)
        o_ref[rows, 0:1] += jnp.sum(raw * raw, axis=1, keepdims=True)
        o_ref[rows, 1:2] += jnp.sum(scaled * raw, axis=1, keepdims=True)


def grad_kernel(
    block_len, q_ref, r_ref, g_ref, n_ref, c_ref, pair_ref, end_ref, row_ref,
    d_ref, suffix_ref, pay_ref,
):
    count = q_ref.shape[1] // block_len
    width = q_ref.shape[2]
    parts = []
    for n in range(count):
        rows = pl.ds(n * block_len, block_len)
        q = q_ref[0, rows, :]
        raw = r_ref[0, rows, :]
        scaled = n_ref[0] * g_ref[0, rows, :].astype(jnp.float32)
        root_mean = c_ref[rows, 0:1]
        factor = c_ref[rows, 1:2]
        d = ((scaled - raw * factor) / root_mean).astype(jnp.bfloat16)
        d_ref[0, rows, :] = d
        parts.append(lax.dot_general(q, d, _ROWS_MAJOR, preferred_element_type=jnp.float32))
    for b in range(count):
        suffix_ref[0, b] = _sum_blocks(pair_ref, b * count, parts)
    pay_ref[0, :width, :] = _sum_blocks(end_ref, 0, parts)
    pay_ref[0, width:, :] = row_ref[...]


def query_grad_kernel(block_len, q_ref, k_ref, v_ref, d_ref, s_ref, dq_ref, dk_ref, dv_ref):
    causal = _causal(block_len)
    for n in range(k_ref.shape[1] // block_len):
        rows = pl.ds(n * block_len, block_len)
        q, k, v = q_ref[0, rows, :], k_ref[0, rows, :], v_ref[0, rows, :]
        d = d_ref[0, rows, :]
        scores = lax.dot_general(q, k, _ROWS_MINOR, preferred_element_type=jnp.float32)
        probs = jnp.where(causal, scores, 0.0).astype(jnp.bfloat16)
        grad_scores = lax.dot_general(d, v, _ROWS_MINOR, preferred_element_type=jnp.float32)
        grad_probs = jnp.where(causal, grad_scores, 0.0).astype(jnp.bfloat16)
        dq = jnp.dot(grad_probs, k, preferred_element_type=jnp.float32)
        dq = dq + lax.dot_general(d, s_ref[0, n], _ROWS_MINOR, preferred_element_type=jnp.float32)
        dq_ref[0, rows, :] = dq.astype(dq_ref.dtype)
        dk_ref[0, rows, :] = lax.dot_general(
            grad_probs, q, _ROWS_MAJOR, preferred_element_type=jnp.float32
        )
        dv_ref[0, rows, :] = lax.dot_general(
            probs, d, _ROWS_MAJOR, preferred_element_type=jnp.float32
        )


def key_value_grad_kernel(
    block_len, ik_ref, iv_ref, k_ref, v_ref, suffix_ref, carry_ref, doc_ref, dk_ref, dv_ref
):
    for n in range(k_ref.shape[1] // block_len):
        rows = pl.ds(n * block_len, block_len)
        state = _carried(suffix_ref, doc_ref, n, carry_ref)
        dk = ik_ref[0, rows, :] + lax.dot_general(
            v_ref[0, rows, :], state, _ROWS_MINOR, preferred_element_type=jnp.float32
        )
        dv = iv_ref[0, rows, :] + jnp.dot(
            k_ref[0, rows, :], state, preferred_element_type=jnp.float32
        )
        dk_ref[0, rows, :] = dk.astype(dk_ref.dtype)
        dv_ref[0, rows, :] = dv.astype(dv_ref.dtype)


def per_head_call(kernel, inputs, outputs, flops):
    def spec(shape, per_head):
        if per_head:
            return pl.BlockSpec((1,) + shape[1:], lambda h: (h,) + (0,) * (len(shape) - 1))
        return pl.BlockSpec(shape, lambda h: (0,) * len(shape))

    head_count = inputs[0][0].shape[0]
    in_bytes = sum(x.size * x.dtype.itemsize for x, _ in inputs)
    out_bytes = sum(math.prod(o.shape) * o.dtype.itemsize for o, _ in outputs)
    return pl.pallas_call(
        kernel,
        grid=(head_count,),
        in_specs=[spec(x.shape, h) for x, h in inputs],
        out_specs=[spec(o.shape, h) for o, h in outputs],
        out_shape=[o for o, _ in outputs],
        cost_estimate=pl.CostEstimate(
            flops=flops, transcendentals=0, bytes_accessed=in_bytes + out_bytes
        ),
    )(*[x for x, _ in inputs])


def combine(near, far):
    return pl.pallas_call(
        combine_kernel,
        out_shape=jax.ShapeDtypeStruct(near.shape, near.dtype),
        cost_estimate=pl.CostEstimate(
            flops=2 * near.size, transcendentals=0, bytes_accessed=3 * near.size * 4
        ),
    )(near, far)


def carry(payload, axis, reverse, reach, cover):
    peers = lax.axis_size(axis)
    reach = min(reach, peers - 1)

    def shift(value, step):
        if reverse:
            pairs = [(j, j - step) for j in range(step, peers)]
        else:
            pairs = [(j, j + step) for j in range(peers - step)]
        return lax.ppermute(value, axis, pairs)

    if reach < 1:
        return jnp.zeros_like(payload), cover()
    got = shift(payload, 1)
    covered_value = cover()
    got, covered_value = lax.optimization_barrier((got, covered_value))
    if reach <= 2:
        if reach == 2:
            got = shift(combine(payload, got), 1)
        return got, covered_value
    earlier, inclusive = got, combine(payload, got)
    covered = 1
    while covered < reach:
        step = covered + 1
        got = shift(inclusive, step)
        earlier = combine(earlier, got)
        covered = covered + step
        if covered < reach:
            inclusive = combine(inclusive, got)
    return earlier, covered_value


def on_device(queries, keys, values, out_grad, norm_gain, doc_ids):
    head_count, tok_count, head_width = queries.shape
    block_count = doc_ids.shape[0]
    block_len = tok_count // block_count
    gain = norm_gain.reshape(head_count, 1, head_width)
    doc_values = doc_ids.astype(jnp.float32)
    block_pos = jnp.arange(block_count, dtype=jnp.int32)
    same_doc = doc_values[:, None] == doc_values[None, :]
    earlier_mask = (same_doc & (block_pos[None, :] < block_pos[:, None])).astype(jnp.float32)
    later_mask = (same_doc & (block_pos[None, :] > block_pos[:, None])).astype(jnp.float32)
    last_match = (doc_values == doc_values[-1]).astype(jnp.float32)
    first_match = (doc_values == doc_values[0]).astype(jnp.float32)

    def lanes(table, rows):
        return jnp.broadcast_to(table.reshape(rows, 1), (rows, head_width))

    earlier_rows = lanes(earlier_mask, block_count * block_count)
    later_rows = lanes(later_mask, block_count * block_count)
    last_rows = lanes(last_match, block_count)
    first_rows = lanes(first_match, block_count)
    doc_rows = lanes(doc_values + 1.0, block_count)
    last_doc_rows = jnp.broadcast_to(doc_values[-1] + 1.0, (8, head_width))
    first_doc_rows = jnp.broadcast_to(doc_values[0] + 1.0, (8, head_width))

    pair_flops = 2 * head_count * block_count * block_len * block_len * head_width
    full = jax.ShapeDtypeStruct(queries.shape, jnp.bfloat16)
    wide = jax.ShapeDtypeStruct(queries.shape, jnp.float32)
    states = jax.ShapeDtypeStruct((head_count, block_count, head_width, head_width), jnp.float32)
    payload = jax.ShapeDtypeStruct((head_count, head_width + 8, head_width), jnp.float32)
    ctx_size = lax.axis_size("ctx")
    longest_doc = ctx_size * block_count // 2
    reach = (longest_doc - 2) // block_count + 1

    local_prefix, kv_payload = per_head_call(
        functools.partial(state_kernel, block_len),
        [(keys, True), (values, True), (earlier_rows, False), (last_rows, False),
         (last_doc_rows, False)],
        [(states, True), (payload, True)],
        pair_flops // 2,
    )
    prior, intra_part = carry(
        kv_payload,
        "ctx",
        False,
        reach,
        lambda: per_head_call(
            functools.partial(intra_kernel, block_len),
            [(queries, True), (keys, True), (values, True)],
            [(wide, True)],
            2 * pair_flops,
        )[0],
    )
    local_sums, preceding_states, raw_attn = per_head_call(
        functools.partial(forward_kernel, block_len),
        [(intra_part, True), (queries, True), (out_grad, True), (gain, True),
         (local_prefix, True), (prior, True), (doc_rows, False)],
        [(jax.ShapeDtypeStruct((tok_count, 2), jnp.float32), False),
         (jax.ShapeDtypeStruct(states.shape, jnp.bfloat16), True), (wide, True)],
        pair_flops // 2,
    )
    feature_count = head_count * head_width * lax.axis_size(("sub", "head"))
    total_sums = local_sums.T.reshape(2 * tok_count)
    for axis in ("head", "sub"):
        if lax.axis_size(axis) == 2:
            total_sums = total_sums + lax.ppermute(total_sums, axis, [(0, 1), (1, 0)])
        elif lax.axis_size(axis) > 2:
            total_sums = lax.psum(total_sums, axis)
    root_mean = jnp.sqrt(total_sums[:tok_count] / feature_count + 1e-06)
    inner_mean = total_sums[tok_count:] / feature_count
    factor = inner_mean / (root_mean * root_mean)
    coefs = jnp.stack([root_mean, factor], axis=1)
    d_attn, local_suffix, qd_payload = per_head_call(
        functools.partial(grad_kernel, block_len),
        [(queries, True), (raw_attn, True), (out_grad, True), (gain, True),
         (coefs, False), (later_rows, False), (first_rows, False), (first_doc_rows, False)],
        [(full, True), (states, True), (payload, True)],
        pair_flops // 2,
    )
    following, (query_gradient, key_intra, value_intra) = carry(
        qd_payload,
        "ctx",
        True,
        reach,
        lambda: per_head_call(
            functools.partial(query_grad_kernel, block_len),
            [(queries, True), (keys, True), (values, True), (d_attn, True),
             (preceding_states, True)],
            [(full, True), (wide, True), (wide, True)],
            5 * pair_flops,
        ),
    )
    key_gradient, value_gradient = per_head_call(
        functools.partial(key_value_grad_kernel, block_len),
        [(key_intra, True), (value_intra, True), (keys, True), (values, True),
         (local_suffix, True), (following, True), (doc_rows, False)],
        [(full, True), (full, True)],
        pair_flops,
    )
    return query_gradient, key_gradient, value_gradient


def solution(mesh):
    return jax.shard_map(
        on_device,
        mesh=mesh,
        in_specs=(
            P(("sub", "head"), ("groups", "ctx"), None),
            P(("sub", "head"), ("groups", "ctx"), None),
            P(("sub", "head"), ("groups", "ctx"), None),
            P(("sub", "head"), ("groups", "ctx"), None),
            P(("sub", "head"), None),
            P(("groups", "ctx")),
        ),
        out_specs=(
            P(("sub", "head"), ("groups", "ctx"), None),
            P(("sub", "head"), ("groups", "ctx"), None),
            P(("sub", "head"), ("groups", "ctx"), None),
        ),
        check_vma=False,
    )
```

```python
import functools
import math

import jax
import jax.numpy as jnp
from jax import lax
from jax.experimental import pallas as pl
from jax.sharding import PartitionSpec as P

_ROWS_MINOR = (((1,), (1,)), ((), ()))
_ROWS_MAJOR = (((0,), (0,)), ((), ()))


def _causal(block_len):
    row_ids = lax.broadcasted_iota(jnp.int32, (block_len, block_len), 0)
    col_ids = lax.broadcasted_iota(jnp.int32, (block_len, block_len), 1)
    return row_ids >= col_ids


def _sum_blocks(mask_ref, first_row, parts):
    total = mask_ref[first_row : first_row + 1, :] * parts[0]
    for c in range(1, len(parts)):
        total = total + mask_ref[first_row + c : first_row + c + 1, :] * parts[c]
    return total


def _carried(state_ref, doc_ref, n, carry_ref):
    width = carry_ref.shape[2]
    joined = doc_ref[n : n + 1, :] == carry_ref[0, width : width + 1, :]
    total = state_ref[0, n] + jnp.where(joined, carry_ref[0, :width, :], 0.0)
    return total.astype(jnp.bfloat16)


def _key_value_parts(block_len, k_ref, v_ref):
    parts = []
    for n in range(k_ref.shape[1] // block_len):
        rows = pl.ds(n * block_len, block_len)
        parts.append(
            lax.dot_general(
                k_ref[0, rows, :], v_ref[0, rows, :], _ROWS_MAJOR,
                preferred_element_type=jnp.float32,
            )
        )
    return parts


def payload_kernel(block_len, k_ref, v_ref, end_ref, row_ref, pay_ref):
    width = k_ref.shape[2]
    parts = _key_value_parts(block_len, k_ref, v_ref)
    pay_ref[0, :width, :] = _sum_blocks(end_ref, 0, parts)
    pay_ref[0, width:, :] = row_ref[...]


def prefix_kernel(block_len, k_ref, v_ref, pair_ref, prefix_ref):
    parts = _key_value_parts(block_len, k_ref, v_ref)
    count = len(parts)
    for b in range(count):
        prefix_ref[0, b] = _sum_blocks(pair_ref, b * count, parts)


def combine_kernel(near_ref, far_ref, o_ref):
    width = near_ref.shape[2]
    for h in range(near_ref.shape[0]):
        joined = near_ref[h, width : width + 1, :] == far_ref[h, width : width + 1, :]
        o_ref[h, :width, :] = near_ref[h, :width, :] + jnp.where(
            joined, far_ref[h, :width, :], 0.0
        )
        o_ref[h, width:, :] = near_ref[h, width:, :]


def intra_kernel(block_len, q_ref, k_ref, v_ref, o_ref):
    causal = _causal(block_len)
    for n in range(q_ref.shape[1] // block_len):
        rows = pl.ds(n * block_len, block_len)
        q, k, v = q_ref[0, rows, :], k_ref[0, rows, :], v_ref[0, rows, :]
        scores = lax.dot_general(q, k, _ROWS_MINOR, preferred_element_type=jnp.float32)
        probs = jnp.where(causal, scores, 0.0).astype(jnp.bfloat16)
        o_ref[0, rows, :] = jnp.dot(probs, v, preferred_element_type=jnp.float32)


def forward_kernel(
    block_len, i_ref, q_ref, g_ref, n_ref, prefix_ref, carry_ref, doc_ref, o_ref, s_ref, r_ref
):
    @pl.when(pl.program_id(0) == 0)
    def _():
        o_ref[...] = jnp.zeros_like(o_ref)

    for n in range(q_ref.shape[1] // block_len):
        rows = pl.ds(n * block_len, block_len)
        state = _carried(prefix_ref, doc_ref, n, carry_ref)
        s_ref[0, n] = state
        raw = i_ref[0, rows, :] + jnp.dot(
            q_ref[0, rows, :], state, preferred_element_type=jnp.float32
        )
        r_ref[0, rows, :] = raw
        scaled = n_ref[0] * g_ref[0, rows, :].astype(jnp.float32)
        o_ref[rows, 0:1] += jnp.sum(raw * raw, axis=1, keepdims=True)
        o_ref[rows, 1:2] += jnp.sum(scaled * raw, axis=1, keepdims=True)


def grad_kernel(
    block_len, q_ref, r_ref, g_ref, n_ref, c_ref, pair_ref, end_ref, row_ref,
    d_ref, suffix_ref, pay_ref,
):
    count = q_ref.shape[1] // block_len
    width = q_ref.shape[2]
    parts = []
    for n in range(count):
        rows = pl.ds(n * block_len, block_len)
        q = q_ref[0, rows, :]
        raw = r_ref[0, rows, :]
        scaled = n_ref[0] * g_ref[0, rows, :].astype(jnp.float32)
        root_mean = c_ref[rows, 0:1]
        factor = c_ref[rows, 1:2]
        d = ((scaled - raw * factor) / root_mean).astype(jnp.bfloat16)
        d_ref[0, rows, :] = d
        parts.append(lax.dot_general(q, d, _ROWS_MAJOR, preferred_element_type=jnp.float32))
    for b in range(count):
        suffix_ref[0, b] = _sum_blocks(pair_ref, b * count, parts)
    pay_ref[0, :width, :] = _sum_blocks(end_ref, 0, parts)
    pay_ref[0, width:, :] = row_ref[...]


def query_grad_kernel(block_len, q_ref, k_ref, v_ref, d_ref, s_ref, dq_ref, dk_ref, dv_ref):
    causal = _causal(block_len)
    for n in range(k_ref.shape[1] // block_len):
        rows = pl.ds(n * block_len, block_len)
        q, k, v = q_ref[0, rows, :], k_ref[0, rows, :], v_ref[0, rows, :]
        d = d_ref[0, rows, :]
        scores = lax.dot_general(q, k, _ROWS_MINOR, preferred_element_type=jnp.float32)
        probs = jnp.where(causal, scores, 0.0).astype(jnp.bfloat16)
        grad_scores = lax.dot_general(d, v, _ROWS_MINOR, preferred_element_type=jnp.float32)
        grad_probs = jnp.where(causal, grad_scores, 0.0).astype(jnp.bfloat16)
        dq = jnp.dot(grad_probs, k, preferred_element_type=jnp.float32)
        dq = dq + lax.dot_general(d, s_ref[0, n], _ROWS_MINOR, preferred_element_type=jnp.float32)
        dq_ref[0, rows, :] = dq.astype(dq_ref.dtype)
        dk_ref[0, rows, :] = lax.dot_general(
            grad_probs, q, _ROWS_MAJOR, preferred_element_type=jnp.float32
        )
        dv_ref[0, rows, :] = lax.dot_general(
            probs, d, _ROWS_MAJOR, preferred_element_type=jnp.float32
        )


def key_value_grad_kernel(
    block_len, ik_ref, iv_ref, k_ref, v_ref, suffix_ref, carry_ref, doc_ref, dk_ref, dv_ref
):
    for n in range(k_ref.shape[1] // block_len):
        rows = pl.ds(n * block_len, block_len)
        state = _carried(suffix_ref, doc_ref, n, carry_ref)
        dk = ik_ref[0, rows, :] + lax.dot_general(
            v_ref[0, rows, :], state, _ROWS_MINOR, preferred_element_type=jnp.float32
        )
        dv = iv_ref[0, rows, :] + jnp.dot(
            k_ref[0, rows, :], state, preferred_element_type=jnp.float32
        )
        dk_ref[0, rows, :] = dk.astype(dk_ref.dtype)
        dv_ref[0, rows, :] = dv.astype(dv_ref.dtype)


def per_head_call(kernel, inputs, outputs, flops):
    def spec(shape, per_head):
        if per_head:
            return pl.BlockSpec((1,) + shape[1:], lambda h: (h,) + (0,) * (len(shape) - 1))
        return pl.BlockSpec(shape, lambda h: (0,) * len(shape))

    head_count = inputs[0][0].shape[0]
    in_bytes = sum(x.size * x.dtype.itemsize for x, _ in inputs)
    out_bytes = sum(math.prod(o.shape) * o.dtype.itemsize for o, _ in outputs)
    return pl.pallas_call(
        kernel,
        grid=(head_count,),
        in_specs=[spec(x.shape, h) for x, h in inputs],
        out_specs=[spec(o.shape, h) for o, h in outputs],
        out_shape=[o for o, _ in outputs],
        cost_estimate=pl.CostEstimate(
            flops=flops, transcendentals=0, bytes_accessed=in_bytes + out_bytes
        ),
    )(*[x for x, _ in inputs])


def combine(near, far):
    return pl.pallas_call(
        combine_kernel,
        out_shape=jax.ShapeDtypeStruct(near.shape, near.dtype),
        cost_estimate=pl.CostEstimate(
            flops=2 * near.size, transcendentals=0, bytes_accessed=3 * near.size * 4
        ),
    )(near, far)


def carry(payload, axis, reverse, reach, cover):
    peers = lax.axis_size(axis)
    reach = min(reach, peers - 1)

    def shift(value, step):
        if reverse:
            pairs = [(j, j - step) for j in range(step, peers)]
        else:
            pairs = [(j, j + step) for j in range(peers - step)]
        return lax.ppermute(value, axis, pairs)

    if reach < 1:
        return jnp.zeros_like(payload), cover()
    got = shift(payload, 1)
    covered_value = cover()
    got, covered_value = lax.optimization_barrier((got, covered_value))
    if reach <= 2:
        if reach == 2:
            got = shift(combine(payload, got), 1)
        return got, covered_value
    earlier, inclusive = got, combine(payload, got)
    covered = 1
    while covered < reach:
        step = covered + 1
        got = shift(inclusive, step)
        earlier = combine(earlier, got)
        covered = covered + step
        if covered < reach:
            inclusive = combine(inclusive, got)
    return earlier, covered_value


def on_device(queries, keys, values, out_grad, norm_gain, doc_ids):
    head_count, tok_count, head_width = queries.shape
    block_count = doc_ids.shape[0]
    block_len = tok_count // block_count
    gain = norm_gain.reshape(head_count, 1, head_width)
    doc_values = doc_ids.astype(jnp.float32)
    block_pos = jnp.arange(block_count, dtype=jnp.int32)
    same_doc = doc_values[:, None] == doc_values[None, :]
    earlier_mask = (same_doc & (block_pos[None, :] < block_pos[:, None])).astype(jnp.float32)
    later_mask = (same_doc & (block_pos[None, :] > block_pos[:, None])).astype(jnp.float32)
    last_match = (doc_values == doc_values[-1]).astype(jnp.float32)
    first_match = (doc_values == doc_values[0]).astype(jnp.float32)

    def lanes(table, rows):
        return jnp.broadcast_to(table.reshape(rows, 1), (rows, head_width))

    earlier_rows = lanes(earlier_mask, block_count * block_count)
    later_rows = lanes(later_mask, block_count * block_count)
    last_rows = lanes(last_match, block_count)
    first_rows = lanes(first_match, block_count)
    doc_rows = lanes(doc_values + 1.0, block_count)
    last_doc_rows = jnp.broadcast_to(doc_values[-1] + 1.0, (8, head_width))
    first_doc_rows = jnp.broadcast_to(doc_values[0] + 1.0, (8, head_width))

    pair_flops = 2 * head_count * block_count * block_len * block_len * head_width
    full = jax.ShapeDtypeStruct(queries.shape, jnp.bfloat16)
    wide = jax.ShapeDtypeStruct(queries.shape, jnp.float32)
    states = jax.ShapeDtypeStruct((head_count, block_count, head_width, head_width), jnp.float32)
    payload = jax.ShapeDtypeStruct((head_count, head_width + 8, head_width), jnp.float32)
    ctx_size = lax.axis_size("ctx")
    longest_doc = ctx_size * block_count // 2
    reach = (longest_doc - 2) // block_count + 1

    (kv_payload,) = per_head_call(
        functools.partial(payload_kernel, block_len),
        [(keys, True), (values, True), (last_rows, False), (last_doc_rows, False)],
        [(payload, True)],
        pair_flops // 2,
    )

    def forward_cover():
        (intra,) = per_head_call(
            functools.partial(intra_kernel, block_len),
            [(queries, True), (keys, True), (values, True)],
            [(wide, True)],
            2 * pair_flops,
        )
        (prefix,) = per_head_call(
            functools.partial(prefix_kernel, block_len),
            [(keys, True), (values, True), (earlier_rows, False)],
            [(states, True)],
            pair_flops // 2,
        )
        return intra, prefix

    prior, (intra_part, local_prefix) = carry(kv_payload, "ctx", False, reach, forward_cover)
    local_sums, preceding_states, raw_attn = per_head_call(
        functools.partial(forward_kernel, block_len),
        [(intra_part, True), (queries, True), (out_grad, True), (gain, True),
         (local_prefix, True), (prior, True), (doc_rows, False)],
        [(jax.ShapeDtypeStruct((tok_count, 2), jnp.float32), False),
         (jax.ShapeDtypeStruct(states.shape, jnp.bfloat16), True), (wide, True)],
        pair_flops // 2,
    )
    feature_count = head_count * head_width * lax.axis_size(("sub", "head"))
    total_sums = local_sums.T.reshape(2 * tok_count)
    for axis in ("head", "sub"):
        if lax.axis_size(axis) == 2:
            total_sums = total_sums + lax.ppermute(total_sums, axis, [(0, 1), (1, 0)])
        elif lax.axis_size(axis) > 2:
            total_sums = lax.psum(total_sums, axis)
    root_mean = jnp.sqrt(total_sums[:tok_count] / feature_count + 1e-06)
    inner_mean = total_sums[tok_count:] / feature_count
    factor = inner_mean / (root_mean * root_mean)
    coefs = jnp.stack([root_mean, factor], axis=1)
    d_attn, local_suffix, qd_payload = per_head_call(
        functools.partial(grad_kernel, block_len),
        [(queries, True), (raw_attn, True), (out_grad, True), (gain, True),
         (coefs, False), (later_rows, False), (first_rows, False), (first_doc_rows, False)],
        [(full, True), (states, True), (payload, True)],
        pair_flops // 2,
    )
    following, (query_gradient, key_intra, value_intra) = carry(
        qd_payload,
        "ctx",
        True,
        reach,
        lambda: per_head_call(
            functools.partial(query_grad_kernel, block_len),
            [(queries, True), (keys, True), (values, True), (d_attn, True),
             (preceding_states, True)],
            [(full, True), (wide, True), (wide, True)],
            5 * pair_flops,
        ),
    )
    key_gradient, value_gradient = per_head_call(
        functools.partial(key_value_grad_kernel, block_len),
        [(key_intra, True), (value_intra, True), (keys, True), (values, True),
         (local_suffix, True), (following, True), (doc_rows, False)],
        [(full, True), (full, True)],
        pair_flops,
    )
    return query_gradient, key_gradient, value_gradient


def solution(mesh):
    return jax.shard_map(
        on_device,
        mesh=mesh,
        in_specs=(
            P(("sub", "head"), ("groups", "ctx"), None),
            P(("sub", "head"), ("groups", "ctx"), None),
            P(("sub", "head"), ("groups", "ctx"), None),
            P(("sub", "head"), ("groups", "ctx"), None),
            P(("sub", "head"), None),
            P(("groups", "ctx")),
        ),
        out_specs=(
            P(("sub", "head"), ("groups", "ctx"), None),
            P(("sub", "head"), ("groups", "ctx"), None),
            P(("sub", "head"), ("groups", "ctx"), None),
        ),
        check_vma=False,
    )
```

```python
import functools
import math

import jax
import jax.numpy as jnp
from jax import lax
from jax.experimental import pallas as pl
from jax.sharding import PartitionSpec as P

_ROWS_MINOR = (((1,), (1,)), ((), ()))
_ROWS_MAJOR = (((0,), (0,)), ((), ()))


def _causal(block_len):
    row_ids = lax.broadcasted_iota(jnp.int32, (block_len, block_len), 0)
    col_ids = lax.broadcasted_iota(jnp.int32, (block_len, block_len), 1)
    return row_ids >= col_ids


def _sum_blocks(mask_ref, first_row, parts):
    total = mask_ref[first_row : first_row + 1, :] * parts[0]
    for c in range(1, len(parts)):
        total = total + mask_ref[first_row + c : first_row + c + 1, :] * parts[c]
    return total


def _carried(state_ref, doc_ref, n, carry_ref):
    width = carry_ref.shape[2]
    joined = doc_ref[n : n + 1, :] == carry_ref[0, width : width + 1, :]
    total = state_ref[0, n] + jnp.where(joined, carry_ref[0, :width, :], 0.0)
    return total.astype(jnp.bfloat16)


def state_kernel(block_len, k_ref, v_ref, pair_ref, end_ref, row_ref, prefix_ref, pay_ref):
    count = k_ref.shape[1] // block_len
    width = k_ref.shape[2]
    parts = []
    for n in range(count):
        rows = pl.ds(n * block_len, block_len)
        parts.append(
            lax.dot_general(
                k_ref[0, rows, :], v_ref[0, rows, :], _ROWS_MAJOR,
                preferred_element_type=jnp.float32,
            )
        )
    for b in range(count):
        prefix_ref[0, b] = _sum_blocks(pair_ref, b * count, parts)
    pay_ref[0, :width, :] = _sum_blocks(end_ref, 0, parts)
    pay_ref[0, width:, :] = row_ref[...]


def combine_kernel(near_ref, far_ref, o_ref):
    width = near_ref.shape[2]
    for h in range(near_ref.shape[0]):
        joined = near_ref[h, width : width + 1, :] == far_ref[h, width : width + 1, :]
        o_ref[h, :width, :] = near_ref[h, :width, :] + jnp.where(
            joined, far_ref[h, :width, :], 0.0
        )
        o_ref[h, width:, :] = near_ref[h, width:, :]


def intra_kernel(block_len, q_ref, k_ref, v_ref, o_ref):
    causal = _causal(block_len)
    for n in range(q_ref.shape[1] // block_len):
        rows = pl.ds(n * block_len, block_len)
        q, k, v = q_ref[0, rows, :], k_ref[0, rows, :], v_ref[0, rows, :]
        scores = lax.dot_general(q, k, _ROWS_MINOR, preferred_element_type=jnp.float32)
        probs = jnp.where(causal, scores, 0.0).astype(jnp.bfloat16)
        o_ref[0, rows, :] = jnp.dot(probs, v, preferred_element_type=jnp.float32)


def forward_kernel(
    block_len, i_ref, q_ref, g_ref, n_ref, prefix_ref, carry_ref, doc_ref, o_ref, s_ref, r_ref
):
    @pl.when(pl.program_id(0) == 0)
    def _():
        o_ref[...] = jnp.zeros_like(o_ref)

    for n in range(q_ref.shape[1] // block_len):
        rows = pl.ds(n * block_len, block_len)
        state = _carried(prefix_ref, doc_ref, n, carry_ref)
        s_ref[0, n] = state
        raw = i_ref[0, rows, :] + jnp.dot(
            q_ref[0, rows, :], state, preferred_element_type=jnp.float32
        )
        r_ref[0, rows, :] = raw
        scaled = n_ref[0] * g_ref[0, rows, :].astype(jnp.float32)
        o_ref[rows, 0:1] += jnp.sum(raw * raw, axis=1, keepdims=True)
        o_ref[rows, 1:2] += jnp.sum(scaled * raw, axis=1, keepdims=True)


def grad_kernel(
    block_len, q_ref, r_ref, g_ref, n_ref, c_ref, pair_ref, end_ref, row_ref,
    d_ref, suffix_ref, pay_ref,
):
    count = q_ref.shape[1] // block_len
    width = q_ref.shape[2]
    parts = []
    for n in range(count):
        rows = pl.ds(n * block_len, block_len)
        q = q_ref[0, rows, :]
        raw = r_ref[0, rows, :]
        scaled = n_ref[0] * g_ref[0, rows, :].astype(jnp.float32)
        root_mean = c_ref[rows, 0:1]
        factor = c_ref[rows, 1:2]
        d = ((scaled - raw * factor) / root_mean).astype(jnp.bfloat16)
        d_ref[0, rows, :] = d
        parts.append(lax.dot_general(q, d, _ROWS_MAJOR, preferred_element_type=jnp.float32))
    for b in range(count):
        suffix_ref[0, b] = _sum_blocks(pair_ref, b * count, parts)
    pay_ref[0, :width, :] = _sum_blocks(end_ref, 0, parts)
    pay_ref[0, width:, :] = row_ref[...]


def query_grad_kernel(block_len, q_ref, k_ref, v_ref, d_ref, s_ref, dq_ref, dk_ref, dv_ref):
    causal = _causal(block_len)
    for n in range(k_ref.shape[1] // block_len):
        rows = pl.ds(n * block_len, block_len)
        q, k, v = q_ref[0, rows, :], k_ref[0, rows, :], v_ref[0, rows, :]
        d = d_ref[0, rows, :]
        scores = lax.dot_general(q, k, _ROWS_MINOR, preferred_element_type=jnp.float32)
        probs = jnp.where(causal, scores, 0.0).astype(jnp.bfloat16)
        grad_scores = lax.dot_general(d, v, _ROWS_MINOR, preferred_element_type=jnp.float32)
        grad_probs = jnp.where(causal, grad_scores, 0.0).astype(jnp.bfloat16)
        dq = jnp.dot(grad_probs, k, preferred_element_type=jnp.float32)
        dq = dq + lax.dot_general(d, s_ref[0, n], _ROWS_MINOR, preferred_element_type=jnp.float32)
        dq_ref[0, rows, :] = dq.astype(dq_ref.dtype)
        dk_ref[0, rows, :] = lax.dot_general(
            grad_probs, q, _ROWS_MAJOR, preferred_element_type=jnp.float32
        )
        dv_ref[0, rows, :] = lax.dot_general(
            probs, d, _ROWS_MAJOR, preferred_element_type=jnp.float32
        )


def key_value_grad_kernel(
    block_len, ik_ref, iv_ref, k_ref, v_ref, suffix_ref, carry_ref, doc_ref, dk_ref, dv_ref
):
    for n in range(k_ref.shape[1] // block_len):
        rows = pl.ds(n * block_len, block_len)
        state = _carried(suffix_ref, doc_ref, n, carry_ref)
        dk = ik_ref[0, rows, :] + lax.dot_general(
            v_ref[0, rows, :], state, _ROWS_MINOR, preferred_element_type=jnp.float32
        )
        dv = iv_ref[0, rows, :] + jnp.dot(
            k_ref[0, rows, :], state, preferred_element_type=jnp.float32
        )
        dk_ref[0, rows, :] = dk.astype(dk_ref.dtype)
        dv_ref[0, rows, :] = dv.astype(dv_ref.dtype)


def per_head_call(kernel, inputs, outputs, flops, heads=None, into=()):
    def spec(shape, per_head, first):
        if per_head:
            return pl.BlockSpec(
                (1,) + shape[1:], lambda h: (h + first,) + (0,) * (len(shape) - 1)
            )
        return pl.BlockSpec(shape, lambda h: (0,) * len(shape))

    head_count = inputs[0][0].shape[0]
    first, count = heads if heads is not None else (0, head_count)
    share = count / head_count
    in_bytes = sum(x.size * x.dtype.itemsize for x, _ in inputs) * share
    out_bytes = sum(math.prod(o.shape) * o.dtype.itemsize for o, _ in outputs) * share
    skip = len(inputs)

    def body(*refs):
        kernel(*refs[:skip], *refs[skip + len(into):])

    return pl.pallas_call(
        body,
        grid=(count,),
        in_specs=[spec(x.shape, h, first) for x, h in inputs]
        + [pl.BlockSpec(memory_space=pl.ANY) for _ in into],
        out_specs=[spec(o.shape, h, first) for o, h in outputs],
        out_shape=[o for o, _ in outputs],
        input_output_aliases={skip + i: i for i in range(len(into))},
        cost_estimate=pl.CostEstimate(
            flops=int(flops * share), transcendentals=0,
            bytes_accessed=int(in_bytes + out_bytes),
        ),
    )(*[x for x, _ in inputs], *into)


def combine(near, far):
    return pl.pallas_call(
        combine_kernel,
        out_shape=jax.ShapeDtypeStruct(near.shape, near.dtype),
        cost_estimate=pl.CostEstimate(
            flops=2 * near.size, transcendentals=0, bytes_accessed=3 * near.size * 4
        ),
    )(near, far)


def carry(payload, axis, reverse, reach, cover):
    peers = lax.axis_size(axis)
    reach = min(reach, peers - 1)

    def shift(value, step):
        if reverse:
            pairs = [(j, j - step) for j in range(step, peers)]
        else:
            pairs = [(j, j + step) for j in range(peers - step)]
        return lax.ppermute(value, axis, pairs)

    first_cover, second_cover = cover
    if reach < 1:
        return jnp.zeros_like(payload), second_cover(first_cover())
    got = shift(payload, 1)
    covered_value = first_cover()
    got, covered_value = lax.optimization_barrier((got, covered_value))
    if reach <= 2:
        if reach == 2:
            got = shift(combine(payload, got), 1)
            covered_value = second_cover(covered_value)
            got, covered_value = lax.optimization_barrier((got, covered_value))
            return got, covered_value
        return got, second_cover(covered_value)
    earlier, inclusive = got, combine(payload, got)
    covered = 1
    while covered < reach:
        step = covered + 1
        got = shift(inclusive, step)
        earlier = combine(earlier, got)
        covered = covered + step
        if covered < reach:
            inclusive = combine(inclusive, got)
    return earlier, second_cover(covered_value)


def on_device(queries, keys, values, out_grad, norm_gain, doc_ids):
    head_count, tok_count, head_width = queries.shape
    block_count = doc_ids.shape[0]
    block_len = tok_count // block_count
    gain = norm_gain.reshape(head_count, 1, head_width)
    doc_values = doc_ids.astype(jnp.float32)
    block_pos = jnp.arange(block_count, dtype=jnp.int32)
    same_doc = doc_values[:, None] == doc_values[None, :]
    earlier_mask = (same_doc & (block_pos[None, :] < block_pos[:, None])).astype(jnp.float32)
    later_mask = (same_doc & (block_pos[None, :] > block_pos[:, None])).astype(jnp.float32)
    last_match = (doc_values == doc_values[-1]).astype(jnp.float32)
    first_match = (doc_values == doc_values[0]).astype(jnp.float32)

    def lanes(table, rows):
        return jnp.broadcast_to(table.reshape(rows, 1), (rows, head_width))

    earlier_rows = lanes(earlier_mask, block_count * block_count)
    later_rows = lanes(later_mask, block_count * block_count)
    last_rows = lanes(last_match, block_count)
    first_rows = lanes(first_match, block_count)
    doc_rows = lanes(doc_values + 1.0, block_count)
    last_doc_rows = jnp.broadcast_to(doc_values[-1] + 1.0, (8, head_width))
    first_doc_rows = jnp.broadcast_to(doc_values[0] + 1.0, (8, head_width))

    pair_flops = 2 * head_count * block_count * block_len * block_len * head_width
    full = jax.ShapeDtypeStruct(queries.shape, jnp.bfloat16)
    wide = jax.ShapeDtypeStruct(queries.shape, jnp.float32)
    states = jax.ShapeDtypeStruct((head_count, block_count, head_width, head_width), jnp.float32)
    payload = jax.ShapeDtypeStruct((head_count, head_width + 8, head_width), jnp.float32)
    ctx_size = lax.axis_size("ctx")
    longest_doc = ctx_size * block_count // 2
    reach = (longest_doc - 2) // block_count + 1

    local_prefix, kv_payload = per_head_call(
        functools.partial(state_kernel, block_len),
        [(keys, True), (values, True), (earlier_rows, False), (last_rows, False),
         (last_doc_rows, False)],
        [(states, True), (payload, True)],
        pair_flops // 2,
    )
    prior, intra_part = carry(
        kv_payload,
        "ctx",
        False,
        reach,
        (
            lambda: per_head_call(
                functools.partial(intra_kernel, block_len),
                [(queries, True), (keys, True), (values, True)],
                [(wide, True)],
                2 * pair_flops,
            )[0],
            lambda intra: intra,
        ),
    )
    local_sums, preceding_states, raw_attn = per_head_call(
        functools.partial(forward_kernel, block_len),
        [(intra_part, True), (queries, True), (out_grad, True), (gain, True),
         (local_prefix, True), (prior, True), (doc_rows, False)],
        [(jax.ShapeDtypeStruct((tok_count, 2), jnp.float32), False),
         (jax.ShapeDtypeStruct(states.shape, jnp.bfloat16), True), (wide, True)],
        pair_flops // 2,
    )
    feature_count = head_count * head_width * lax.axis_size(("sub", "head"))
    total_sums = local_sums.T.reshape(2 * tok_count)
    for axis in ("head", "sub"):
        if lax.axis_size(axis) == 2:
            total_sums = total_sums + lax.ppermute(total_sums, axis, [(0, 1), (1, 0)])
        elif lax.axis_size(axis) > 2:
            total_sums = lax.psum(total_sums, axis)
    root_mean = jnp.sqrt(total_sums[:tok_count] / feature_count + 1e-06)
    inner_mean = total_sums[tok_count:] / feature_count
    factor = inner_mean / (root_mean * root_mean)
    coefs = jnp.stack([root_mean, factor], axis=1)
    d_attn, local_suffix, qd_payload = per_head_call(
        functools.partial(grad_kernel, block_len),
        [(queries, True), (raw_attn, True), (out_grad, True), (gain, True),
         (coefs, False), (later_rows, False), (first_rows, False), (first_doc_rows, False)],
        [(full, True), (states, True), (payload, True)],
        pair_flops // 2,
    )
    half = head_count // 2

    def query_grads(heads, into):
        return per_head_call(
            functools.partial(query_grad_kernel, block_len),
            [(queries, True), (keys, True), (values, True), (d_attn, True),
             (preceding_states, True)],
            [(full, True), (wide, True), (wide, True)],
            5 * pair_flops,
            heads=heads,
            into=into,
        )

    following, (query_gradient, key_intra, value_intra) = carry(
        qd_payload,
        "ctx",
        True,
        reach,
        (
            lambda: query_grads((0, half), ()),
            lambda done: query_grads((half, head_count - half), tuple(done)),
        ),
    )
    key_gradient, value_gradient = per_head_call(
        functools.partial(key_value_grad_kernel, block_len),
        [(key_intra, True), (value_intra, True), (keys, True), (values, True),
         (local_suffix, True), (following, True), (doc_rows, False)],
        [(full, True), (full, True)],
        pair_flops,
    )
    return query_gradient, key_gradient, value_gradient


def solution(mesh):
    return jax.shard_map(
        on_device,
        mesh=mesh,
        in_specs=(
            P(("sub", "head"), ("groups", "ctx"), None),
            P(("sub", "head"), ("groups", "ctx"), None),
            P(("sub", "head"), ("groups", "ctx"), None),
            P(("sub", "head"), ("groups", "ctx"), None),
            P(("sub", "head"), None),
            P(("groups", "ctx")),
        ),
        out_specs=(
            P(("sub", "head"), ("groups", "ctx"), None),
            P(("sub", "head"), ("groups", "ctx"), None),
            P(("sub", "head"), ("groups", "ctx"), None),
        ),
        check_vma=False,
    )
```

```python
import functools
import math

import jax
import jax.numpy as jnp
from jax import lax
from jax.experimental import pallas as pl
from jax.sharding import PartitionSpec as P

_ROWS_MINOR = (((1,), (1,)), ((), ()))
_ROWS_MAJOR = (((0,), (0,)), ((), ()))


def _causal(block_len):
    row_ids = lax.broadcasted_iota(jnp.int32, (block_len, block_len), 0)
    col_ids = lax.broadcasted_iota(jnp.int32, (block_len, block_len), 1)
    return row_ids >= col_ids


def _sum_blocks(mask_ref, first_row, parts):
    total = mask_ref[first_row : first_row + 1, :] * parts[0]
    for c in range(1, len(parts)):
        total = total + mask_ref[first_row + c : first_row + c + 1, :] * parts[c]
    return total


def _carried(state_ref, doc_ref, n, carry_ref):
    width = carry_ref.shape[2]
    joined = doc_ref[n : n + 1, :] == carry_ref[0, width : width + 1, :]
    total = state_ref[0, n] + jnp.where(joined, carry_ref[0, :width, :], 0.0)
    return total.astype(jnp.bfloat16)


def state_kernel(block_len, k_ref, v_ref, pair_ref, end_ref, row_ref, prefix_ref, pay_ref):
    count = k_ref.shape[1] // block_len
    width = k_ref.shape[2]
    parts = []
    for n in range(count):
        rows = pl.ds(n * block_len, block_len)
        parts.append(
            lax.dot_general(
                k_ref[0, rows, :], v_ref[0, rows, :], _ROWS_MAJOR,
                preferred_element_type=jnp.float32,
            )
        )
    for b in range(count):
        prefix_ref[0, b] = _sum_blocks(pair_ref, b * count, parts)
    pay_ref[0, :width, :] = _sum_blocks(end_ref, 0, parts)
    pay_ref[0, width:, :] = row_ref[...]


def combine_kernel(near_ref, far_ref, o_ref):
    width = near_ref.shape[2]
    for h in range(near_ref.shape[0]):
        joined = near_ref[h, width : width + 1, :] == far_ref[h, width : width + 1, :]
        o_ref[h, :width, :] = near_ref[h, :width, :] + jnp.where(
            joined, far_ref[h, :width, :], 0.0
        )
        o_ref[h, width:, :] = near_ref[h, width:, :]


def intra_kernel(block_len, q_ref, k_ref, v_ref, o_ref):
    causal = _causal(block_len)
    for n in range(q_ref.shape[1] // block_len):
        rows = pl.ds(n * block_len, block_len)
        q, k, v = q_ref[0, rows, :], k_ref[0, rows, :], v_ref[0, rows, :]
        scores = lax.dot_general(q, k, _ROWS_MINOR, preferred_element_type=jnp.float32)
        probs = jnp.where(causal, scores, 0.0).astype(jnp.bfloat16)
        o_ref[0, rows, :] = jnp.dot(probs, v, preferred_element_type=jnp.float32)


def forward_kernel(
    block_len, i_ref, q_ref, g_ref, n_ref, prefix_ref, carry_ref, doc_ref, o_ref, s_ref
):
    @pl.when(pl.program_id(0) == 0)
    def _():
        o_ref[...] = jnp.zeros_like(o_ref)

    for n in range(q_ref.shape[1] // block_len):
        rows = pl.ds(n * block_len, block_len)
        state = _carried(prefix_ref, doc_ref, n, carry_ref)
        s_ref[0, n] = state
        raw = i_ref[0, rows, :] + jnp.dot(
            q_ref[0, rows, :], state, preferred_element_type=jnp.float32
        )
        scaled = n_ref[0] * g_ref[0, rows, :].astype(jnp.float32)
        o_ref[rows, 0:1] += jnp.sum(raw * raw, axis=1, keepdims=True)
        o_ref[rows, 1:2] += jnp.sum(scaled * raw, axis=1, keepdims=True)


def grad_kernel(
    block_len, q_ref, i_ref, s_ref, g_ref, n_ref, c_ref, pair_ref, end_ref, row_ref,
    d_ref, suffix_ref, pay_ref,
):
    count = q_ref.shape[1] // block_len
    width = q_ref.shape[2]
    parts = []
    for n in range(count):
        rows = pl.ds(n * block_len, block_len)
        q = q_ref[0, rows, :]
        raw = i_ref[0, rows, :] + jnp.dot(q, s_ref[0, n], preferred_element_type=jnp.float32)
        scaled = n_ref[0] * g_ref[0, rows, :].astype(jnp.float32)
        root_mean = c_ref[rows, 0:1]
        factor = c_ref[rows, 1:2]
        d = ((scaled - raw * factor) / root_mean).astype(jnp.bfloat16)
        d_ref[0, rows, :] = d
        parts.append(lax.dot_general(q, d, _ROWS_MAJOR, preferred_element_type=jnp.float32))
    for b in range(count):
        suffix_ref[0, b] = _sum_blocks(pair_ref, b * count, parts)
    pay_ref[0, :width, :] = _sum_blocks(end_ref, 0, parts)
    pay_ref[0, width:, :] = row_ref[...]


def query_grad_kernel(block_len, q_ref, k_ref, v_ref, d_ref, s_ref, dq_ref, dk_ref, dv_ref):
    causal = _causal(block_len)
    for n in range(k_ref.shape[1] // block_len):
        rows = pl.ds(n * block_len, block_len)
        q, k, v = q_ref[0, rows, :], k_ref[0, rows, :], v_ref[0, rows, :]
        d = d_ref[0, rows, :]
        scores = lax.dot_general(q, k, _ROWS_MINOR, preferred_element_type=jnp.float32)
        probs = jnp.where(causal, scores, 0.0).astype(jnp.bfloat16)
        grad_scores = lax.dot_general(d, v, _ROWS_MINOR, preferred_element_type=jnp.float32)
        grad_probs = jnp.where(causal, grad_scores, 0.0).astype(jnp.bfloat16)
        dq = jnp.dot(grad_probs, k, preferred_element_type=jnp.float32)
        dq = dq + lax.dot_general(d, s_ref[0, n], _ROWS_MINOR, preferred_element_type=jnp.float32)
        dq_ref[0, rows, :] = dq.astype(dq_ref.dtype)
        dk_ref[0, rows, :] = lax.dot_general(
            grad_probs, q, _ROWS_MAJOR, preferred_element_type=jnp.float32
        )
        dv_ref[0, rows, :] = lax.dot_general(
            probs, d, _ROWS_MAJOR, preferred_element_type=jnp.float32
        )


def key_value_grad_kernel(
    block_len, ik_ref, iv_ref, k_ref, v_ref, suffix_ref, carry_ref, doc_ref, dk_ref, dv_ref
):
    for n in range(k_ref.shape[1] // block_len):
        rows = pl.ds(n * block_len, block_len)
        state = _carried(suffix_ref, doc_ref, n, carry_ref)
        dk = ik_ref[0, rows, :] + lax.dot_general(
            v_ref[0, rows, :], state, _ROWS_MINOR, preferred_element_type=jnp.float32
        )
        dv = iv_ref[0, rows, :] + jnp.dot(
            k_ref[0, rows, :], state, preferred_element_type=jnp.float32
        )
        dk_ref[0, rows, :] = dk.astype(dk_ref.dtype)
        dv_ref[0, rows, :] = dv.astype(dv_ref.dtype)


def per_head_call(kernel, inputs, outputs, flops, heads=None, into=()):
    def spec(shape, per_head, first):
        if per_head:
            return pl.BlockSpec(
                (1,) + shape[1:], lambda h: (h + first,) + (0,) * (len(shape) - 1)
            )
        return pl.BlockSpec(shape, lambda h: (0,) * len(shape))

    head_count = inputs[0][0].shape[0]
    first, count = heads if heads is not None else (0, head_count)
    share = count / head_count
    in_bytes = sum(x.size * x.dtype.itemsize for x, _ in inputs) * share
    out_bytes = sum(math.prod(o.shape) * o.dtype.itemsize for o, _ in outputs) * share
    skip = len(inputs)

    def body(*refs):
        kernel(*refs[:skip], *refs[skip + len(into):])

    return pl.pallas_call(
        body,
        grid=(count,),
        in_specs=[spec(x.shape, h, first) for x, h in inputs]
        + [pl.BlockSpec(memory_space=pl.ANY) for _ in into],
        out_specs=[spec(o.shape, h, first) for o, h in outputs],
        out_shape=[o for o, _ in outputs],
        input_output_aliases={skip + i: i for i in range(len(into))},
        cost_estimate=pl.CostEstimate(
            flops=int(flops * share), transcendentals=0,
            bytes_accessed=int(in_bytes + out_bytes),
        ),
    )(*[x for x, _ in inputs], *into)


def combine(near, far):
    return pl.pallas_call(
        combine_kernel,
        out_shape=jax.ShapeDtypeStruct(near.shape, near.dtype),
        cost_estimate=pl.CostEstimate(
            flops=2 * near.size, transcendentals=0, bytes_accessed=3 * near.size * 4
        ),
    )(near, far)


def carry(payload, axis, reverse, reach, cover):
    peers = lax.axis_size(axis)
    reach = min(reach, peers - 1)

    def shift(value, step):
        if reverse:
            pairs = [(j, j - step) for j in range(step, peers)]
        else:
            pairs = [(j, j + step) for j in range(peers - step)]
        return lax.ppermute(value, axis, pairs)

    first_cover, second_cover = cover
    if reach < 1:
        return jnp.zeros_like(payload), second_cover(first_cover())
    got = shift(payload, 1)
    covered_value = first_cover()
    got, covered_value = lax.optimization_barrier((got, covered_value))
    if reach <= 2:
        if reach == 2:
            got = shift(combine(payload, got), 1)
            covered_value = second_cover(covered_value)
            got, covered_value = lax.optimization_barrier((got, covered_value))
            return got, covered_value
        return got, second_cover(covered_value)
    earlier, inclusive = got, combine(payload, got)
    covered = 1
    while covered < reach:
        step = covered + 1
        got = shift(inclusive, step)
        earlier = combine(earlier, got)
        covered = covered + step
        if covered < reach:
            inclusive = combine(inclusive, got)
    return earlier, second_cover(covered_value)


def on_device(queries, keys, values, out_grad, norm_gain, doc_ids):
    head_count, tok_count, head_width = queries.shape
    block_count = doc_ids.shape[0]
    block_len = tok_count // block_count
    gain = norm_gain.reshape(head_count, 1, head_width)
    doc_values = doc_ids.astype(jnp.float32)
    block_pos = jnp.arange(block_count, dtype=jnp.int32)
    same_doc = doc_values[:, None] == doc_values[None, :]
    earlier_mask = (same_doc & (block_pos[None, :] < block_pos[:, None])).astype(jnp.float32)
    later_mask = (same_doc & (block_pos[None, :] > block_pos[:, None])).astype(jnp.float32)
    last_match = (doc_values == doc_values[-1]).astype(jnp.float32)
    first_match = (doc_values == doc_values[0]).astype(jnp.float32)

    def lanes(table, rows):
        return jnp.broadcast_to(table.reshape(rows, 1), (rows, head_width))

    earlier_rows = lanes(earlier_mask, block_count * block_count)
    later_rows = lanes(later_mask, block_count * block_count)
    last_rows = lanes(last_match, block_count)
    first_rows = lanes(first_match, block_count)
    doc_rows = lanes(doc_values + 1.0, block_count)
    last_doc_rows = jnp.broadcast_to(doc_values[-1] + 1.0, (8, head_width))
    first_doc_rows = jnp.broadcast_to(doc_values[0] + 1.0, (8, head_width))

    pair_flops = 2 * head_count * block_count * block_len * block_len * head_width
    full = jax.ShapeDtypeStruct(queries.shape, jnp.bfloat16)
    wide = jax.ShapeDtypeStruct(queries.shape, jnp.float32)
    states = jax.ShapeDtypeStruct((head_count, block_count, head_width, head_width), jnp.float32)
    payload = jax.ShapeDtypeStruct((head_count, head_width + 8, head_width), jnp.float32)
    ctx_size = lax.axis_size("ctx")
    longest_doc = ctx_size * block_count // 2
    reach = (longest_doc - 2) // block_count + 1

    local_prefix, kv_payload = per_head_call(
        functools.partial(state_kernel, block_len),
        [(keys, True), (values, True), (earlier_rows, False), (last_rows, False),
         (last_doc_rows, False)],
        [(states, True), (payload, True)],
        pair_flops // 2,
    )
    prior, intra_part = carry(
        kv_payload,
        "ctx",
        False,
        reach,
        (
            lambda: per_head_call(
                functools.partial(intra_kernel, block_len),
                [(queries, True), (keys, True), (values, True)],
                [(wide, True)],
                2 * pair_flops,
            )[0],
            lambda intra: intra,
        ),
    )
    local_sums, preceding_states = per_head_call(
        functools.partial(forward_kernel, block_len),
        [(intra_part, True), (queries, True), (out_grad, True), (gain, True),
         (local_prefix, True), (prior, True), (doc_rows, False)],
        [(jax.ShapeDtypeStruct((tok_count, 2), jnp.float32), False),
         (jax.ShapeDtypeStruct(states.shape, jnp.bfloat16), True)],
        pair_flops // 2,
    )
    feature_count = head_count * head_width * lax.axis_size(("sub", "head"))
    total_sums = local_sums.T.reshape(2 * tok_count)
    for axis in ("head", "sub"):
        if lax.axis_size(axis) == 2:
            total_sums = total_sums + lax.ppermute(total_sums, axis, [(0, 1), (1, 0)])
        elif lax.axis_size(axis) > 2:
            total_sums = lax.psum(total_sums, axis)
    root_mean = jnp.sqrt(total_sums[:tok_count] / feature_count + 1e-06)
    inner_mean = total_sums[tok_count:] / feature_count
    factor = inner_mean / (root_mean * root_mean)
    coefs = jnp.stack([root_mean, factor], axis=1)
    d_attn, local_suffix, qd_payload = per_head_call(
        functools.partial(grad_kernel, block_len),
        [(queries, True), (intra_part, True), (preceding_states, True), (out_grad, True),
         (gain, True),
         (coefs, False), (later_rows, False), (first_rows, False), (first_doc_rows, False)],
        [(full, True), (states, True), (payload, True)],
        pair_flops // 2,
    )
    half = head_count // 2

    def query_grads(heads, into):
        return per_head_call(
            functools.partial(query_grad_kernel, block_len),
            [(queries, True), (keys, True), (values, True), (d_attn, True),
             (preceding_states, True)],
            [(full, True), (wide, True), (wide, True)],
            5 * pair_flops,
            heads=heads,
            into=into,
        )

    following, (query_gradient, key_intra, value_intra) = carry(
        qd_payload,
        "ctx",
        True,
        reach,
        (
            lambda: query_grads((0, half), ()),
            lambda done: query_grads((half, head_count - half), tuple(done)),
        ),
    )
    key_gradient, value_gradient = per_head_call(
        functools.partial(key_value_grad_kernel, block_len),
        [(key_intra, True), (value_intra, True), (keys, True), (values, True),
         (local_suffix, True), (following, True), (doc_rows, False)],
        [(full, True), (full, True)],
        pair_flops,
    )
    return query_gradient, key_gradient, value_gradient


def solution(mesh):
    return jax.shard_map(
        on_device,
        mesh=mesh,
        in_specs=(
            P(("sub", "head"), ("groups", "ctx"), None),
            P(("sub", "head"), ("groups", "ctx"), None),
            P(("sub", "head"), ("groups", "ctx"), None),
            P(("sub", "head"), ("groups", "ctx"), None),
            P(("sub", "head"), None),
            P(("groups", "ctx")),
        ),
        out_specs=(
            P(("sub", "head"), ("groups", "ctx"), None),
            P(("sub", "head"), ("groups", "ctx"), None),
            P(("sub", "head"), ("groups", "ctx"), None),
        ),
        check_vma=False,
    )
```

```python
import functools
import math

import jax
import jax.numpy as jnp
from jax import lax
from jax.experimental import pallas as pl
from jax.experimental.pallas import tpu as pltpu
from jax.sharding import PartitionSpec as P

_ROWS_MINOR = (((1,), (1,)), ((), ()))
_ROWS_MAJOR = (((0,), (0,)), ((), ()))


def _causal(block_len):
    row_ids = lax.broadcasted_iota(jnp.int32, (block_len, block_len), 0)
    col_ids = lax.broadcasted_iota(jnp.int32, (block_len, block_len), 1)
    return row_ids >= col_ids


def _doc_sum(doc_ref, parts, keep):
    total = jnp.zeros_like(parts[0])
    for c in range(len(parts)):
        total = total + jnp.where(keep(c), parts[c], 0.0)
    return total


def _doc_row(doc_ref, n, shape):
    return jnp.full(shape, doc_ref[n].astype(jnp.float32) + 1.0, jnp.float32)


def _carried(state_ref, doc_ref, n, carry_ref):
    width = carry_ref.shape[2]
    joined = carry_ref[0, width : width + 1, :] == doc_ref[n].astype(jnp.float32) + 1.0
    total = state_ref[0, n] + jnp.where(joined, carry_ref[0, :width, :], 0.0)
    return total.astype(jnp.bfloat16)


def state_kernel(block_len, doc_ref, k_ref, v_ref, prefix_ref, pay_ref):
    count = k_ref.shape[1] // block_len
    width = k_ref.shape[2]
    parts = []
    for n in range(count):
        rows = pl.ds(n * block_len, block_len)
        parts.append(
            lax.dot_general(
                k_ref[0, rows, :], v_ref[0, rows, :], _ROWS_MAJOR,
                preferred_element_type=jnp.float32,
            )
        )
    for b in range(count):
        prefix_ref[0, b] = _doc_sum(
            doc_ref, parts, lambda c: jnp.logical_and(c < b, doc_ref[c] == doc_ref[b])
        )
    pay_ref[0, :width, :] = _doc_sum(doc_ref, parts, lambda c: doc_ref[c] == doc_ref[count - 1])
    pay_ref[0, width:, :] = _doc_row(doc_ref, count - 1, (8, width))


def combine_kernel(near_ref, far_ref, o_ref):
    width = near_ref.shape[2]
    for h in range(near_ref.shape[0]):
        joined = near_ref[h, width : width + 1, :] == far_ref[h, width : width + 1, :]
        o_ref[h, :width, :] = near_ref[h, :width, :] + jnp.where(
            joined, far_ref[h, :width, :], 0.0
        )
        o_ref[h, width:, :] = near_ref[h, width:, :]


def intra_kernel(block_len, q_ref, k_ref, v_ref, o_ref):
    causal = _causal(block_len)
    for n in range(q_ref.shape[1] // block_len):
        rows = pl.ds(n * block_len, block_len)
        q, k, v = q_ref[0, rows, :], k_ref[0, rows, :], v_ref[0, rows, :]
        scores = lax.dot_general(q, k, _ROWS_MINOR, preferred_element_type=jnp.float32)
        probs = jnp.where(causal, scores, 0.0).astype(jnp.bfloat16)
        o_ref[0, rows, :] = jnp.dot(probs, v, preferred_element_type=jnp.float32)


def forward_kernel(
    block_len, doc_ref, i_ref, q_ref, g_ref, n_ref, prefix_ref, carry_ref, o_ref, s_ref
):
    @pl.when(pl.program_id(0) == 0)
    def _():
        o_ref[...] = jnp.zeros_like(o_ref)

    for n in range(q_ref.shape[1] // block_len):
        rows = pl.ds(n * block_len, block_len)
        state = _carried(prefix_ref, doc_ref, n, carry_ref)
        s_ref[0, n] = state
        raw = i_ref[0, rows, :] + jnp.dot(
            q_ref[0, rows, :], state, preferred_element_type=jnp.float32
        )
        scaled = n_ref[0] * g_ref[0, rows, :].astype(jnp.float32)
        o_ref[rows, 0:1] += jnp.sum(raw * raw, axis=1, keepdims=True)
        o_ref[rows, 1:2] += jnp.sum(scaled * raw, axis=1, keepdims=True)


def grad_kernel(
    block_len, doc_ref, q_ref, i_ref, s_ref, g_ref, n_ref, c_ref, d_ref, suffix_ref, pay_ref
):
    count = q_ref.shape[1] // block_len
    width = q_ref.shape[2]
    parts = []
    for n in range(count):
        rows = pl.ds(n * block_len, block_len)
        q = q_ref[0, rows, :]
        raw = i_ref[0, rows, :] + jnp.dot(q, s_ref[0, n], preferred_element_type=jnp.float32)
        scaled = n_ref[0] * g_ref[0, rows, :].astype(jnp.float32)
        root_mean = c_ref[rows, 0:1]
        factor = c_ref[rows, 1:2]
        d = ((scaled - raw * factor) / root_mean).astype(jnp.bfloat16)
        d_ref[0, rows, :] = d
        parts.append(lax.dot_general(q, d, _ROWS_MAJOR, preferred_element_type=jnp.float32))
    for b in range(count):
        suffix_ref[0, b] = _doc_sum(
            doc_ref, parts, lambda c: jnp.logical_and(c > b, doc_ref[c] == doc_ref[b])
        )
    pay_ref[0, :width, :] = _doc_sum(doc_ref, parts, lambda c: doc_ref[c] == doc_ref[0])
    pay_ref[0, width:, :] = _doc_row(doc_ref, 0, (8, width))


def query_grad_kernel(block_len, q_ref, k_ref, v_ref, d_ref, s_ref, dq_ref, dk_ref, dv_ref):
    causal = _causal(block_len)
    for n in range(k_ref.shape[1] // block_len):
        rows = pl.ds(n * block_len, block_len)
        q, k, v = q_ref[0, rows, :], k_ref[0, rows, :], v_ref[0, rows, :]
        d = d_ref[0, rows, :]
        scores = lax.dot_general(q, k, _ROWS_MINOR, preferred_element_type=jnp.float32)
        probs = jnp.where(causal, scores, 0.0).astype(jnp.bfloat16)
        grad_scores = lax.dot_general(d, v, _ROWS_MINOR, preferred_element_type=jnp.float32)
        grad_probs = jnp.where(causal, grad_scores, 0.0).astype(jnp.bfloat16)
        dq = jnp.dot(grad_probs, k, preferred_element_type=jnp.float32)
        dq = dq + lax.dot_general(d, s_ref[0, n], _ROWS_MINOR, preferred_element_type=jnp.float32)
        dq_ref[0, rows, :] = dq.astype(dq_ref.dtype)
        dk_ref[0, rows, :] = lax.dot_general(
            grad_probs, q, _ROWS_MAJOR, preferred_element_type=jnp.float32
        )
        dv_ref[0, rows, :] = lax.dot_general(
            probs, d, _ROWS_MAJOR, preferred_element_type=jnp.float32
        )


def key_value_grad_kernel(
    block_len, doc_ref, ik_ref, iv_ref, k_ref, v_ref, suffix_ref, carry_ref, dk_ref, dv_ref
):
    for n in range(k_ref.shape[1] // block_len):
        rows = pl.ds(n * block_len, block_len)
        state = _carried(suffix_ref, doc_ref, n, carry_ref)
        dk = ik_ref[0, rows, :] + lax.dot_general(
            v_ref[0, rows, :], state, _ROWS_MINOR, preferred_element_type=jnp.float32
        )
        dv = iv_ref[0, rows, :] + jnp.dot(
            k_ref[0, rows, :], state, preferred_element_type=jnp.float32
        )
        dk_ref[0, rows, :] = dk.astype(dk_ref.dtype)
        dv_ref[0, rows, :] = dv.astype(dv_ref.dtype)


def per_head_call(kernel, inputs, outputs, flops, heads=None, into=(), scalars=None):
    def spec(shape, per_head, first):
        if per_head:
            return pl.BlockSpec(
                (1,) + shape[1:], lambda h, *_: (h + first,) + (0,) * (len(shape) - 1)
            )
        return pl.BlockSpec(shape, lambda h, *_: (0,) * len(shape))

    head_count = inputs[0][0].shape[0]
    first, count = heads if heads is not None else (0, head_count)
    share = count / head_count
    in_bytes = sum(x.size * x.dtype.itemsize for x, _ in inputs) * share
    out_bytes = sum(math.prod(o.shape) * o.dtype.itemsize for o, _ in outputs) * share
    lead = 0 if scalars is None else 1
    skip = lead + len(inputs)

    def body(*refs):
        kernel(*refs[:skip], *refs[skip + len(into):])

    grid_spec = pltpu.PrefetchScalarGridSpec(
        num_scalar_prefetch=lead,
        grid=(count,),
        in_specs=[spec(x.shape, h, first) for x, h in inputs]
        + [pl.BlockSpec(memory_space=pl.ANY) for _ in into],
        out_specs=[spec(o.shape, h, first) for o, h in outputs],
    )
    return pl.pallas_call(
        body,
        grid_spec=grid_spec,
        out_shape=[o for o, _ in outputs],
        input_output_aliases={skip + i: i for i in range(len(into))},
        cost_estimate=pl.CostEstimate(
            flops=int(flops * share), transcendentals=0,
            bytes_accessed=int(in_bytes + out_bytes),
        ),
    )(*([] if scalars is None else [scalars]), *[x for x, _ in inputs], *into)


def combine(near, far):
    return pl.pallas_call(
        combine_kernel,
        out_shape=jax.ShapeDtypeStruct(near.shape, near.dtype),
        cost_estimate=pl.CostEstimate(
            flops=2 * near.size, transcendentals=0, bytes_accessed=3 * near.size * 4
        ),
    )(near, far)


def carry(payload, axis, reverse, reach, cover):
    peers = lax.axis_size(axis)
    reach = min(reach, peers - 1)

    def shift(value, step):
        if reverse:
            pairs = [(j, j - step) for j in range(step, peers)]
        else:
            pairs = [(j, j + step) for j in range(peers - step)]
        return lax.ppermute(value, axis, pairs)

    first_cover, second_cover = cover
    if reach < 1:
        return jnp.zeros_like(payload), second_cover(first_cover())
    got = shift(payload, 1)
    covered_value = first_cover()
    got, covered_value = lax.optimization_barrier((got, covered_value))
    if reach <= 2:
        if reach == 2:
            got = shift(combine(payload, got), 1)
            covered_value = second_cover(covered_value)
            got, covered_value = lax.optimization_barrier((got, covered_value))
            return got, covered_value
        return got, second_cover(covered_value)
    earlier, inclusive = got, combine(payload, got)
    covered = 1
    while covered < reach:
        step = covered + 1
        got = shift(inclusive, step)
        earlier = combine(earlier, got)
        covered = covered + step
        if covered < reach:
            inclusive = combine(inclusive, got)
    return earlier, second_cover(covered_value)


def on_device(queries, keys, values, out_grad, norm_gain, doc_ids):
    head_count, tok_count, head_width = queries.shape
    block_count = doc_ids.shape[0]
    block_len = tok_count // block_count
    gain = norm_gain.reshape(head_count, 1, head_width)
    pair_flops = 2 * head_count * block_count * block_len * block_len * head_width
    full = jax.ShapeDtypeStruct(queries.shape, jnp.bfloat16)
    wide = jax.ShapeDtypeStruct(queries.shape, jnp.float32)
    states = jax.ShapeDtypeStruct((head_count, block_count, head_width, head_width), jnp.float32)
    payload = jax.ShapeDtypeStruct((head_count, head_width + 8, head_width), jnp.float32)
    ctx_size = lax.axis_size("ctx")
    longest_doc = ctx_size * block_count // 2
    reach = (longest_doc - 2) // block_count + 1

    local_prefix, kv_payload = per_head_call(
        functools.partial(state_kernel, block_len),
        [(keys, True), (values, True)],
        [(states, True), (payload, True)],
        pair_flops // 2,
        scalars=doc_ids,
    )
    prior, intra_part = carry(
        kv_payload,
        "ctx",
        False,
        reach,
        (
            lambda: per_head_call(
                functools.partial(intra_kernel, block_len),
                [(queries, True), (keys, True), (values, True)],
                [(wide, True)],
                2 * pair_flops,
            )[0],
            lambda intra: intra,
        ),
    )
    local_sums, preceding_states = per_head_call(
        functools.partial(forward_kernel, block_len),
        [(intra_part, True), (queries, True), (out_grad, True), (gain, True),
         (local_prefix, True), (prior, True)],
        [(jax.ShapeDtypeStruct((tok_count, 2), jnp.float32), False),
         (jax.ShapeDtypeStruct(states.shape, jnp.bfloat16), True)],
        pair_flops // 2,
        scalars=doc_ids,
    )
    feature_count = head_count * head_width * lax.axis_size(("sub", "head"))
    total_sums = local_sums.T.reshape(2 * tok_count)
    for axis in ("head", "sub"):
        if lax.axis_size(axis) == 2:
            total_sums = total_sums + lax.ppermute(total_sums, axis, [(0, 1), (1, 0)])
        elif lax.axis_size(axis) > 2:
            total_sums = lax.psum(total_sums, axis)
    root_mean = jnp.sqrt(total_sums[:tok_count] / feature_count + 1e-06)
    inner_mean = total_sums[tok_count:] / feature_count
    factor = inner_mean / (root_mean * root_mean)
    coefs = jnp.stack([root_mean, factor], axis=1)
    d_attn, local_suffix, qd_payload = per_head_call(
        functools.partial(grad_kernel, block_len),
        [(queries, True), (intra_part, True), (preceding_states, True), (out_grad, True),
         (gain, True),
         (coefs, False)],
        [(full, True), (states, True), (payload, True)],
        pair_flops // 2,
        scalars=doc_ids,
    )
    half = head_count // 2

    def query_grads(heads, into):
        return per_head_call(
            functools.partial(query_grad_kernel, block_len),
            [(queries, True), (keys, True), (values, True), (d_attn, True),
             (preceding_states, True)],
            [(full, True), (wide, True), (wide, True)],
            5 * pair_flops,
            heads=heads,
            into=into,
        )

    following, (query_gradient, key_intra, value_intra) = carry(
        qd_payload,
        "ctx",
        True,
        reach,
        (
            lambda: query_grads((0, half), ()),
            lambda done: query_grads((half, head_count - half), tuple(done)),
        ),
    )
    key_gradient, value_gradient = per_head_call(
        functools.partial(key_value_grad_kernel, block_len),
        [(key_intra, True), (value_intra, True), (keys, True), (values, True),
         (local_suffix, True), (following, True)],
        [(full, True), (full, True)],
        pair_flops,
        scalars=doc_ids,
    )
    return query_gradient, key_gradient, value_gradient


def solution(mesh):
    return jax.shard_map(
        on_device,
        mesh=mesh,
        in_specs=(
            P(("sub", "head"), ("groups", "ctx"), None),
            P(("sub", "head"), ("groups", "ctx"), None),
            P(("sub", "head"), ("groups", "ctx"), None),
            P(("sub", "head"), ("groups", "ctx"), None),
            P(("sub", "head"), None),
            P(("groups", "ctx")),
        ),
        out_specs=(
            P(("sub", "head"), ("groups", "ctx"), None),
            P(("sub", "head"), ("groups", "ctx"), None),
            P(("sub", "head"), ("groups", "ctx"), None),
        ),
        check_vma=False,
    )
```

```python
import functools
import math

import jax
import jax.numpy as jnp
from jax import lax
from jax.experimental import pallas as pl
from jax.experimental.pallas import tpu as pltpu
from jax.sharding import PartitionSpec as P

_ROWS_MINOR = (((1,), (1,)), ((), ()))
_ROWS_MAJOR = (((0,), (0,)), ((), ()))


def _causal(block_len):
    row_ids = lax.broadcasted_iota(jnp.int32, (block_len, block_len), 0)
    col_ids = lax.broadcasted_iota(jnp.int32, (block_len, block_len), 1)
    return row_ids >= col_ids


def _doc_sum(doc_ref, parts, keep):
    total = jnp.zeros_like(parts[0])
    for c in range(len(parts)):
        total = total + jnp.where(keep(c), parts[c], 0.0)
    return total


def _doc_row(doc_ref, n, shape):
    return jnp.full(shape, doc_ref[n].astype(jnp.float32) + 1.0, jnp.float32)


def _carried(state_ref, doc_ref, n, carry_ref):
    width = carry_ref.shape[2]
    joined = carry_ref[0, width : width + 1, :] == doc_ref[n].astype(jnp.float32) + 1.0
    total = state_ref[0, n] + jnp.where(joined, carry_ref[0, :width, :], 0.0)
    return total.astype(jnp.bfloat16)


def payload_kernel(doc_ref, kv_ref, pay_ref):
    count = kv_ref.shape[1]
    width = kv_ref.shape[2]
    parts = [kv_ref[0, c] for c in range(count)]
    pay_ref[0, :width, :] = _doc_sum(doc_ref, parts, lambda c: doc_ref[c] == doc_ref[count - 1])
    pay_ref[0, width:, :] = _doc_row(doc_ref, count - 1, (8, width))


def prefix_kernel(doc_ref, kv_ref, prefix_ref):
    count = kv_ref.shape[1]
    parts = [kv_ref[0, c] for c in range(count)]
    for b in range(count):
        prefix_ref[0, b] = _doc_sum(
            doc_ref, parts, lambda c: jnp.logical_and(c < b, doc_ref[c] == doc_ref[b])
        )


def combine_kernel(near_ref, far_ref, o_ref):
    width = near_ref.shape[2]
    for h in range(near_ref.shape[0]):
        joined = near_ref[h, width : width + 1, :] == far_ref[h, width : width + 1, :]
        o_ref[h, :width, :] = near_ref[h, :width, :] + jnp.where(
            joined, far_ref[h, :width, :], 0.0
        )
        o_ref[h, width:, :] = near_ref[h, width:, :]


def intra_kernel(block_len, q_ref, k_ref, v_ref, o_ref):
    causal = _causal(block_len)
    for n in range(q_ref.shape[1] // block_len):
        rows = pl.ds(n * block_len, block_len)
        q, k, v = q_ref[0, rows, :], k_ref[0, rows, :], v_ref[0, rows, :]
        scores = lax.dot_general(q, k, _ROWS_MINOR, preferred_element_type=jnp.float32)
        probs = jnp.where(causal, scores, 0.0).astype(jnp.bfloat16)
        o_ref[0, rows, :] = jnp.dot(probs, v, preferred_element_type=jnp.float32)


def forward_kernel(
    block_len, doc_ref, i_ref, q_ref, g_ref, n_ref, prefix_ref, carry_ref, o_ref, s_ref
):
    @pl.when(pl.program_id(0) == 0)
    def _():
        o_ref[...] = jnp.zeros_like(o_ref)

    for n in range(q_ref.shape[1] // block_len):
        rows = pl.ds(n * block_len, block_len)
        state = _carried(prefix_ref, doc_ref, n, carry_ref)
        s_ref[0, n] = state
        raw = i_ref[0, rows, :] + jnp.dot(
            q_ref[0, rows, :], state, preferred_element_type=jnp.float32
        )
        scaled = n_ref[0] * g_ref[0, rows, :].astype(jnp.float32)
        o_ref[rows, 0:1] += jnp.sum(raw * raw, axis=1, keepdims=True)
        o_ref[rows, 1:2] += jnp.sum(scaled * raw, axis=1, keepdims=True)


def grad_kernel(
    block_len, doc_ref, q_ref, i_ref, s_ref, g_ref, n_ref, c_ref, d_ref, suffix_ref, pay_ref
):
    count = q_ref.shape[1] // block_len
    width = q_ref.shape[2]
    parts = []
    for n in range(count):
        rows = pl.ds(n * block_len, block_len)
        q = q_ref[0, rows, :]
        raw = i_ref[0, rows, :] + jnp.dot(q, s_ref[0, n], preferred_element_type=jnp.float32)
        scaled = n_ref[0] * g_ref[0, rows, :].astype(jnp.float32)
        root_mean = c_ref[rows, 0:1]
        factor = c_ref[rows, 1:2]
        d = ((scaled - raw * factor) / root_mean).astype(jnp.bfloat16)
        d_ref[0, rows, :] = d
        parts.append(lax.dot_general(q, d, _ROWS_MAJOR, preferred_element_type=jnp.float32))
    for b in range(count):
        suffix_ref[0, b] = _doc_sum(
            doc_ref, parts, lambda c: jnp.logical_and(c > b, doc_ref[c] == doc_ref[b])
        )
    pay_ref[0, :width, :] = _doc_sum(doc_ref, parts, lambda c: doc_ref[c] == doc_ref[0])
    pay_ref[0, width:, :] = _doc_row(doc_ref, 0, (8, width))


def query_grad_kernel(block_len, q_ref, k_ref, v_ref, d_ref, s_ref, dq_ref, dk_ref, dv_ref):
    causal = _causal(block_len)
    for n in range(k_ref.shape[1] // block_len):
        rows = pl.ds(n * block_len, block_len)
        q, k, v = q_ref[0, rows, :], k_ref[0, rows, :], v_ref[0, rows, :]
        d = d_ref[0, rows, :]
        scores = lax.dot_general(q, k, _ROWS_MINOR, preferred_element_type=jnp.float32)
        probs = jnp.where(causal, scores, 0.0).astype(jnp.bfloat16)
        grad_scores = lax.dot_general(d, v, _ROWS_MINOR, preferred_element_type=jnp.float32)
        grad_probs = jnp.where(causal, grad_scores, 0.0).astype(jnp.bfloat16)
        dq = jnp.dot(grad_probs, k, preferred_element_type=jnp.float32)
        dq = dq + lax.dot_general(d, s_ref[0, n], _ROWS_MINOR, preferred_element_type=jnp.float32)
        dq_ref[0, rows, :] = dq.astype(dq_ref.dtype)
        dk_ref[0, rows, :] = lax.dot_general(
            grad_probs, q, _ROWS_MAJOR, preferred_element_type=jnp.float32
        )
        dv_ref[0, rows, :] = lax.dot_general(
            probs, d, _ROWS_MAJOR, preferred_element_type=jnp.float32
        )


def key_value_grad_kernel(
    block_len, doc_ref, ik_ref, iv_ref, k_ref, v_ref, suffix_ref, carry_ref, dk_ref, dv_ref
):
    for n in range(k_ref.shape[1] // block_len):
        rows = pl.ds(n * block_len, block_len)
        state = _carried(suffix_ref, doc_ref, n, carry_ref)
        dk = ik_ref[0, rows, :] + lax.dot_general(
            v_ref[0, rows, :], state, _ROWS_MINOR, preferred_element_type=jnp.float32
        )
        dv = iv_ref[0, rows, :] + jnp.dot(
            k_ref[0, rows, :], state, preferred_element_type=jnp.float32
        )
        dk_ref[0, rows, :] = dk.astype(dk_ref.dtype)
        dv_ref[0, rows, :] = dv.astype(dv_ref.dtype)


def per_head_call(kernel, inputs, outputs, flops, heads=None, into=(), scalars=None):
    def spec(shape, per_head, first):
        if per_head:
            return pl.BlockSpec(
                (1,) + shape[1:], lambda h, *_: (h + first,) + (0,) * (len(shape) - 1)
            )
        return pl.BlockSpec(shape, lambda h, *_: (0,) * len(shape))

    head_count = inputs[0][0].shape[0]
    first, count = heads if heads is not None else (0, head_count)
    share = count / head_count
    in_bytes = sum(x.size * x.dtype.itemsize for x, _ in inputs) * share
    out_bytes = sum(math.prod(o.shape) * o.dtype.itemsize for o, _ in outputs) * share
    lead = 0 if scalars is None else 1
    skip = lead + len(inputs)

    def body(*refs):
        kernel(*refs[:skip], *refs[skip + len(into):])

    grid_spec = pltpu.PrefetchScalarGridSpec(
        num_scalar_prefetch=lead,
        grid=(count,),
        in_specs=[spec(x.shape, h, first) for x, h in inputs]
        + [pl.BlockSpec(memory_space=pl.ANY) for _ in into],
        out_specs=[spec(o.shape, h, first) for o, h in outputs],
    )
    return pl.pallas_call(
        body,
        grid_spec=grid_spec,
        out_shape=[o for o, _ in outputs],
        input_output_aliases={skip + i: i for i in range(len(into))},
        cost_estimate=pl.CostEstimate(
            flops=int(flops * share), transcendentals=0,
            bytes_accessed=int(in_bytes + out_bytes),
        ),
    )(*([] if scalars is None else [scalars]), *[x for x, _ in inputs], *into)


def combine(near, far):
    return pl.pallas_call(
        combine_kernel,
        out_shape=jax.ShapeDtypeStruct(near.shape, near.dtype),
        cost_estimate=pl.CostEstimate(
            flops=2 * near.size, transcendentals=0, bytes_accessed=3 * near.size * 4
        ),
    )(near, far)


def carry(payload, axis, reverse, reach, cover):
    peers = lax.axis_size(axis)
    reach = min(reach, peers - 1)

    def shift(value, step):
        if reverse:
            pairs = [(j, j - step) for j in range(step, peers)]
        else:
            pairs = [(j, j + step) for j in range(peers - step)]
        return lax.ppermute(value, axis, pairs)

    first_cover, second_cover = cover
    if reach < 1:
        return jnp.zeros_like(payload), second_cover(first_cover())
    got = shift(payload, 1)
    covered_value = first_cover()
    got, covered_value = lax.optimization_barrier((got, covered_value))
    if reach <= 2:
        if reach == 2:
            got = shift(combine(payload, got), 1)
            covered_value = second_cover(covered_value)
            got, covered_value = lax.optimization_barrier((got, covered_value))
            return got, covered_value
        return got, second_cover(covered_value)
    earlier, inclusive = got, combine(payload, got)
    covered = 1
    while covered < reach:
        step = covered + 1
        got = shift(inclusive, step)
        earlier = combine(earlier, got)
        covered = covered + step
        if covered < reach:
            inclusive = combine(inclusive, got)
    return earlier, second_cover(covered_value)


def on_device(queries, keys, values, out_grad, norm_gain, doc_ids):
    head_count, tok_count, head_width = queries.shape
    block_count = doc_ids.shape[0]
    block_len = tok_count // block_count
    gain = norm_gain.reshape(head_count, 1, head_width)
    pair_flops = 2 * head_count * block_count * block_len * block_len * head_width
    full = jax.ShapeDtypeStruct(queries.shape, jnp.bfloat16)
    wide = jax.ShapeDtypeStruct(queries.shape, jnp.float32)
    states = jax.ShapeDtypeStruct((head_count, block_count, head_width, head_width), jnp.float32)
    payload = jax.ShapeDtypeStruct((head_count, head_width + 8, head_width), jnp.float32)
    ctx_size = lax.axis_size("ctx")
    longest_doc = ctx_size * block_count // 2
    reach = (longest_doc - 2) // block_count + 1

    block_shape = (head_count, block_count, block_len, head_width)
    key_value_block = jnp.einsum(
        "hnid,hnie->hnde",
        keys.reshape(block_shape),
        values.reshape(block_shape),
        preferred_element_type=jnp.float32,
    )
    (kv_payload,) = per_head_call(
        payload_kernel, [(key_value_block, True)], [(payload, True)], 0, scalars=doc_ids
    )
    prior, (intra_part, local_prefix) = carry(
        kv_payload,
        "ctx",
        False,
        reach,
        (
            lambda: per_head_call(
                functools.partial(intra_kernel, block_len),
                [(queries, True), (keys, True), (values, True)],
                [(wide, True)],
                2 * pair_flops,
            )[0],
            lambda intra: (
                intra,
                per_head_call(
                    prefix_kernel, [(key_value_block, True)], [(states, True)], 0,
                    scalars=doc_ids,
                )[0],
            ),
        ),
    )
    local_sums, preceding_states = per_head_call(
        functools.partial(forward_kernel, block_len),
        [(intra_part, True), (queries, True), (out_grad, True), (gain, True),
         (local_prefix, True), (prior, True)],
        [(jax.ShapeDtypeStruct((tok_count, 2), jnp.float32), False),
         (jax.ShapeDtypeStruct(states.shape, jnp.bfloat16), True)],
        pair_flops // 2,
        scalars=doc_ids,
    )
    feature_count = head_count * head_width * lax.axis_size(("sub", "head"))
    total_sums = local_sums.T.reshape(2 * tok_count)
    for axis in ("head", "sub"):
        if lax.axis_size(axis) == 2:
            total_sums = total_sums + lax.ppermute(total_sums, axis, [(0, 1), (1, 0)])
        elif lax.axis_size(axis) > 2:
            total_sums = lax.psum(total_sums, axis)
    root_mean = jnp.sqrt(total_sums[:tok_count] / feature_count + 1e-06)
    inner_mean = total_sums[tok_count:] / feature_count
    factor = inner_mean / (root_mean * root_mean)
    coefs = jnp.stack([root_mean, factor], axis=1)
    d_attn, local_suffix, qd_payload = per_head_call(
        functools.partial(grad_kernel, block_len),
        [(queries, True), (intra_part, True), (preceding_states, True), (out_grad, True),
         (gain, True),
         (coefs, False)],
        [(full, True), (states, True), (payload, True)],
        pair_flops // 2,
        scalars=doc_ids,
    )
    half = head_count // 2

    def query_grads(heads, into):
        return per_head_call(
            functools.partial(query_grad_kernel, block_len),
            [(queries, True), (keys, True), (values, True), (d_attn, True),
             (preceding_states, True)],
            [(full, True), (wide, True), (wide, True)],
            5 * pair_flops,
            heads=heads,
            into=into,
        )

    following, (query_gradient, key_intra, value_intra) = carry(
        qd_payload,
        "ctx",
        True,
        reach,
        (
            lambda: query_grads((0, half), ()),
            lambda done: query_grads((half, head_count - half), tuple(done)),
        ),
    )
    key_gradient, value_gradient = per_head_call(
        functools.partial(key_value_grad_kernel, block_len),
        [(key_intra, True), (value_intra, True), (keys, True), (values, True),
         (local_suffix, True), (following, True)],
        [(full, True), (full, True)],
        pair_flops,
        scalars=doc_ids,
    )
    return query_gradient, key_gradient, value_gradient


def solution(mesh):
    return jax.shard_map(
        on_device,
        mesh=mesh,
        in_specs=(
            P(("sub", "head"), ("groups", "ctx"), None),
            P(("sub", "head"), ("groups", "ctx"), None),
            P(("sub", "head"), ("groups", "ctx"), None),
            P(("sub", "head"), ("groups", "ctx"), None),
            P(("sub", "head"), None),
            P(("groups", "ctx")),
        ),
        out_specs=(
            P(("sub", "head"), ("groups", "ctx"), None),
            P(("sub", "head"), ("groups", "ctx"), None),
            P(("sub", "head"), ("groups", "ctx"), None),
        ),
        check_vma=False,
    )
```

```python
import functools
import math

import jax
import jax.numpy as jnp
from jax import lax
from jax.experimental import pallas as pl
from jax.experimental.pallas import tpu as pltpu
from jax.sharding import PartitionSpec as P

_ROWS_MINOR = (((1,), (1,)), ((), ()))
_ROWS_MAJOR = (((0,), (0,)), ((), ()))


def _causal(block_len):
    row_ids = lax.broadcasted_iota(jnp.int32, (block_len, block_len), 0)
    col_ids = lax.broadcasted_iota(jnp.int32, (block_len, block_len), 1)
    return row_ids >= col_ids


def _doc_sum(doc_ref, parts, keep):
    total = jnp.zeros_like(parts[0])
    for c in range(len(parts)):
        total = total + jnp.where(keep(c), parts[c], 0.0)
    return total


def _doc_row(doc_ref, n, shape):
    return jnp.full(shape, doc_ref[n].astype(jnp.float32) + 1.0, jnp.float32)


def _carried(state_ref, doc_ref, n, carry_ref, j):
    width = carry_ref.shape[2]
    joined = carry_ref[j, width : width + 1, :] == doc_ref[n].astype(jnp.float32) + 1.0
    total = state_ref[j, n] + jnp.where(joined, carry_ref[j, :width, :], 0.0)
    return total.astype(jnp.bfloat16)


def state_kernel(block_len, doc_ref, k_ref, v_ref, prefix_ref, pay_ref):
    for j in range(k_ref.shape[0]):
        count = k_ref.shape[1] // block_len
        width = k_ref.shape[2]
        parts = []
        for n in range(count):
            rows = pl.ds(n * block_len, block_len)
            parts.append(
                lax.dot_general(
                    k_ref[j, rows, :], v_ref[j, rows, :], _ROWS_MAJOR,
                    preferred_element_type=jnp.float32,
                )
            )
        for b in range(count):
            prefix_ref[j, b] = _doc_sum(
                doc_ref, parts, lambda c: jnp.logical_and(c < b, doc_ref[c] == doc_ref[b])
            )
        pay_ref[j, :width, :] = _doc_sum(doc_ref, parts, lambda c: doc_ref[c] == doc_ref[count - 1])
        pay_ref[j, width:, :] = _doc_row(doc_ref, count - 1, (8, width))


def combine_kernel(near_ref, far_ref, o_ref):
    width = near_ref.shape[2]
    for h in range(near_ref.shape[0]):
        joined = near_ref[h, width : width + 1, :] == far_ref[h, width : width + 1, :]
        o_ref[h, :width, :] = near_ref[h, :width, :] + jnp.where(
            joined, far_ref[h, :width, :], 0.0
        )
        o_ref[h, width:, :] = near_ref[h, width:, :]


def intra_kernel(block_len, q_ref, k_ref, v_ref, o_ref):
    for j in range(q_ref.shape[0]):
        causal = _causal(block_len)
        for n in range(q_ref.shape[1] // block_len):
            rows = pl.ds(n * block_len, block_len)
            q, k, v = q_ref[j, rows, :], k_ref[j, rows, :], v_ref[j, rows, :]
            scores = lax.dot_general(q, k, _ROWS_MINOR, preferred_element_type=jnp.float32)
            probs = jnp.where(causal, scores, 0.0).astype(jnp.bfloat16)
            o_ref[j, rows, :] = jnp.dot(probs, v, preferred_element_type=jnp.float32)


def forward_kernel(
    block_len, doc_ref, i_ref, q_ref, g_ref, n_ref, prefix_ref, carry_ref, o_ref, s_ref
):
    @pl.when(pl.program_id(0) == 0)
    def _():
        o_ref[...] = jnp.zeros_like(o_ref)

    for j in range(q_ref.shape[0]):
        for n in range(q_ref.shape[1] // block_len):
            rows = pl.ds(n * block_len, block_len)
            state = _carried(prefix_ref, doc_ref, n, carry_ref, j)
            s_ref[j, n] = state
            raw = i_ref[j, rows, :] + jnp.dot(
                q_ref[j, rows, :], state, preferred_element_type=jnp.float32
            )
            scaled = n_ref[j] * g_ref[j, rows, :].astype(jnp.float32)
            o_ref[rows, 0:1] += jnp.sum(raw * raw, axis=1, keepdims=True)
            o_ref[rows, 1:2] += jnp.sum(scaled * raw, axis=1, keepdims=True)


def grad_kernel(
    block_len, doc_ref, q_ref, i_ref, s_ref, g_ref, n_ref, c_ref, d_ref, suffix_ref, pay_ref
):
    for j in range(q_ref.shape[0]):
        count = q_ref.shape[1] // block_len
        width = q_ref.shape[2]
        parts = []
        for n in range(count):
            rows = pl.ds(n * block_len, block_len)
            q = q_ref[j, rows, :]
            raw = i_ref[j, rows, :] + jnp.dot(q, s_ref[j, n], preferred_element_type=jnp.float32)
            scaled = n_ref[j] * g_ref[j, rows, :].astype(jnp.float32)
            root_mean = c_ref[rows, 0:1]
            factor = c_ref[rows, 1:2]
            d = ((scaled - raw * factor) / root_mean).astype(jnp.bfloat16)
            d_ref[j, rows, :] = d
            parts.append(lax.dot_general(q, d, _ROWS_MAJOR, preferred_element_type=jnp.float32))
        for b in range(count):
            suffix_ref[j, b] = _doc_sum(
                doc_ref, parts, lambda c: jnp.logical_and(c > b, doc_ref[c] == doc_ref[b])
            )
        pay_ref[j, :width, :] = _doc_sum(doc_ref, parts, lambda c: doc_ref[c] == doc_ref[0])
        pay_ref[j, width:, :] = _doc_row(doc_ref, 0, (8, width))


def query_grad_kernel(block_len, q_ref, k_ref, v_ref, d_ref, s_ref, dq_ref, dk_ref, dv_ref):
    for j in range(q_ref.shape[0]):
        causal = _causal(block_len)
        for n in range(k_ref.shape[1] // block_len):
            rows = pl.ds(n * block_len, block_len)
            q, k, v = q_ref[j, rows, :], k_ref[j, rows, :], v_ref[j, rows, :]
            d = d_ref[j, rows, :]
            scores = lax.dot_general(q, k, _ROWS_MINOR, preferred_element_type=jnp.float32)
            probs = jnp.where(causal, scores, 0.0).astype(jnp.bfloat16)
            grad_scores = lax.dot_general(d, v, _ROWS_MINOR, preferred_element_type=jnp.float32)
            grad_probs = jnp.where(causal, grad_scores, 0.0).astype(jnp.bfloat16)
            dq = jnp.dot(grad_probs, k, preferred_element_type=jnp.float32)
            dq = dq + lax.dot_general(d, s_ref[j, n], _ROWS_MINOR, preferred_element_type=jnp.float32)
            dq_ref[j, rows, :] = dq.astype(dq_ref.dtype)
            dk_ref[j, rows, :] = lax.dot_general(
                grad_probs, q, _ROWS_MAJOR, preferred_element_type=jnp.float32
            )
            dv_ref[j, rows, :] = lax.dot_general(
                probs, d, _ROWS_MAJOR, preferred_element_type=jnp.float32
            )


def key_value_grad_kernel(
    block_len, doc_ref, ik_ref, iv_ref, k_ref, v_ref, suffix_ref, carry_ref, dk_ref, dv_ref
):
    for j in range(ik_ref.shape[0]):
        for n in range(k_ref.shape[1] // block_len):
            rows = pl.ds(n * block_len, block_len)
            state = _carried(suffix_ref, doc_ref, n, carry_ref, j)
            dk = ik_ref[j, rows, :] + lax.dot_general(
                v_ref[j, rows, :], state, _ROWS_MINOR, preferred_element_type=jnp.float32
            )
            dv = iv_ref[j, rows, :] + jnp.dot(
                k_ref[j, rows, :], state, preferred_element_type=jnp.float32
            )
            dk_ref[j, rows, :] = dk.astype(dk_ref.dtype)
            dv_ref[j, rows, :] = dv.astype(dv_ref.dtype)


def per_head_call(kernel, inputs, outputs, flops, heads=None, into=(), scalars=None):
    head_count = inputs[0][0].shape[0]
    first, count = heads if heads is not None else (0, head_count)
    group = math.gcd(math.gcd(first, count), 2)

    def spec(shape, per_head, first):
        if per_head:
            return pl.BlockSpec(
                (group,) + shape[1:],
                lambda h, *_: (h + first // group,) + (0,) * (len(shape) - 1),
            )
        return pl.BlockSpec(shape, lambda h, *_: (0,) * len(shape))

    share = count / head_count
    in_bytes = sum(x.size * x.dtype.itemsize for x, _ in inputs) * share
    out_bytes = sum(math.prod(o.shape) * o.dtype.itemsize for o, _ in outputs) * share
    lead = 0 if scalars is None else 1
    skip = lead + len(inputs)

    def body(*refs):
        kernel(*refs[:skip], *refs[skip + len(into):])

    grid_spec = pltpu.PrefetchScalarGridSpec(
        num_scalar_prefetch=lead,
        grid=(count // group,),
        in_specs=[spec(x.shape, h, first) for x, h in inputs]
        + [pl.BlockSpec(memory_space=pl.ANY) for _ in into],
        out_specs=[spec(o.shape, h, first) for o, h in outputs],
    )
    return pl.pallas_call(
        body,
        grid_spec=grid_spec,
        out_shape=[o for o, _ in outputs],
        input_output_aliases={skip + i: i for i in range(len(into))},
        cost_estimate=pl.CostEstimate(
            flops=int(flops * share), transcendentals=0,
            bytes_accessed=int(in_bytes + out_bytes),
        ),
    )(*([] if scalars is None else [scalars]), *[x for x, _ in inputs], *into)


def combine(near, far):
    return pl.pallas_call(
        combine_kernel,
        out_shape=jax.ShapeDtypeStruct(near.shape, near.dtype),
        cost_estimate=pl.CostEstimate(
            flops=2 * near.size, transcendentals=0, bytes_accessed=3 * near.size * 4
        ),
    )(near, far)


def carry(payload, axis, reverse, reach, cover):
    peers = lax.axis_size(axis)
    reach = min(reach, peers - 1)

    def shift(value, step):
        if reverse:
            pairs = [(j, j - step) for j in range(step, peers)]
        else:
            pairs = [(j, j + step) for j in range(peers - step)]
        return lax.ppermute(value, axis, pairs)

    first_cover, second_cover = cover
    if reach < 1:
        return jnp.zeros_like(payload), second_cover(first_cover())
    got = shift(payload, 1)
    covered_value = first_cover()
    got, covered_value = lax.optimization_barrier((got, covered_value))
    if reach <= 2:
        if reach == 2:
            got = shift(combine(payload, got), 1)
            covered_value = second_cover(covered_value)
            got, covered_value = lax.optimization_barrier((got, covered_value))
            return got, covered_value
        return got, second_cover(covered_value)
    earlier, inclusive = got, combine(payload, got)
    covered = 1
    while covered < reach:
        step = covered + 1
        got = shift(inclusive, step)
        earlier = combine(earlier, got)
        covered = covered + step
        if covered < reach:
            inclusive = combine(inclusive, got)
    return earlier, second_cover(covered_value)


def on_device(queries, keys, values, out_grad, norm_gain, doc_ids):
    head_count, tok_count, head_width = queries.shape
    block_count = doc_ids.shape[0]
    block_len = tok_count // block_count
    gain = norm_gain.reshape(head_count, 1, head_width)
    pair_flops = 2 * head_count * block_count * block_len * block_len * head_width
    full = jax.ShapeDtypeStruct(queries.shape, jnp.bfloat16)
    wide = jax.ShapeDtypeStruct(queries.shape, jnp.float32)
    states = jax.ShapeDtypeStruct((head_count, block_count, head_width, head_width), jnp.float32)
    payload = jax.ShapeDtypeStruct((head_count, head_width + 8, head_width), jnp.float32)
    ctx_size = lax.axis_size("ctx")
    longest_doc = ctx_size * block_count // 2
    reach = (longest_doc - 2) // block_count + 1

    local_prefix, kv_payload = per_head_call(
        functools.partial(state_kernel, block_len),
        [(keys, True), (values, True)],
        [(states, True), (payload, True)],
        pair_flops // 2,
        scalars=doc_ids,
    )
    prior, intra_part = carry(
        kv_payload,
        "ctx",
        False,
        reach,
        (
            lambda: per_head_call(
                functools.partial(intra_kernel, block_len),
                [(queries, True), (keys, True), (values, True)],
                [(wide, True)],
                2 * pair_flops,
            )[0],
            lambda intra: intra,
        ),
    )
    local_sums, preceding_states = per_head_call(
        functools.partial(forward_kernel, block_len),
        [(intra_part, True), (queries, True), (out_grad, True), (gain, True),
         (local_prefix, True), (prior, True)],
        [(jax.ShapeDtypeStruct((tok_count, 2), jnp.float32), False),
         (jax.ShapeDtypeStruct(states.shape, jnp.bfloat16), True)],
        pair_flops // 2,
        scalars=doc_ids,
    )
    feature_count = head_count * head_width * lax.axis_size(("sub", "head"))
    total_sums = local_sums.T.reshape(2 * tok_count)
    for axis in ("head", "sub"):
        if lax.axis_size(axis) == 2:
            total_sums = total_sums + lax.ppermute(total_sums, axis, [(0, 1), (1, 0)])
        elif lax.axis_size(axis) > 2:
            total_sums = lax.psum(total_sums, axis)
    root_mean = jnp.sqrt(total_sums[:tok_count] / feature_count + 1e-06)
    inner_mean = total_sums[tok_count:] / feature_count
    factor = inner_mean / (root_mean * root_mean)
    coefs = jnp.stack([root_mean, factor], axis=1)
    d_attn, local_suffix, qd_payload = per_head_call(
        functools.partial(grad_kernel, block_len),
        [(queries, True), (intra_part, True), (preceding_states, True), (out_grad, True),
         (gain, True),
         (coefs, False)],
        [(full, True), (states, True), (payload, True)],
        pair_flops // 2,
        scalars=doc_ids,
    )
    half = head_count // 2

    def query_grads(heads, into):
        return per_head_call(
            functools.partial(query_grad_kernel, block_len),
            [(queries, True), (keys, True), (values, True), (d_attn, True),
             (preceding_states, True)],
            [(full, True), (wide, True), (wide, True)],
            5 * pair_flops,
            heads=heads,
            into=into,
        )

    following, (query_gradient, key_intra, value_intra) = carry(
        qd_payload,
        "ctx",
        True,
        reach,
        (
            lambda: query_grads((0, half), ()),
            lambda done: query_grads((half, head_count - half), tuple(done)),
        ),
    )
    key_gradient, value_gradient = per_head_call(
        functools.partial(key_value_grad_kernel, block_len),
        [(key_intra, True), (value_intra, True), (keys, True), (values, True),
         (local_suffix, True), (following, True)],
        [(full, True), (full, True)],
        pair_flops,
        scalars=doc_ids,
    )
    return query_gradient, key_gradient, value_gradient


def solution(mesh):
    return jax.shard_map(
        on_device,
        mesh=mesh,
        in_specs=(
            P(("sub", "head"), ("groups", "ctx"), None),
            P(("sub", "head"), ("groups", "ctx"), None),
            P(("sub", "head"), ("groups", "ctx"), None),
            P(("sub", "head"), ("groups", "ctx"), None),
            P(("sub", "head"), None),
            P(("groups", "ctx")),
        ),
        out_specs=(
            P(("sub", "head"), ("groups", "ctx"), None),
            P(("sub", "head"), ("groups", "ctx"), None),
            P(("sub", "head"), ("groups", "ctx"), None),
        ),
        check_vma=False,
    )
```

```python
import functools
import math

import jax
import jax.numpy as jnp
from jax import lax
from jax.experimental import pallas as pl
from jax.experimental.pallas import tpu as pltpu
from jax.sharding import PartitionSpec as P

_ROWS_MINOR = (((1,), (1,)), ((), ()))
_ROWS_MAJOR = (((0,), (0,)), ((), ()))


def _causal(block_len):
    row_ids = lax.broadcasted_iota(jnp.int32, (block_len, block_len), 0)
    col_ids = lax.broadcasted_iota(jnp.int32, (block_len, block_len), 1)
    return row_ids >= col_ids


def _doc_sum(doc_ref, parts, keep):
    total = jnp.zeros_like(parts[0])
    for c in range(len(parts)):
        total = total + jnp.where(keep(c), parts[c], 0.0)
    return total


def _doc_row(doc_ref, n, shape):
    return jnp.full(shape, doc_ref[n].astype(jnp.float32) + 1.0, jnp.float32)


def _carried(state_ref, doc_ref, n, carry_ref, j):
    width = carry_ref.shape[2]
    joined = carry_ref[j, width : width + 1, :] == doc_ref[n].astype(jnp.float32) + 1.0
    total = state_ref[j, n] + jnp.where(joined, carry_ref[j, :width, :], 0.0)
    return total.astype(jnp.bfloat16)


def state_kernel(block_len, doc_ref, k_ref, v_ref, prefix_ref, pay_ref):
    for j in range(k_ref.shape[0]):
        count = k_ref.shape[1] // block_len
        width = k_ref.shape[2]
        parts = []
        for n in range(count):
            rows = pl.ds(n * block_len, block_len)
            parts.append(
                lax.dot_general(
                    k_ref[j, rows, :], v_ref[j, rows, :], _ROWS_MAJOR,
                    preferred_element_type=jnp.float32,
                )
            )
        for b in range(count):
            prefix_ref[j, b] = _doc_sum(
                doc_ref, parts, lambda c: jnp.logical_and(c < b, doc_ref[c] == doc_ref[b])
            )
        pay_ref[j, :width, :] = _doc_sum(doc_ref, parts, lambda c: doc_ref[c] == doc_ref[count - 1])
        pay_ref[j, width:, :] = _doc_row(doc_ref, count - 1, (8, width))


def combine_kernel(near_ref, far_ref, o_ref):
    width = near_ref.shape[2]
    for h in range(near_ref.shape[0]):
        joined = near_ref[h, width : width + 1, :] == far_ref[h, width : width + 1, :]
        o_ref[h, :width, :] = near_ref[h, :width, :] + jnp.where(
            joined, far_ref[h, :width, :], 0.0
        )
        o_ref[h, width:, :] = near_ref[h, width:, :]


def intra_kernel(block_len, q_ref, k_ref, v_ref, o_ref):
    for j in range(q_ref.shape[0]):
        causal = _causal(block_len)
        for n in range(q_ref.shape[1] // block_len):
            rows = pl.ds(n * block_len, block_len)
            q, k, v = q_ref[j, rows, :], k_ref[j, rows, :], v_ref[j, rows, :]
            scores = lax.dot_general(q, k, _ROWS_MINOR, preferred_element_type=jnp.float32)
            probs = jnp.where(causal, scores, 0.0).astype(jnp.bfloat16)
            o_ref[j, rows, :] = jnp.dot(probs, v, preferred_element_type=jnp.float32)


def forward_kernel(
    block_len, doc_ref, i_ref, q_ref, g_ref, n_ref, prefix_ref, carry_ref, o_ref, s_ref
):
    @pl.when(pl.program_id(0) == 0)
    def _():
        o_ref[...] = jnp.zeros_like(o_ref)

    for j in range(q_ref.shape[0]):
        for n in range(q_ref.shape[1] // block_len):
            rows = pl.ds(n * block_len, block_len)
            state = _carried(prefix_ref, doc_ref, n, carry_ref, j)
            s_ref[j, n] = state
            raw = i_ref[j, rows, :] + jnp.dot(
                q_ref[j, rows, :], state, preferred_element_type=jnp.float32
            )
            scaled = n_ref[j] * g_ref[j, rows, :].astype(jnp.float32)
            o_ref[rows, 0:1] += jnp.sum(raw * raw, axis=1, keepdims=True)
            o_ref[rows, 1:2] += jnp.sum(scaled * raw, axis=1, keepdims=True)


def grad_kernel(
    block_len, doc_ref, q_ref, i_ref, s_ref, g_ref, n_ref, c_ref, d_ref, suffix_ref, pay_ref
):
    for j in range(q_ref.shape[0]):
        count = q_ref.shape[1] // block_len
        width = q_ref.shape[2]
        parts = []
        for n in range(count):
            rows = pl.ds(n * block_len, block_len)
            q = q_ref[j, rows, :]
            raw = i_ref[j, rows, :] + jnp.dot(q, s_ref[j, n], preferred_element_type=jnp.float32)
            scaled = n_ref[j] * g_ref[j, rows, :].astype(jnp.float32)
            root_mean = c_ref[rows, 0:1]
            factor = c_ref[rows, 1:2]
            d = ((scaled - raw * factor) / root_mean).astype(jnp.bfloat16)
            d_ref[j, rows, :] = d
            parts.append(lax.dot_general(q, d, _ROWS_MAJOR, preferred_element_type=jnp.float32))
        for b in range(count):
            suffix_ref[j, b] = _doc_sum(
                doc_ref, parts, lambda c: jnp.logical_and(c > b, doc_ref[c] == doc_ref[b])
            )
        pay_ref[j, :width, :] = _doc_sum(doc_ref, parts, lambda c: doc_ref[c] == doc_ref[0])
        pay_ref[j, width:, :] = _doc_row(doc_ref, 0, (8, width))


def query_grad_kernel(block_len, q_ref, k_ref, v_ref, d_ref, s_ref, dq_ref, dk_ref, dv_ref):
    for j in range(q_ref.shape[0]):
        causal = _causal(block_len)
        for n in range(k_ref.shape[1] // block_len):
            rows = pl.ds(n * block_len, block_len)
            q, k, v = q_ref[j, rows, :], k_ref[j, rows, :], v_ref[j, rows, :]
            d = d_ref[j, rows, :]
            scores = lax.dot_general(q, k, _ROWS_MINOR, preferred_element_type=jnp.float32)
            probs = jnp.where(causal, scores, 0.0).astype(jnp.bfloat16)
            grad_scores = lax.dot_general(d, v, _ROWS_MINOR, preferred_element_type=jnp.float32)
            grad_probs = jnp.where(causal, grad_scores, 0.0).astype(jnp.bfloat16)
            dq = jnp.dot(grad_probs, k, preferred_element_type=jnp.float32)
            dq = dq + lax.dot_general(d, s_ref[j, n], _ROWS_MINOR, preferred_element_type=jnp.float32)
            dq_ref[j, rows, :] = dq.astype(dq_ref.dtype)
            dk_ref[j, rows, :] = lax.dot_general(
                grad_probs, q, _ROWS_MAJOR, preferred_element_type=jnp.float32
            )
            dv_ref[j, rows, :] = lax.dot_general(
                probs, d, _ROWS_MAJOR, preferred_element_type=jnp.float32
            )


def key_value_grad_kernel(
    block_len, doc_ref, ik_ref, iv_ref, k_ref, v_ref, suffix_ref, carry_ref, dk_ref, dv_ref
):
    for j in range(ik_ref.shape[0]):
        for n in range(k_ref.shape[1] // block_len):
            rows = pl.ds(n * block_len, block_len)
            state = _carried(suffix_ref, doc_ref, n, carry_ref, j)
            dk = ik_ref[j, rows, :] + lax.dot_general(
                v_ref[j, rows, :], state, _ROWS_MINOR, preferred_element_type=jnp.float32
            )
            dv = iv_ref[j, rows, :] + jnp.dot(
                k_ref[j, rows, :], state, preferred_element_type=jnp.float32
            )
            dk_ref[j, rows, :] = dk.astype(dk_ref.dtype)
            dv_ref[j, rows, :] = dv.astype(dv_ref.dtype)


def per_head_call(kernel, inputs, outputs, flops, heads=None, into=(), scalars=None):
    head_count = inputs[0][0].shape[0]
    first, count = heads if heads is not None else (0, head_count)
    group = math.gcd(math.gcd(first, count), 4 if count >= 8 else 2)

    def spec(shape, per_head, first):
        if per_head:
            return pl.BlockSpec(
                (group,) + shape[1:],
                lambda h, *_: (h + first // group,) + (0,) * (len(shape) - 1),
            )
        return pl.BlockSpec(shape, lambda h, *_: (0,) * len(shape))

    share = count / head_count
    in_bytes = sum(x.size * x.dtype.itemsize for x, _ in inputs) * share
    out_bytes = sum(math.prod(o.shape) * o.dtype.itemsize for o, _ in outputs) * share
    lead = 0 if scalars is None else 1
    skip = lead + len(inputs)

    def body(*refs):
        kernel(*refs[:skip], *refs[skip + len(into):])

    grid_spec = pltpu.PrefetchScalarGridSpec(
        num_scalar_prefetch=lead,
        grid=(count // group,),
        in_specs=[spec(x.shape, h, first) for x, h in inputs]
        + [pl.BlockSpec(memory_space=pl.ANY) for _ in into],
        out_specs=[spec(o.shape, h, first) for o, h in outputs],
    )
    return pl.pallas_call(
        body,
        grid_spec=grid_spec,
        out_shape=[o for o, _ in outputs],
        input_output_aliases={skip + i: i for i in range(len(into))},
        cost_estimate=pl.CostEstimate(
            flops=int(flops * share), transcendentals=0,
            bytes_accessed=int(in_bytes + out_bytes),
        ),
    )(*([] if scalars is None else [scalars]), *[x for x, _ in inputs], *into)


def combine(near, far):
    return pl.pallas_call(
        combine_kernel,
        out_shape=jax.ShapeDtypeStruct(near.shape, near.dtype),
        cost_estimate=pl.CostEstimate(
            flops=2 * near.size, transcendentals=0, bytes_accessed=3 * near.size * 4
        ),
    )(near, far)


def carry(payload, axis, reverse, reach, cover):
    peers = lax.axis_size(axis)
    reach = min(reach, peers - 1)

    def shift(value, step):
        if reverse:
            pairs = [(j, j - step) for j in range(step, peers)]
        else:
            pairs = [(j, j + step) for j in range(peers - step)]
        return lax.ppermute(value, axis, pairs)

    first_cover, second_cover = cover
    if reach < 1:
        return jnp.zeros_like(payload), second_cover(first_cover())
    got = shift(payload, 1)
    covered_value = first_cover()
    got, covered_value = lax.optimization_barrier((got, covered_value))
    if reach <= 2:
        if reach == 2:
            got = shift(combine(payload, got), 1)
            covered_value = second_cover(covered_value)
            got, covered_value = lax.optimization_barrier((got, covered_value))
            return got, covered_value
        return got, second_cover(covered_value)
    earlier, inclusive = got, combine(payload, got)
    covered = 1
    while covered < reach:
        step = covered + 1
        got = shift(inclusive, step)
        earlier = combine(earlier, got)
        covered = covered + step
        if covered < reach:
            inclusive = combine(inclusive, got)
    return earlier, second_cover(covered_value)


def on_device(queries, keys, values, out_grad, norm_gain, doc_ids):
    head_count, tok_count, head_width = queries.shape
    block_count = doc_ids.shape[0]
    block_len = tok_count // block_count
    gain = norm_gain.reshape(head_count, 1, head_width)
    pair_flops = 2 * head_count * block_count * block_len * block_len * head_width
    full = jax.ShapeDtypeStruct(queries.shape, jnp.bfloat16)
    wide = jax.ShapeDtypeStruct(queries.shape, jnp.float32)
    states = jax.ShapeDtypeStruct((head_count, block_count, head_width, head_width), jnp.float32)
    payload = jax.ShapeDtypeStruct((head_count, head_width + 8, head_width), jnp.float32)
    ctx_size = lax.axis_size("ctx")
    longest_doc = ctx_size * block_count // 2
    reach = (longest_doc - 2) // block_count + 1

    local_prefix, kv_payload = per_head_call(
        functools.partial(state_kernel, block_len),
        [(keys, True), (values, True)],
        [(states, True), (payload, True)],
        pair_flops // 2,
        scalars=doc_ids,
    )
    prior, intra_part = carry(
        kv_payload,
        "ctx",
        False,
        reach,
        (
            lambda: per_head_call(
                functools.partial(intra_kernel, block_len),
                [(queries, True), (keys, True), (values, True)],
                [(wide, True)],
                2 * pair_flops,
            )[0],
            lambda intra: intra,
        ),
    )
    local_sums, preceding_states = per_head_call(
        functools.partial(forward_kernel, block_len),
        [(intra_part, True), (queries, True), (out_grad, True), (gain, True),
         (local_prefix, True), (prior, True)],
        [(jax.ShapeDtypeStruct((tok_count, 2), jnp.float32), False),
         (jax.ShapeDtypeStruct(states.shape, jnp.bfloat16), True)],
        pair_flops // 2,
        scalars=doc_ids,
    )
    feature_count = head_count * head_width * lax.axis_size(("sub", "head"))
    total_sums = local_sums.T.reshape(2 * tok_count)
    if lax.axis_size("head") == 2 and lax.axis_size("sub") == 2:
        partners = [
            lax.ppermute(total_sums, ("sub", "head"), [(k, k ^ flip) for k in range(4)])
            for flip in (1, 2, 3)
        ]
        total_sums = (total_sums + partners[0]) + (partners[1] + partners[2])
    else:
        total_sums = lax.psum(total_sums, ("sub", "head"))
    root_mean = jnp.sqrt(total_sums[:tok_count] / feature_count + 1e-06)
    inner_mean = total_sums[tok_count:] / feature_count
    factor = inner_mean / (root_mean * root_mean)
    coefs = jnp.stack([root_mean, factor], axis=1)
    d_attn, local_suffix, qd_payload = per_head_call(
        functools.partial(grad_kernel, block_len),
        [(queries, True), (intra_part, True), (preceding_states, True), (out_grad, True),
         (gain, True),
         (coefs, False)],
        [(full, True), (states, True), (payload, True)],
        pair_flops // 2,
        scalars=doc_ids,
    )
    half = head_count // 2

    def query_grads(heads, into):
        return per_head_call(
            functools.partial(query_grad_kernel, block_len),
            [(queries, True), (keys, True), (values, True), (d_attn, True),
             (preceding_states, True)],
            [(full, True), (wide, True), (wide, True)],
            5 * pair_flops,
            heads=heads,
            into=into,
        )

    following, (query_gradient, key_intra, value_intra) = carry(
        qd_payload,
        "ctx",
        True,
        reach,
        (
            lambda: query_grads((0, half), ()),
            lambda done: query_grads((half, head_count - half), tuple(done)),
        ),
    )
    key_gradient, value_gradient = per_head_call(
        functools.partial(key_value_grad_kernel, block_len),
        [(key_intra, True), (value_intra, True), (keys, True), (values, True),
         (local_suffix, True), (following, True)],
        [(full, True), (full, True)],
        pair_flops,
        scalars=doc_ids,
    )
    return query_gradient, key_gradient, value_gradient


def solution(mesh):
    return jax.shard_map(
        on_device,
        mesh=mesh,
        in_specs=(
            P(("sub", "head"), ("groups", "ctx"), None),
            P(("sub", "head"), ("groups", "ctx"), None),
            P(("sub", "head"), ("groups", "ctx"), None),
            P(("sub", "head"), ("groups", "ctx"), None),
            P(("sub", "head"), None),
            P(("groups", "ctx")),
        ),
        out_specs=(
            P(("sub", "head"), ("groups", "ctx"), None),
            P(("sub", "head"), ("groups", "ctx"), None),
            P(("sub", "head"), ("groups", "ctx"), None),
        ),
        check_vma=False,
    )
```

```python
import functools
import math

import jax
import jax.numpy as jnp
from jax import lax
from jax.experimental import pallas as pl
from jax.experimental.pallas import tpu as pltpu
from jax.sharding import PartitionSpec as P

_ROWS_MINOR = (((1,), (1,)), ((), ()))
_ROWS_MAJOR = (((0,), (0,)), ((), ()))


def _causal(block_len):
    row_ids = lax.broadcasted_iota(jnp.int32, (block_len, block_len), 0)
    col_ids = lax.broadcasted_iota(jnp.int32, (block_len, block_len), 1)
    return row_ids >= col_ids


def _doc_sum(doc_ref, parts, keep):
    total = jnp.zeros_like(parts[0])
    for c in range(len(parts)):
        total = total + jnp.where(keep(c), parts[c], 0.0)
    return total


def _doc_row(doc_ref, n, shape):
    return jnp.full(shape, doc_ref[n].astype(jnp.float32) + 1.0, jnp.float32)


def _carried(state_ref, doc_ref, n, carry_ref, j):
    width = carry_ref.shape[2]
    joined = carry_ref[j, width : width + 1, :] == doc_ref[n].astype(jnp.float32) + 1.0
    total = state_ref[j, n] + jnp.where(joined, carry_ref[j, :width, :], 0.0)
    return total.astype(jnp.bfloat16)


def state_kernel(block_len, doc_ref, k_ref, v_ref, prefix_ref, pay_ref):
    for j in range(k_ref.shape[0]):
        count = k_ref.shape[1] // block_len
        width = k_ref.shape[2]
        parts = []
        for n in range(count):
            rows = pl.ds(n * block_len, block_len)
            parts.append(
                lax.dot_general(
                    k_ref[j, rows, :], v_ref[j, rows, :], _ROWS_MAJOR,
                    preferred_element_type=jnp.float32,
                )
            )
        for b in range(count):
            prefix_ref[j, b] = _doc_sum(
                doc_ref, parts, lambda c: jnp.logical_and(c < b, doc_ref[c] == doc_ref[b])
            )
        pay_ref[j, :width, :] = _doc_sum(doc_ref, parts, lambda c: doc_ref[c] == doc_ref[count - 1])
        pay_ref[j, width:, :] = _doc_row(doc_ref, count - 1, (8, width))


def combine_kernel(near_ref, far_ref, o_ref):
    width = near_ref.shape[2]
    for h in range(near_ref.shape[0]):
        joined = near_ref[h, width : width + 1, :] == far_ref[h, width : width + 1, :]
        o_ref[h, :width, :] = near_ref[h, :width, :] + jnp.where(
            joined, far_ref[h, :width, :], 0.0
        )
        o_ref[h, width:, :] = near_ref[h, width:, :]


def intra_kernel(block_len, q_ref, k_ref, v_ref, o_ref):
    for j in range(q_ref.shape[0]):
        causal = _causal(block_len)
        for n in range(q_ref.shape[1] // block_len):
            rows = pl.ds(n * block_len, block_len)
            q, k, v = q_ref[j, rows, :], k_ref[j, rows, :], v_ref[j, rows, :]
            scores = lax.dot_general(q, k, _ROWS_MINOR, preferred_element_type=jnp.float32)
            probs = jnp.where(causal, scores, 0.0).astype(jnp.bfloat16)
            o_ref[j, rows, :] = jnp.dot(probs, v, preferred_element_type=jnp.float32)


def forward_kernel(
    block_len, doc_ref, i_ref, q_ref, g_ref, n_ref, prefix_ref, carry_ref, o_ref, s_ref
):
    @pl.when(pl.program_id(0) == 0)
    def _():
        o_ref[...] = jnp.zeros_like(o_ref)

    for j in range(q_ref.shape[0]):
        for n in range(q_ref.shape[1] // block_len):
            rows = pl.ds(n * block_len, block_len)
            state = _carried(prefix_ref, doc_ref, n, carry_ref, j)
            s_ref[j, n] = state
            raw = i_ref[j, rows, :] + jnp.dot(
                q_ref[j, rows, :], state, preferred_element_type=jnp.float32
            )
            scaled = n_ref[j] * g_ref[j, rows, :].astype(jnp.float32)
            o_ref[rows, 0:1] += jnp.sum(raw * raw, axis=1, keepdims=True)
            o_ref[rows, 1:2] += jnp.sum(scaled * raw, axis=1, keepdims=True)


def grad_kernel(
    block_len, doc_ref, q_ref, i_ref, s_ref, g_ref, n_ref, c_ref, d_ref, suffix_ref, pay_ref
):
    for j in range(q_ref.shape[0]):
        count = q_ref.shape[1] // block_len
        width = q_ref.shape[2]
        parts = []
        for n in range(count):
            rows = pl.ds(n * block_len, block_len)
            q = q_ref[j, rows, :]
            raw = i_ref[j, rows, :] + jnp.dot(q, s_ref[j, n], preferred_element_type=jnp.float32)
            scaled = n_ref[j] * g_ref[j, rows, :].astype(jnp.float32)
            root_mean = c_ref[rows, 0:1]
            factor = c_ref[rows, 1:2]
            d = ((scaled - raw * factor) / root_mean).astype(jnp.bfloat16)
            d_ref[j, rows, :] = d
            parts.append(lax.dot_general(q, d, _ROWS_MAJOR, preferred_element_type=jnp.float32))
        for b in range(count):
            suffix_ref[j, b] = _doc_sum(
                doc_ref, parts, lambda c: jnp.logical_and(c > b, doc_ref[c] == doc_ref[b])
            )
        pay_ref[j, :width, :] = _doc_sum(doc_ref, parts, lambda c: doc_ref[c] == doc_ref[0])
        pay_ref[j, width:, :] = _doc_row(doc_ref, 0, (8, width))


def query_grad_kernel(block_len, q_ref, k_ref, v_ref, d_ref, s_ref, dq_ref, dk_ref, dv_ref):
    for j in range(q_ref.shape[0]):
        causal = _causal(block_len)
        for n in range(k_ref.shape[1] // block_len):
            rows = pl.ds(n * block_len, block_len)
            q, k, v = q_ref[j, rows, :], k_ref[j, rows, :], v_ref[j, rows, :]
            d = d_ref[j, rows, :]
            scores = lax.dot_general(q, k, _ROWS_MINOR, preferred_element_type=jnp.float32)
            probs = jnp.where(causal, scores, 0.0).astype(jnp.bfloat16)
            grad_scores = lax.dot_general(d, v, _ROWS_MINOR, preferred_element_type=jnp.float32)
            grad_probs = jnp.where(causal, grad_scores, 0.0).astype(jnp.bfloat16)
            dq = jnp.dot(grad_probs, k, preferred_element_type=jnp.float32)
            dq = dq + lax.dot_general(d, s_ref[j, n], _ROWS_MINOR, preferred_element_type=jnp.float32)
            dq_ref[j, rows, :] = dq.astype(dq_ref.dtype)
            dk_ref[j, rows, :] = lax.dot_general(
                grad_probs, q, _ROWS_MAJOR, preferred_element_type=jnp.float32
            )
            dv_ref[j, rows, :] = lax.dot_general(
                probs, d, _ROWS_MAJOR, preferred_element_type=jnp.float32
            )


def key_value_grad_kernel(
    block_len, doc_ref, ik_ref, iv_ref, k_ref, v_ref, suffix_ref, carry_ref, dk_ref, dv_ref
):
    for j in range(ik_ref.shape[0]):
        for n in range(k_ref.shape[1] // block_len):
            rows = pl.ds(n * block_len, block_len)
            state = _carried(suffix_ref, doc_ref, n, carry_ref, j)
            dk = ik_ref[j, rows, :] + lax.dot_general(
                v_ref[j, rows, :], state, _ROWS_MINOR, preferred_element_type=jnp.float32
            )
            dv = iv_ref[j, rows, :] + jnp.dot(
                k_ref[j, rows, :], state, preferred_element_type=jnp.float32
            )
            dk_ref[j, rows, :] = dk.astype(dk_ref.dtype)
            dv_ref[j, rows, :] = dv.astype(dv_ref.dtype)


def per_head_call(
    kernel, inputs, outputs, flops, heads=None, into=(), scalars=None, per_step=2
):
    head_count = inputs[0][0].shape[0]
    first, count = heads if heads is not None else (0, head_count)
    group = math.gcd(math.gcd(first, count), per_step)

    def spec(shape, per_head, first):
        if per_head:
            return pl.BlockSpec(
                (group,) + shape[1:],
                lambda h, *_: (h + first // group,) + (0,) * (len(shape) - 1),
            )
        return pl.BlockSpec(shape, lambda h, *_: (0,) * len(shape))

    share = count / head_count
    in_bytes = sum(x.size * x.dtype.itemsize for x, _ in inputs) * share
    out_bytes = sum(math.prod(o.shape) * o.dtype.itemsize for o, _ in outputs) * share
    lead = 0 if scalars is None else 1
    skip = lead + len(inputs)

    def body(*refs):
        kernel(*refs[:skip], *refs[skip + len(into):])

    grid_spec = pltpu.PrefetchScalarGridSpec(
        num_scalar_prefetch=lead,
        grid=(count // group,),
        in_specs=[spec(x.shape, h, first) for x, h in inputs]
        + [pl.BlockSpec(memory_space=pl.ANY) for _ in into],
        out_specs=[spec(o.shape, h, first) for o, h in outputs],
    )
    return pl.pallas_call(
        body,
        grid_spec=grid_spec,
        out_shape=[o for o, _ in outputs],
        input_output_aliases={skip + i: i for i in range(len(into))},
        cost_estimate=pl.CostEstimate(
            flops=int(flops * share), transcendentals=0,
            bytes_accessed=int(in_bytes + out_bytes),
        ),
    )(*([] if scalars is None else [scalars]), *[x for x, _ in inputs], *into)


def combine(near, far):
    return pl.pallas_call(
        combine_kernel,
        out_shape=jax.ShapeDtypeStruct(near.shape, near.dtype),
        cost_estimate=pl.CostEstimate(
            flops=2 * near.size, transcendentals=0, bytes_accessed=3 * near.size * 4
        ),
    )(near, far)


def carry(payload, axis, reverse, reach, cover):
    peers = lax.axis_size(axis)
    reach = min(reach, peers - 1)

    def shift(value, step):
        if reverse:
            pairs = [(j, j - step) for j in range(step, peers)]
        else:
            pairs = [(j, j + step) for j in range(peers - step)]
        return lax.ppermute(value, axis, pairs)

    first_cover, second_cover = cover
    if reach < 1:
        return jnp.zeros_like(payload), second_cover(first_cover())
    got = shift(payload, 1)
    covered_value = first_cover()
    got, covered_value = lax.optimization_barrier((got, covered_value))
    if reach <= 2:
        if reach == 2:
            got = shift(combine(payload, got), 1)
            covered_value = second_cover(covered_value)
            got, covered_value = lax.optimization_barrier((got, covered_value))
            return got, covered_value
        return got, second_cover(covered_value)
    earlier, inclusive = got, combine(payload, got)
    covered = 1
    while covered < reach:
        step = covered + 1
        got = shift(inclusive, step)
        earlier = combine(earlier, got)
        covered = covered + step
        if covered < reach:
            inclusive = combine(inclusive, got)
    return earlier, second_cover(covered_value)


def on_device(queries, keys, values, out_grad, norm_gain, doc_ids):
    head_count, tok_count, head_width = queries.shape
    block_count = doc_ids.shape[0]
    block_len = tok_count // block_count
    gain = norm_gain.reshape(head_count, 1, head_width)
    pair_flops = 2 * head_count * block_count * block_len * block_len * head_width
    full = jax.ShapeDtypeStruct(queries.shape, jnp.bfloat16)
    wide = jax.ShapeDtypeStruct(queries.shape, jnp.float32)
    states = jax.ShapeDtypeStruct((head_count, block_count, head_width, head_width), jnp.float32)
    payload = jax.ShapeDtypeStruct((head_count, head_width + 8, head_width), jnp.float32)
    ctx_size = lax.axis_size("ctx")
    longest_doc = ctx_size * block_count // 2
    reach = (longest_doc - 2) // block_count + 1

    local_prefix, kv_payload = per_head_call(
        functools.partial(state_kernel, block_len),
        [(keys, True), (values, True)],
        [(states, True), (payload, True)],
        pair_flops // 2,
        scalars=doc_ids,
        per_step=4,
    )
    prior, intra_part = carry(
        kv_payload,
        "ctx",
        False,
        reach,
        (
            lambda: per_head_call(
                functools.partial(intra_kernel, block_len),
                [(queries, True), (keys, True), (values, True)],
                [(wide, True)],
                2 * pair_flops,
                per_step=4,
            )[0],
            lambda intra: intra,
        ),
    )
    local_sums, preceding_states = per_head_call(
        functools.partial(forward_kernel, block_len),
        [(intra_part, True), (queries, True), (out_grad, True), (gain, True),
         (local_prefix, True), (prior, True)],
        [(jax.ShapeDtypeStruct((tok_count, 2), jnp.float32), False),
         (jax.ShapeDtypeStruct(states.shape, jnp.bfloat16), True)],
        pair_flops // 2,
        scalars=doc_ids,
        per_step=4,
    )
    feature_count = head_count * head_width * lax.axis_size(("sub", "head"))
    total_sums = local_sums.T.reshape(2 * tok_count)
    if lax.axis_size("head") == 2 and lax.axis_size("sub") == 2:
        partners = [
            lax.ppermute(total_sums, ("sub", "head"), [(k, k ^ flip) for k in range(4)])
            for flip in (1, 2, 3)
        ]
        total_sums = (total_sums + partners[0]) + (partners[1] + partners[2])
    else:
        total_sums = lax.psum(total_sums, ("sub", "head"))
    root_mean = jnp.sqrt(total_sums[:tok_count] / feature_count + 1e-06)
    inner_mean = total_sums[tok_count:] / feature_count
    factor = inner_mean / (root_mean * root_mean)
    coefs = jnp.stack([root_mean, factor], axis=1)
    d_attn, local_suffix, qd_payload = per_head_call(
        functools.partial(grad_kernel, block_len),
        [(queries, True), (intra_part, True), (preceding_states, True), (out_grad, True),
         (gain, True),
         (coefs, False)],
        [(full, True), (states, True), (payload, True)],
        pair_flops // 2,
        scalars=doc_ids,
    )
    half = head_count // 2

    def query_grads(heads, into):
        return per_head_call(
            functools.partial(query_grad_kernel, block_len),
            [(queries, True), (keys, True), (values, True), (d_attn, True),
             (preceding_states, True)],
            [(full, True), (wide, True), (wide, True)],
            5 * pair_flops,
            heads=heads,
            into=into,
        )

    following, (query_gradient, key_intra, value_intra) = carry(
        qd_payload,
        "ctx",
        True,
        reach,
        (
            lambda: query_grads((0, half), ()),
            lambda done: query_grads((half, head_count - half), tuple(done)),
        ),
    )
    key_gradient, value_gradient = per_head_call(
        functools.partial(key_value_grad_kernel, block_len),
        [(key_intra, True), (value_intra, True), (keys, True), (values, True),
         (local_suffix, True), (following, True)],
        [(full, True), (full, True)],
        pair_flops,
        scalars=doc_ids,
    )
    return query_gradient, key_gradient, value_gradient


def solution(mesh):
    return jax.shard_map(
        on_device,
        mesh=mesh,
        in_specs=(
            P(("sub", "head"), ("groups", "ctx"), None),
            P(("sub", "head"), ("groups", "ctx"), None),
            P(("sub", "head"), ("groups", "ctx"), None),
            P(("sub", "head"), ("groups", "ctx"), None),
            P(("sub", "head"), None),
            P(("groups", "ctx")),
        ),
        out_specs=(
            P(("sub", "head"), ("groups", "ctx"), None),
            P(("sub", "head"), ("groups", "ctx"), None),
            P(("sub", "head"), ("groups", "ctx"), None),
        ),
        check_vma=False,
    )
```

```python
import functools
import math

import jax
import jax.numpy as jnp
from jax import lax
from jax.experimental import pallas as pl
from jax.experimental.pallas import tpu as pltpu
from jax.sharding import PartitionSpec as P

_ROWS_MINOR = (((1,), (1,)), ((), ()))
_ROWS_MAJOR = (((0,), (0,)), ((), ()))


def _causal(block_len):
    row_ids = lax.broadcasted_iota(jnp.int32, (block_len, block_len), 0)
    col_ids = lax.broadcasted_iota(jnp.int32, (block_len, block_len), 1)
    return row_ids >= col_ids


def _doc_sum(doc_ref, parts, keep):
    total = jnp.zeros_like(parts[0])
    for c in range(len(parts)):
        total = total + jnp.where(keep(c), parts[c], 0.0)
    return total


def _doc_row(doc_ref, n, shape):
    return jnp.full(shape, doc_ref[n].astype(jnp.float32) + 1.0, jnp.float32)


def _carried(state_ref, doc_ref, n, near_ref, far_ref, j):
    width = near_ref.shape[2]
    near_doc = near_ref[j, width : width + 1, :]
    carried = near_ref[j, :width, :] + jnp.where(
        near_doc == far_ref[j, width : width + 1, :], far_ref[j, :width, :], 0.0
    )
    joined = near_doc == doc_ref[n].astype(jnp.float32) + 1.0
    total = state_ref[j, n] + jnp.where(joined, carried, 0.0)
    return total.astype(jnp.bfloat16)


def state_kernel(block_len, doc_ref, k_ref, v_ref, prefix_ref, pay_ref):
    for j in range(k_ref.shape[0]):
        count = k_ref.shape[1] // block_len
        width = k_ref.shape[2]
        parts = []
        for n in range(count):
            rows = pl.ds(n * block_len, block_len)
            parts.append(
                lax.dot_general(
                    k_ref[j, rows, :], v_ref[j, rows, :], _ROWS_MAJOR,
                    preferred_element_type=jnp.float32,
                )
            )
        for b in range(count):
            prefix_ref[j, b] = _doc_sum(
                doc_ref, parts, lambda c: jnp.logical_and(c < b, doc_ref[c] == doc_ref[b])
            )
        pay_ref[j, :width, :] = _doc_sum(doc_ref, parts, lambda c: doc_ref[c] == doc_ref[count - 1])
        pay_ref[j, width:, :] = _doc_row(doc_ref, count - 1, (8, width))


def combine_kernel(near_ref, far_ref, o_ref):
    width = near_ref.shape[2]
    for h in range(near_ref.shape[0]):
        joined = near_ref[h, width : width + 1, :] == far_ref[h, width : width + 1, :]
        o_ref[h, :width, :] = near_ref[h, :width, :] + jnp.where(
            joined, far_ref[h, :width, :], 0.0
        )
        o_ref[h, width:, :] = near_ref[h, width:, :]


def intra_kernel(block_len, q_ref, k_ref, v_ref, o_ref):
    for j in range(q_ref.shape[0]):
        causal = _causal(block_len)
        for n in range(q_ref.shape[1] // block_len):
            rows = pl.ds(n * block_len, block_len)
            q, k, v = q_ref[j, rows, :], k_ref[j, rows, :], v_ref[j, rows, :]
            scores = lax.dot_general(q, k, _ROWS_MINOR, preferred_element_type=jnp.float32)
            probs = jnp.where(causal, scores, 0.0).astype(jnp.bfloat16)
            o_ref[j, rows, :] = jnp.dot(probs, v, preferred_element_type=jnp.float32)


def forward_kernel(
    block_len, doc_ref, i_ref, q_ref, g_ref, n_ref, prefix_ref, near_ref, far_ref, o_ref, s_ref
):
    @pl.when(pl.program_id(0) == 0)
    def _():
        o_ref[...] = jnp.zeros_like(o_ref)

    for j in range(q_ref.shape[0]):
        for n in range(q_ref.shape[1] // block_len):
            rows = pl.ds(n * block_len, block_len)
            state = _carried(prefix_ref, doc_ref, n, near_ref, far_ref, j)
            s_ref[j, n] = state
            raw = i_ref[j, rows, :] + jnp.dot(
                q_ref[j, rows, :], state, preferred_element_type=jnp.float32
            )
            scaled = n_ref[j] * g_ref[j, rows, :].astype(jnp.float32)
            o_ref[rows, 0:1] += jnp.sum(raw * raw, axis=1, keepdims=True)
            o_ref[rows, 1:2] += jnp.sum(scaled * raw, axis=1, keepdims=True)


def grad_kernel(
    block_len, doc_ref, q_ref, i_ref, s_ref, g_ref, n_ref, c_ref, d_ref, suffix_ref, pay_ref
):
    for j in range(q_ref.shape[0]):
        count = q_ref.shape[1] // block_len
        width = q_ref.shape[2]
        parts = []
        for n in range(count):
            rows = pl.ds(n * block_len, block_len)
            q = q_ref[j, rows, :]
            raw = i_ref[j, rows, :] + jnp.dot(q, s_ref[j, n], preferred_element_type=jnp.float32)
            scaled = n_ref[j] * g_ref[j, rows, :].astype(jnp.float32)
            root_mean = c_ref[rows, 0:1]
            factor = c_ref[rows, 1:2]
            d = ((scaled - raw * factor) / root_mean).astype(jnp.bfloat16)
            d_ref[j, rows, :] = d
            parts.append(lax.dot_general(q, d, _ROWS_MAJOR, preferred_element_type=jnp.float32))
        for b in range(count):
            suffix_ref[j, b] = _doc_sum(
                doc_ref, parts, lambda c: jnp.logical_and(c > b, doc_ref[c] == doc_ref[b])
            )
        pay_ref[j, :width, :] = _doc_sum(doc_ref, parts, lambda c: doc_ref[c] == doc_ref[0])
        pay_ref[j, width:, :] = _doc_row(doc_ref, 0, (8, width))


def query_grad_kernel(block_len, q_ref, k_ref, v_ref, d_ref, s_ref, dq_ref, dk_ref, dv_ref):
    for j in range(q_ref.shape[0]):
        causal = _causal(block_len)
        for n in range(k_ref.shape[1] // block_len):
            rows = pl.ds(n * block_len, block_len)
            q, k, v = q_ref[j, rows, :], k_ref[j, rows, :], v_ref[j, rows, :]
            d = d_ref[j, rows, :]
            scores = lax.dot_general(q, k, _ROWS_MINOR, preferred_element_type=jnp.float32)
            probs = jnp.where(causal, scores, 0.0).astype(jnp.bfloat16)
            grad_scores = lax.dot_general(d, v, _ROWS_MINOR, preferred_element_type=jnp.float32)
            grad_probs = jnp.where(causal, grad_scores, 0.0).astype(jnp.bfloat16)
            dq = jnp.dot(grad_probs, k, preferred_element_type=jnp.float32)
            dq = dq + lax.dot_general(d, s_ref[j, n], _ROWS_MINOR, preferred_element_type=jnp.float32)
            dq_ref[j, rows, :] = dq.astype(dq_ref.dtype)
            dk_ref[j, rows, :] = lax.dot_general(
                grad_probs, q, _ROWS_MAJOR, preferred_element_type=jnp.float32
            )
            dv_ref[j, rows, :] = lax.dot_general(
                probs, d, _ROWS_MAJOR, preferred_element_type=jnp.float32
            )


def key_value_grad_kernel(
    block_len, doc_ref, ik_ref, iv_ref, k_ref, v_ref, suffix_ref, near_ref, far_ref, dk_ref,
    dv_ref,
):
    for j in range(ik_ref.shape[0]):
        for n in range(k_ref.shape[1] // block_len):
            rows = pl.ds(n * block_len, block_len)
            state = _carried(suffix_ref, doc_ref, n, near_ref, far_ref, j)
            dk = ik_ref[j, rows, :] + lax.dot_general(
                v_ref[j, rows, :], state, _ROWS_MINOR, preferred_element_type=jnp.float32
            )
            dv = iv_ref[j, rows, :] + jnp.dot(
                k_ref[j, rows, :], state, preferred_element_type=jnp.float32
            )
            dk_ref[j, rows, :] = dk.astype(dk_ref.dtype)
            dv_ref[j, rows, :] = dv.astype(dv_ref.dtype)


def per_head_call(
    kernel, inputs, outputs, flops, heads=None, into=(), scalars=None, per_step=2
):
    head_count = inputs[0][0].shape[0]
    first, count = heads if heads is not None else (0, head_count)
    group = math.gcd(math.gcd(first, count), per_step)

    def spec(shape, per_head, first):
        if per_head:
            return pl.BlockSpec(
                (group,) + shape[1:],
                lambda h, *_: (h + first // group,) + (0,) * (len(shape) - 1),
            )
        return pl.BlockSpec(shape, lambda h, *_: (0,) * len(shape))

    share = count / head_count
    in_bytes = sum(x.size * x.dtype.itemsize for x, _ in inputs) * share
    out_bytes = sum(math.prod(o.shape) * o.dtype.itemsize for o, _ in outputs) * share
    lead = 0 if scalars is None else 1
    skip = lead + len(inputs)

    def body(*refs):
        kernel(*refs[:skip], *refs[skip + len(into):])

    grid_spec = pltpu.PrefetchScalarGridSpec(
        num_scalar_prefetch=lead,
        grid=(count // group,),
        in_specs=[spec(x.shape, h, first) for x, h in inputs]
        + [pl.BlockSpec(memory_space=pl.ANY) for _ in into],
        out_specs=[spec(o.shape, h, first) for o, h in outputs],
    )
    return pl.pallas_call(
        body,
        grid_spec=grid_spec,
        out_shape=[o for o, _ in outputs],
        input_output_aliases={skip + i: i for i in range(len(into))},
        cost_estimate=pl.CostEstimate(
            flops=int(flops * share), transcendentals=0,
            bytes_accessed=int(in_bytes + out_bytes),
        ),
    )(*([] if scalars is None else [scalars]), *[x for x, _ in inputs], *into)


def combine(near, far):
    return pl.pallas_call(
        combine_kernel,
        out_shape=jax.ShapeDtypeStruct(near.shape, near.dtype),
        cost_estimate=pl.CostEstimate(
            flops=2 * near.size, transcendentals=0, bytes_accessed=3 * near.size * 4
        ),
    )(near, far)


def carry(payload, axis, reverse, reach, cover):
    peers = lax.axis_size(axis)
    reach = min(reach, peers - 1)

    def shift(value, step):
        if reverse:
            pairs = [(j, j - step) for j in range(step, peers)]
        else:
            pairs = [(j, j + step) for j in range(peers - step)]
        return lax.ppermute(value, axis, pairs)

    first_cover, second_cover = cover
    none = jnp.zeros_like(payload)
    if reach < 1:
        return (none, none), second_cover(first_cover())
    got = shift(payload, 1)
    covered_value = first_cover()
    got, covered_value = lax.optimization_barrier((got, covered_value))
    if reach <= 2:
        if reach == 2:
            beyond = shift(got, 1)
            covered_value = second_cover(covered_value)
            beyond, covered_value = lax.optimization_barrier((beyond, covered_value))
            return (got, beyond), covered_value
        return (got, none), second_cover(covered_value)
    earlier, inclusive = got, combine(payload, got)
    covered = 1
    while covered < reach:
        step = covered + 1
        got = shift(inclusive, step)
        earlier = combine(earlier, got)
        covered = covered + step
        if covered < reach:
            inclusive = combine(inclusive, got)
    return (earlier, none), second_cover(covered_value)


def on_device(queries, keys, values, out_grad, norm_gain, doc_ids):
    head_count, tok_count, head_width = queries.shape
    block_count = doc_ids.shape[0]
    block_len = tok_count // block_count
    gain = norm_gain.reshape(head_count, 1, head_width)
    pair_flops = 2 * head_count * block_count * block_len * block_len * head_width
    full = jax.ShapeDtypeStruct(queries.shape, jnp.bfloat16)
    wide = jax.ShapeDtypeStruct(queries.shape, jnp.float32)
    states = jax.ShapeDtypeStruct((head_count, block_count, head_width, head_width), jnp.float32)
    payload = jax.ShapeDtypeStruct((head_count, head_width + 8, head_width), jnp.float32)
    ctx_size = lax.axis_size("ctx")
    longest_doc = ctx_size * block_count // 2
    reach = (longest_doc - 2) // block_count + 1

    local_prefix, kv_payload = per_head_call(
        functools.partial(state_kernel, block_len),
        [(keys, True), (values, True)],
        [(states, True), (payload, True)],
        pair_flops // 2,
        scalars=doc_ids,
        per_step=4,
    )
    prior, intra_part = carry(
        kv_payload,
        "ctx",
        False,
        reach,
        (
            lambda: per_head_call(
                functools.partial(intra_kernel, block_len),
                [(queries, True), (keys, True), (values, True)],
                [(wide, True)],
                2 * pair_flops,
                per_step=4,
            )[0],
            lambda intra: intra,
        ),
    )
    local_sums, preceding_states = per_head_call(
        functools.partial(forward_kernel, block_len),
        [(intra_part, True), (queries, True), (out_grad, True), (gain, True),
         (local_prefix, True), (prior[0], True), (prior[1], True)],
        [(jax.ShapeDtypeStruct((tok_count, 2), jnp.float32), False),
         (jax.ShapeDtypeStruct(states.shape, jnp.bfloat16), True)],
        pair_flops // 2,
        scalars=doc_ids,
        per_step=4,
    )
    feature_count = head_count * head_width * lax.axis_size(("sub", "head"))
    total_sums = local_sums.T.reshape(2 * tok_count)
    if lax.axis_size("head") == 2 and lax.axis_size("sub") == 2:
        partners = [
            lax.ppermute(total_sums, ("sub", "head"), [(k, k ^ flip) for k in range(4)])
            for flip in (1, 2, 3)
        ]
        total_sums = (total_sums + partners[0]) + (partners[1] + partners[2])
    else:
        total_sums = lax.psum(total_sums, ("sub", "head"))
    root_mean = jnp.sqrt(total_sums[:tok_count] / feature_count + 1e-06)
    inner_mean = total_sums[tok_count:] / feature_count
    factor = inner_mean / (root_mean * root_mean)
    coefs = jnp.stack([root_mean, factor], axis=1)
    d_attn, local_suffix, qd_payload = per_head_call(
        functools.partial(grad_kernel, block_len),
        [(queries, True), (intra_part, True), (preceding_states, True), (out_grad, True),
         (gain, True),
         (coefs, False)],
        [(full, True), (states, True), (payload, True)],
        pair_flops // 2,
        scalars=doc_ids,
    )
    half = head_count // 2

    def query_grads(heads, into):
        return per_head_call(
            functools.partial(query_grad_kernel, block_len),
            [(queries, True), (keys, True), (values, True), (d_attn, True),
             (preceding_states, True)],
            [(full, True), (wide, True), (wide, True)],
            5 * pair_flops,
            heads=heads,
            into=into,
        )

    following, (query_gradient, key_intra, value_intra) = carry(
        qd_payload,
        "ctx",
        True,
        reach,
        (
            lambda: query_grads((0, half), ()),
            lambda done: query_grads((half, head_count - half), tuple(done)),
        ),
    )
    key_gradient, value_gradient = per_head_call(
        functools.partial(key_value_grad_kernel, block_len),
        [(key_intra, True), (value_intra, True), (keys, True), (values, True),
         (local_suffix, True), (following[0], True), (following[1], True)],
        [(full, True), (full, True)],
        pair_flops,
        scalars=doc_ids,
    )
    return query_gradient, key_gradient, value_gradient


def solution(mesh):
    return jax.shard_map(
        on_device,
        mesh=mesh,
        in_specs=(
            P(("sub", "head"), ("groups", "ctx"), None),
            P(("sub", "head"), ("groups", "ctx"), None),
            P(("sub", "head"), ("groups", "ctx"), None),
            P(("sub", "head"), ("groups", "ctx"), None),
            P(("sub", "head"), None),
            P(("groups", "ctx")),
        ),
        out_specs=(
            P(("sub", "head"), ("groups", "ctx"), None),
            P(("sub", "head"), ("groups", "ctx"), None),
            P(("sub", "head"), ("groups", "ctx"), None),
        ),
        check_vma=False,
    )
```

```python
import functools
import math

import jax
import jax.numpy as jnp
from jax import lax
from jax.experimental import pallas as pl
from jax.experimental.pallas import tpu as pltpu
from jax.sharding import PartitionSpec as P

_ROWS_MINOR = (((1,), (1,)), ((), ()))
_ROWS_MAJOR = (((0,), (0,)), ((), ()))


def _causal(block_len):
    row_ids = lax.broadcasted_iota(jnp.int32, (block_len, block_len), 0)
    col_ids = lax.broadcasted_iota(jnp.int32, (block_len, block_len), 1)
    return row_ids >= col_ids


def _doc_sum(doc_ref, parts, keep):
    total = jnp.zeros_like(parts[0])
    for c in range(len(parts)):
        total = total + jnp.where(keep(c), parts[c], 0.0)
    return total


def _doc_row(doc_ref, n, shape):
    return jnp.full(shape, doc_ref[n].astype(jnp.float32) + 1.0, jnp.float32)


def _carried(state_ref, doc_ref, n, near_ref, far_ref, j):
    width = near_ref.shape[2]
    near_doc = near_ref[j, width : width + 1, :]
    carried = near_ref[j, :width, :] + jnp.where(
        near_doc == far_ref[j, width : width + 1, :], far_ref[j, :width, :], 0.0
    )
    joined = near_doc == doc_ref[n].astype(jnp.float32) + 1.0
    total = state_ref[j, n] + jnp.where(joined, carried, 0.0)
    return total.astype(jnp.bfloat16)


def state_kernel(block_len, doc_ref, k_ref, v_ref, prefix_ref, pay_ref):
    for j in range(k_ref.shape[0]):
        count = k_ref.shape[1] // block_len
        width = k_ref.shape[2]
        parts = []
        for n in range(count):
            rows = pl.ds(n * block_len, block_len)
            parts.append(
                lax.dot_general(
                    k_ref[j, rows, :], v_ref[j, rows, :], _ROWS_MAJOR,
                    preferred_element_type=jnp.float32,
                )
            )
        for b in range(count):
            prefix_ref[j, b] = _doc_sum(
                doc_ref, parts, lambda c: jnp.logical_and(c < b, doc_ref[c] == doc_ref[b])
            )
        pay_ref[j, :width, :] = _doc_sum(doc_ref, parts, lambda c: doc_ref[c] == doc_ref[count - 1])
        pay_ref[j, width:, :] = _doc_row(doc_ref, count - 1, (8, width))


def combine_kernel(near_ref, far_ref, o_ref):
    width = near_ref.shape[2]
    for h in range(near_ref.shape[0]):
        joined = near_ref[h, width : width + 1, :] == far_ref[h, width : width + 1, :]
        o_ref[h, :width, :] = near_ref[h, :width, :] + jnp.where(
            joined, far_ref[h, :width, :], 0.0
        )
        o_ref[h, width:, :] = near_ref[h, width:, :]


def intra_kernel(block_len, q_ref, k_ref, v_ref, o_ref):
    for j in range(q_ref.shape[0]):
        causal = _causal(block_len)
        for n in range(q_ref.shape[1] // block_len):
            rows = pl.ds(n * block_len, block_len)
            q, k, v = q_ref[j, rows, :], k_ref[j, rows, :], v_ref[j, rows, :]
            scores = lax.dot_general(q, k, _ROWS_MINOR, preferred_element_type=jnp.float32)
            probs = jnp.where(causal, scores, 0.0).astype(jnp.bfloat16)
            o_ref[j, rows, :] = jnp.dot(probs, v, preferred_element_type=jnp.float32)


def forward_kernel(
    block_len, doc_ref, i_ref, q_ref, g_ref, n_ref, prefix_ref, near_ref, far_ref, o_ref, s_ref
):
    @pl.when(pl.program_id(0) == 0)
    def _():
        o_ref[...] = jnp.zeros_like(o_ref)

    for j in range(q_ref.shape[0]):
        for n in range(q_ref.shape[1] // block_len):
            rows = pl.ds(n * block_len, block_len)
            state = _carried(prefix_ref, doc_ref, n, near_ref, far_ref, j)
            s_ref[j, n] = state
            raw = i_ref[j, rows, :] + jnp.dot(
                q_ref[j, rows, :], state, preferred_element_type=jnp.float32
            )
            scaled = n_ref[j] * g_ref[j, rows, :].astype(jnp.float32)
            o_ref[rows, 0:1] += jnp.sum(raw * raw, axis=1, keepdims=True)
            o_ref[rows, 1:2] += jnp.sum(scaled * raw, axis=1, keepdims=True)


def grad_kernel(
    block_len, doc_ref, q_ref, i_ref, s_ref, g_ref, n_ref, c_ref, d_ref, suffix_ref, pay_ref
):
    for j in range(q_ref.shape[0]):
        count = q_ref.shape[1] // block_len
        width = q_ref.shape[2]
        parts = []
        for n in range(count):
            rows = pl.ds(n * block_len, block_len)
            q = q_ref[j, rows, :]
            raw = i_ref[j, rows, :] + jnp.dot(q, s_ref[j, n], preferred_element_type=jnp.float32)
            scaled = n_ref[j] * g_ref[j, rows, :].astype(jnp.float32)
            root_mean = c_ref[rows, 0:1]
            factor = c_ref[rows, 1:2]
            d = ((scaled - raw * factor) / root_mean).astype(jnp.bfloat16)
            d_ref[j, rows, :] = d
            parts.append(lax.dot_general(q, d, _ROWS_MAJOR, preferred_element_type=jnp.float32))
        for b in range(count):
            suffix_ref[j, b] = _doc_sum(
                doc_ref, parts, lambda c: jnp.logical_and(c > b, doc_ref[c] == doc_ref[b])
            )
        pay_ref[j, :width, :] = _doc_sum(doc_ref, parts, lambda c: doc_ref[c] == doc_ref[0])
        pay_ref[j, width:, :] = _doc_row(doc_ref, 0, (8, width))


def query_grad_kernel(block_len, q_ref, k_ref, v_ref, d_ref, s_ref, dq_ref, dk_ref, dv_ref):
    for j in range(q_ref.shape[0]):
        causal = _causal(block_len)
        for n in range(k_ref.shape[1] // block_len):
            rows = pl.ds(n * block_len, block_len)
            q, k, v = q_ref[j, rows, :], k_ref[j, rows, :], v_ref[j, rows, :]
            d = d_ref[j, rows, :]
            scores = lax.dot_general(q, k, _ROWS_MINOR, preferred_element_type=jnp.float32)
            probs = jnp.where(causal, scores, 0.0).astype(jnp.bfloat16)
            grad_scores = lax.dot_general(d, v, _ROWS_MINOR, preferred_element_type=jnp.float32)
            grad_probs = jnp.where(causal, grad_scores, 0.0).astype(jnp.bfloat16)
            dq = jnp.dot(grad_probs, k, preferred_element_type=jnp.float32)
            dq = dq + lax.dot_general(d, s_ref[j, n], _ROWS_MINOR, preferred_element_type=jnp.float32)
            dq_ref[j, rows, :] = dq.astype(dq_ref.dtype)
            dk_ref[j, rows, :] = lax.dot_general(
                grad_probs, q, _ROWS_MAJOR, preferred_element_type=jnp.float32
            )
            dv_ref[j, rows, :] = lax.dot_general(
                probs, d, _ROWS_MAJOR, preferred_element_type=jnp.float32
            )


def key_value_grad_kernel(
    block_len, doc_ref, ik_ref, iv_ref, k_ref, v_ref, suffix_ref, near_ref, far_ref, dk_ref,
    dv_ref,
):
    for j in range(ik_ref.shape[0]):
        for n in range(k_ref.shape[1] // block_len):
            rows = pl.ds(n * block_len, block_len)
            state = _carried(suffix_ref, doc_ref, n, near_ref, far_ref, j)
            dk = ik_ref[j, rows, :] + lax.dot_general(
                v_ref[j, rows, :], state, _ROWS_MINOR, preferred_element_type=jnp.float32
            )
            dv = iv_ref[j, rows, :] + jnp.dot(
                k_ref[j, rows, :], state, preferred_element_type=jnp.float32
            )
            dk_ref[j, rows, :] = dk.astype(dk_ref.dtype)
            dv_ref[j, rows, :] = dv.astype(dv_ref.dtype)


def per_head_call(
    kernel, inputs, outputs, flops, heads=None, into=(), scalars=None, per_step=2, local=()
):
    head_count = inputs[0][0].shape[0]
    first, count = heads if heads is not None else (0, head_count)
    group = math.gcd(math.gcd(first, count), per_step)

    def spec(shape, per_head, first):
        if per_head:
            return pl.BlockSpec(
                (group,) + shape[1:],
                lambda h, *_: (h + first // group,) + (0,) * (len(shape) - 1),
            )
        return pl.BlockSpec(shape, lambda h, *_: (0,) * len(shape))

    share = count / head_count
    in_bytes = sum(x.size * x.dtype.itemsize for x, _ in inputs) * share
    out_bytes = sum(math.prod(o.shape) * o.dtype.itemsize for o, _ in outputs) * share
    lead = 0 if scalars is None else 1
    skip = lead + len(inputs)

    def body(*refs):
        kernel(*refs[:skip], *refs[skip + len(into):])

    grid_spec = pltpu.PrefetchScalarGridSpec(
        num_scalar_prefetch=lead,
        grid=(count // group,),
        in_specs=[spec(x.shape, h, first) for x, h in inputs]
        + [pl.BlockSpec(memory_space=pl.ANY) for _ in into],
        out_specs=[
            spec(o.shape, h, 0 if i in local else first) for i, (o, h) in enumerate(outputs)
        ],
    )
    return pl.pallas_call(
        body,
        grid_spec=grid_spec,
        out_shape=[o for o, _ in outputs],
        input_output_aliases={skip + i: i for i in range(len(into))},
        cost_estimate=pl.CostEstimate(
            flops=int(flops * share), transcendentals=0,
            bytes_accessed=int(in_bytes + out_bytes),
        ),
    )(*([] if scalars is None else [scalars]), *[x for x, _ in inputs], *into)


def combine(near, far):
    return pl.pallas_call(
        combine_kernel,
        out_shape=jax.ShapeDtypeStruct(near.shape, near.dtype),
        cost_estimate=pl.CostEstimate(
            flops=2 * near.size, transcendentals=0, bytes_accessed=3 * near.size * 4
        ),
    )(near, far)


def shift_along(value, axis, step, reverse):
    peers = lax.axis_size(axis)
    if reverse:
        pairs = [(j, j - step) for j in range(step, peers)]
    else:
        pairs = [(j, j + step) for j in range(peers - step)]
    return lax.ppermute(value, axis, pairs)


def carry(payload, axis, reverse, reach, cover):
    peers = lax.axis_size(axis)
    reach = min(reach, peers - 1)

    def shift(value, step):
        if reverse:
            pairs = [(j, j - step) for j in range(step, peers)]
        else:
            pairs = [(j, j + step) for j in range(peers - step)]
        return lax.ppermute(value, axis, pairs)

    first_cover, second_cover = cover
    none = jnp.zeros_like(payload)
    if reach < 1:
        return (none, none), second_cover(first_cover())
    got = shift(payload, 1)
    covered_value = first_cover()
    got, covered_value = lax.optimization_barrier((got, covered_value))
    if reach <= 2:
        if reach == 2:
            beyond = shift(got, 1)
            covered_value = second_cover(covered_value)
            beyond, covered_value = lax.optimization_barrier((beyond, covered_value))
            return (got, beyond), covered_value
        return (got, none), second_cover(covered_value)
    earlier, inclusive = got, combine(payload, got)
    covered = 1
    while covered < reach:
        step = covered + 1
        got = shift(inclusive, step)
        earlier = combine(earlier, got)
        covered = covered + step
        if covered < reach:
            inclusive = combine(inclusive, got)
    return (earlier, none), second_cover(covered_value)


def on_device(queries, keys, values, out_grad, norm_gain, doc_ids):
    head_count, tok_count, head_width = queries.shape
    block_count = doc_ids.shape[0]
    block_len = tok_count // block_count
    gain = norm_gain.reshape(head_count, 1, head_width)
    pair_flops = 2 * head_count * block_count * block_len * block_len * head_width
    full = jax.ShapeDtypeStruct(queries.shape, jnp.bfloat16)
    wide = jax.ShapeDtypeStruct(queries.shape, jnp.float32)
    states = jax.ShapeDtypeStruct((head_count, block_count, head_width, head_width), jnp.float32)
    payload = jax.ShapeDtypeStruct((head_count, head_width + 8, head_width), jnp.float32)
    ctx_size = lax.axis_size("ctx")
    longest_doc = ctx_size * block_count // 2
    reach = (longest_doc - 2) // block_count + 1

    local_prefix, kv_payload = per_head_call(
        functools.partial(state_kernel, block_len),
        [(keys, True), (values, True)],
        [(states, True), (payload, True)],
        pair_flops // 2,
        scalars=doc_ids,
        per_step=4,
    )
    prior, intra_part = carry(
        kv_payload,
        "ctx",
        False,
        reach,
        (
            lambda: per_head_call(
                functools.partial(intra_kernel, block_len),
                [(queries, True), (keys, True), (values, True)],
                [(wide, True)],
                2 * pair_flops,
                per_step=4,
            )[0],
            lambda intra: intra,
        ),
    )
    local_sums, preceding_states = per_head_call(
        functools.partial(forward_kernel, block_len),
        [(intra_part, True), (queries, True), (out_grad, True), (gain, True),
         (local_prefix, True), (prior[0], True), (prior[1], True)],
        [(jax.ShapeDtypeStruct((tok_count, 2), jnp.float32), False),
         (jax.ShapeDtypeStruct(states.shape, jnp.bfloat16), True)],
        pair_flops // 2,
        scalars=doc_ids,
        per_step=4,
    )
    feature_count = head_count * head_width * lax.axis_size(("sub", "head"))
    total_sums = local_sums.T.reshape(2 * tok_count)
    if lax.axis_size("head") == 2 and lax.axis_size("sub") == 2:
        partners = [
            lax.ppermute(total_sums, ("sub", "head"), [(k, k ^ flip) for k in range(4)])
            for flip in (1, 2, 3)
        ]
        total_sums = (total_sums + partners[0]) + (partners[1] + partners[2])
    else:
        total_sums = lax.psum(total_sums, ("sub", "head"))
    root_mean = jnp.sqrt(total_sums[:tok_count] / feature_count + 1e-06)
    inner_mean = total_sums[tok_count:] / feature_count
    factor = inner_mean / (root_mean * root_mean)
    coefs = jnp.stack([root_mean, factor], axis=1)
    half = head_count // 2

    def grads(heads, into):
        return per_head_call(
            functools.partial(grad_kernel, block_len),
            [(queries, True), (intra_part, True), (preceding_states, True), (out_grad, True),
             (gain, True), (coefs, False)],
            [(full, True), (states, True),
             (jax.ShapeDtypeStruct((heads[1],) + payload.shape[1:], jnp.float32), True)],
            pair_flops // 2,
            scalars=doc_ids,
            heads=heads,
            into=into,
            local=(2,),
        )

    def query_grads(heads, into):
        return per_head_call(
            functools.partial(query_grad_kernel, block_len),
            [(queries, True), (keys, True), (values, True), (d_attn, True),
             (preceding_states, True)],
            [(full, True), (wide, True), (wide, True)],
            5 * pair_flops,
            heads=heads,
            into=into,
        )

    reach_now = min(reach, ctx_size - 1)
    if 1 <= reach_now <= 2 and half * 2 == head_count and half % 2 == 0:
        first_heads, second_heads = (0, half), (half, head_count - half)
        d_attn, local_suffix, first_payload = grads(first_heads, ())
        first_near = shift_along(first_payload, "ctx", 1, True)
        d_attn, local_suffix, second_payload = grads(second_heads, (d_attn, local_suffix))
        first_near, d_attn, local_suffix, second_payload = lax.optimization_barrier(
            (first_near, d_attn, local_suffix, second_payload)
        )
        second_near = shift_along(second_payload, "ctx", 1, True)
        if reach_now == 2:
            first_far = shift_along(first_near, "ctx", 1, True)
        else:
            first_far = jnp.zeros_like(first_near)
        done = query_grads(first_heads, ())
        first_far, second_near, done = lax.optimization_barrier(
            (first_far, second_near, done)
        )
        if reach_now == 2:
            second_far = shift_along(second_near, "ctx", 1, True)
        else:
            second_far = jnp.zeros_like(second_near)
        done = query_grads(second_heads, tuple(done))
        second_far, done = lax.optimization_barrier((second_far, done))
        query_gradient, key_intra, value_intra = done
        following = (
            jnp.concatenate([first_near, second_near], axis=0),
            jnp.concatenate([first_far, second_far], axis=0),
        )
    else:
        d_attn, local_suffix, qd_payload = grads((0, head_count), ())
        following, (query_gradient, key_intra, value_intra) = carry(
            qd_payload,
            "ctx",
            True,
            reach,
            (
                lambda: query_grads((0, half), ()),
                lambda done: query_grads((half, head_count - half), tuple(done)),
            ),
        )
    key_gradient, value_gradient = per_head_call(
        functools.partial(key_value_grad_kernel, block_len),
        [(key_intra, True), (value_intra, True), (keys, True), (values, True),
         (local_suffix, True), (following[0], True), (following[1], True)],
        [(full, True), (full, True)],
        pair_flops,
        scalars=doc_ids,
    )
    return query_gradient, key_gradient, value_gradient


def solution(mesh):
    return jax.shard_map(
        on_device,
        mesh=mesh,
        in_specs=(
            P(("sub", "head"), ("groups", "ctx"), None),
            P(("sub", "head"), ("groups", "ctx"), None),
            P(("sub", "head"), ("groups", "ctx"), None),
            P(("sub", "head"), ("groups", "ctx"), None),
            P(("sub", "head"), None),
            P(("groups", "ctx")),
        ),
        out_specs=(
            P(("sub", "head"), ("groups", "ctx"), None),
            P(("sub", "head"), ("groups", "ctx"), None),
            P(("sub", "head"), ("groups", "ctx"), None),
        ),
        check_vma=False,
    )
```

```python
import functools
import math

import jax
import jax.numpy as jnp
from jax import lax
from jax.experimental import pallas as pl
from jax.experimental.pallas import tpu as pltpu
from jax.sharding import PartitionSpec as P

_ROWS_MINOR = (((1,), (1,)), ((), ()))
_ROWS_MAJOR = (((0,), (0,)), ((), ()))


def _causal(block_len):
    row_ids = lax.broadcasted_iota(jnp.int32, (block_len, block_len), 0)
    col_ids = lax.broadcasted_iota(jnp.int32, (block_len, block_len), 1)
    return row_ids >= col_ids


def _doc_sum(doc_ref, parts, keep):
    total = jnp.zeros_like(parts[0])
    for c in range(len(parts)):
        total = total + jnp.where(keep(c), parts[c], 0.0)
    return total


def _doc_row(doc_ref, n, shape):
    return jnp.full(shape, doc_ref[n].astype(jnp.float32) + 1.0, jnp.float32)


def _carried(state_ref, doc_ref, n, near_ref, far_ref, j):
    width = near_ref.shape[2]
    near_doc = near_ref[j, width : width + 1, :]
    carried = near_ref[j, :width, :] + jnp.where(
        near_doc == far_ref[j, width : width + 1, :], far_ref[j, :width, :], 0.0
    )
    joined = near_doc == doc_ref[n].astype(jnp.float32) + 1.0
    total = state_ref[j, n] + jnp.where(joined, carried, 0.0)
    return total.astype(jnp.bfloat16)


def state_kernel(block_len, doc_ref, k_ref, v_ref, prefix_ref, pay_ref):
    for j in range(k_ref.shape[0]):
        count = k_ref.shape[1] // block_len
        width = k_ref.shape[2]
        parts = []
        for n in range(count):
            rows = pl.ds(n * block_len, block_len)
            parts.append(
                lax.dot_general(
                    k_ref[j, rows, :], v_ref[j, rows, :], _ROWS_MAJOR,
                    preferred_element_type=jnp.float32,
                )
            )
        for b in range(count):
            prefix_ref[j, b] = _doc_sum(
                doc_ref, parts, lambda c: jnp.logical_and(c < b, doc_ref[c] == doc_ref[b])
            )
        pay_ref[j, :width, :] = _doc_sum(doc_ref, parts, lambda c: doc_ref[c] == doc_ref[count - 1])
        pay_ref[j, width:, :] = _doc_row(doc_ref, count - 1, (8, width))


def combine_kernel(near_ref, far_ref, o_ref):
    width = near_ref.shape[2]
    for h in range(near_ref.shape[0]):
        joined = near_ref[h, width : width + 1, :] == far_ref[h, width : width + 1, :]
        o_ref[h, :width, :] = near_ref[h, :width, :] + jnp.where(
            joined, far_ref[h, :width, :], 0.0
        )
        o_ref[h, width:, :] = near_ref[h, width:, :]


def intra_kernel(block_len, q_ref, k_ref, v_ref, o_ref):
    for j in range(q_ref.shape[0]):
        causal = _causal(block_len)
        for n in range(q_ref.shape[1] // block_len):
            rows = pl.ds(n * block_len, block_len)
            q, k, v = q_ref[j, rows, :], k_ref[j, rows, :], v_ref[j, rows, :]
            scores = lax.dot_general(q, k, _ROWS_MINOR, preferred_element_type=jnp.float32)
            probs = jnp.where(causal, scores, 0.0).astype(jnp.bfloat16)
            o_ref[j, rows, :] = jnp.dot(probs, v, preferred_element_type=jnp.float32)


def forward_kernel(
    block_len, doc_ref, i_ref, q_ref, g_ref, n_ref, prefix_ref, near_ref, far_ref, o_ref, s_ref
):
    @pl.when(pl.program_id(0) == 0)
    def _():
        o_ref[...] = jnp.zeros_like(o_ref)

    for j in range(q_ref.shape[0]):
        for n in range(q_ref.shape[1] // block_len):
            rows = pl.ds(n * block_len, block_len)
            state = _carried(prefix_ref, doc_ref, n, near_ref, far_ref, j)
            s_ref[j, n] = state
            raw = i_ref[j, rows, :] + jnp.dot(
                q_ref[j, rows, :], state, preferred_element_type=jnp.float32
            )
            scaled = n_ref[j] * g_ref[j, rows, :].astype(jnp.float32)
            lane = lax.broadcasted_iota(jnp.int32, raw.shape, 1)
            tile = jnp.where(
                lane == 0,
                jnp.sum(raw * raw, axis=1, keepdims=True),
                jnp.where(lane == 1, jnp.sum(scaled * raw, axis=1, keepdims=True), 0.0),
            )
            o_ref[:, rows] += tile.T[0:2, :]


def grad_kernel(
    block_len, doc_ref, q_ref, i_ref, s_ref, g_ref, n_ref, c_ref, d_ref, suffix_ref, pay_ref
):
    head_width = q_ref.shape[2]
    for j in range(q_ref.shape[0]):
        count = q_ref.shape[1] // block_len
        width = q_ref.shape[2]
        parts = []
        for n in range(count):
            rows = pl.ds(n * block_len, block_len)
            q = q_ref[j, rows, :]
            raw = i_ref[j, rows, :] + jnp.dot(q, s_ref[j, n], preferred_element_type=jnp.float32)
            scaled = n_ref[j] * g_ref[j, rows, :].astype(jnp.float32)
            row = lax.broadcasted_iota(jnp.int32, (head_width, block_len), 0)
            table = jnp.where(
                row == 0, c_ref[0:1, rows], jnp.where(row == 1, c_ref[1:2, rows], 0.0)
            ).T
            root_mean = table[:, 0:1]
            factor = table[:, 1:2]
            d = ((scaled - raw * factor) / root_mean).astype(jnp.bfloat16)
            d_ref[j, rows, :] = d
            parts.append(lax.dot_general(q, d, _ROWS_MAJOR, preferred_element_type=jnp.float32))
        for b in range(count):
            suffix_ref[j, b] = _doc_sum(
                doc_ref, parts, lambda c: jnp.logical_and(c > b, doc_ref[c] == doc_ref[b])
            )
        pay_ref[j, :width, :] = _doc_sum(doc_ref, parts, lambda c: doc_ref[c] == doc_ref[0])
        pay_ref[j, width:, :] = _doc_row(doc_ref, 0, (8, width))


def query_grad_kernel(block_len, q_ref, k_ref, v_ref, d_ref, s_ref, dq_ref, dk_ref, dv_ref):
    for j in range(q_ref.shape[0]):
        causal = _causal(block_len)
        for n in range(k_ref.shape[1] // block_len):
            rows = pl.ds(n * block_len, block_len)
            q, k, v = q_ref[j, rows, :], k_ref[j, rows, :], v_ref[j, rows, :]
            d = d_ref[j, rows, :]
            scores = lax.dot_general(q, k, _ROWS_MINOR, preferred_element_type=jnp.float32)
            probs = jnp.where(causal, scores, 0.0).astype(jnp.bfloat16)
            grad_scores = lax.dot_general(d, v, _ROWS_MINOR, preferred_element_type=jnp.float32)
            grad_probs = jnp.where(causal, grad_scores, 0.0).astype(jnp.bfloat16)
            dq = jnp.dot(grad_probs, k, preferred_element_type=jnp.float32)
            dq = dq + lax.dot_general(d, s_ref[j, n], _ROWS_MINOR, preferred_element_type=jnp.float32)
            dq_ref[j, rows, :] = dq.astype(dq_ref.dtype)
            dk_ref[j, rows, :] = lax.dot_general(
                grad_probs, q, _ROWS_MAJOR, preferred_element_type=jnp.float32
            )
            dv_ref[j, rows, :] = lax.dot_general(
                probs, d, _ROWS_MAJOR, preferred_element_type=jnp.float32
            )


def key_value_grad_kernel(
    block_len, doc_ref, ik_ref, iv_ref, k_ref, v_ref, suffix_ref, near_ref, far_ref, dk_ref,
    dv_ref,
):
    for j in range(ik_ref.shape[0]):
        for n in range(k_ref.shape[1] // block_len):
            rows = pl.ds(n * block_len, block_len)
            state = _carried(suffix_ref, doc_ref, n, near_ref, far_ref, j)
            dk = ik_ref[j, rows, :] + lax.dot_general(
                v_ref[j, rows, :], state, _ROWS_MINOR, preferred_element_type=jnp.float32
            )
            dv = iv_ref[j, rows, :] + jnp.dot(
                k_ref[j, rows, :], state, preferred_element_type=jnp.float32
            )
            dk_ref[j, rows, :] = dk.astype(dk_ref.dtype)
            dv_ref[j, rows, :] = dv.astype(dv_ref.dtype)


def per_head_call(
    kernel, inputs, outputs, flops, heads=None, into=(), scalars=None, per_step=2
):
    head_count = inputs[0][0].shape[0]
    first, count = heads if heads is not None else (0, head_count)
    group = math.gcd(math.gcd(first, count), per_step)

    def spec(shape, per_head, first):
        if per_head:
            return pl.BlockSpec(
                (group,) + shape[1:],
                lambda h, *_: (h + first // group,) + (0,) * (len(shape) - 1),
            )
        return pl.BlockSpec(shape, lambda h, *_: (0,) * len(shape))

    share = count / head_count
    in_bytes = sum(x.size * x.dtype.itemsize for x, _ in inputs) * share
    out_bytes = sum(math.prod(o.shape) * o.dtype.itemsize for o, _ in outputs) * share
    lead = 0 if scalars is None else 1
    skip = lead + len(inputs)

    def body(*refs):
        kernel(*refs[:skip], *refs[skip + len(into):])

    grid_spec = pltpu.PrefetchScalarGridSpec(
        num_scalar_prefetch=lead,
        grid=(count // group,),
        in_specs=[spec(x.shape, h, first) for x, h in inputs]
        + [pl.BlockSpec(memory_space=pl.ANY) for _ in into],
        out_specs=[spec(o.shape, h, first) for o, h in outputs],
    )
    return pl.pallas_call(
        body,
        grid_spec=grid_spec,
        out_shape=[o for o, _ in outputs],
        input_output_aliases={skip + i: i for i in range(len(into))},
        cost_estimate=pl.CostEstimate(
            flops=int(flops * share), transcendentals=0,
            bytes_accessed=int(in_bytes + out_bytes),
        ),
    )(*([] if scalars is None else [scalars]), *[x for x, _ in inputs], *into)


def combine(near, far):
    return pl.pallas_call(
        combine_kernel,
        out_shape=jax.ShapeDtypeStruct(near.shape, near.dtype),
        cost_estimate=pl.CostEstimate(
            flops=2 * near.size, transcendentals=0, bytes_accessed=3 * near.size * 4
        ),
    )(near, far)


def carry(payload, axis, reverse, reach, cover):
    peers = lax.axis_size(axis)
    reach = min(reach, peers - 1)

    def shift(value, step):
        if reverse:
            pairs = [(j, j - step) for j in range(step, peers)]
        else:
            pairs = [(j, j + step) for j in range(peers - step)]
        return lax.ppermute(value, axis, pairs)

    first_cover, second_cover = cover
    none = jnp.zeros_like(payload)
    if reach < 1:
        return (none, none), second_cover(first_cover())
    got = shift(payload, 1)
    covered_value = first_cover()
    got, covered_value = lax.optimization_barrier((got, covered_value))
    if reach <= 2:
        if reach == 2:
            beyond = shift(got, 1)
            covered_value = second_cover(covered_value)
            beyond, covered_value = lax.optimization_barrier((beyond, covered_value))
            return (got, beyond), covered_value
        return (got, none), second_cover(covered_value)
    earlier, inclusive = got, combine(payload, got)
    covered = 1
    while covered < reach:
        step = covered + 1
        got = shift(inclusive, step)
        earlier = combine(earlier, got)
        covered = covered + step
        if covered < reach:
            inclusive = combine(inclusive, got)
    return (earlier, none), second_cover(covered_value)


def on_device(queries, keys, values, out_grad, norm_gain, doc_ids):
    head_count, tok_count, head_width = queries.shape
    block_count = doc_ids.shape[0]
    block_len = tok_count // block_count
    gain = norm_gain.reshape(head_count, 1, head_width)
    pair_flops = 2 * head_count * block_count * block_len * block_len * head_width
    full = jax.ShapeDtypeStruct(queries.shape, jnp.bfloat16)
    wide = jax.ShapeDtypeStruct(queries.shape, jnp.float32)
    states = jax.ShapeDtypeStruct((head_count, block_count, head_width, head_width), jnp.float32)
    payload = jax.ShapeDtypeStruct((head_count, head_width + 8, head_width), jnp.float32)
    ctx_size = lax.axis_size("ctx")
    longest_doc = ctx_size * block_count // 2
    reach = (longest_doc - 2) // block_count + 1

    local_prefix, kv_payload = per_head_call(
        functools.partial(state_kernel, block_len),
        [(keys, True), (values, True)],
        [(states, True), (payload, True)],
        pair_flops // 2,
        scalars=doc_ids,
        per_step=4,
    )
    prior, intra_part = carry(
        kv_payload,
        "ctx",
        False,
        reach,
        (
            lambda: per_head_call(
                functools.partial(intra_kernel, block_len),
                [(queries, True), (keys, True), (values, True)],
                [(wide, True)],
                2 * pair_flops,
                per_step=4,
            )[0],
            lambda intra: intra,
        ),
    )
    local_sums, preceding_states = per_head_call(
        functools.partial(forward_kernel, block_len),
        [(intra_part, True), (queries, True), (out_grad, True), (gain, True),
         (local_prefix, True), (prior[0], True), (prior[1], True)],
        [(jax.ShapeDtypeStruct((2, tok_count), jnp.float32), False),
         (jax.ShapeDtypeStruct(states.shape, jnp.bfloat16), True)],
        pair_flops // 2,
        scalars=doc_ids,
        per_step=4,
    )
    feature_count = head_count * head_width * lax.axis_size(("sub", "head"))
    total_sums = local_sums
    if lax.axis_size("head") == 2 and lax.axis_size("sub") == 2:
        partners = [
            lax.ppermute(total_sums, ("sub", "head"), [(k, k ^ flip) for k in range(4)])
            for flip in (1, 2, 3)
        ]
        total_sums = (total_sums + partners[0]) + (partners[1] + partners[2])
    else:
        total_sums = lax.psum(total_sums, ("sub", "head"))
    root_mean = jnp.sqrt(total_sums[0] / feature_count + 1e-06)
    inner_mean = total_sums[1] / feature_count
    factor = inner_mean / (root_mean * root_mean)
    coefs = jnp.stack([root_mean, factor], axis=0)
    d_attn, local_suffix, qd_payload = per_head_call(
        functools.partial(grad_kernel, block_len),
        [(queries, True), (intra_part, True), (preceding_states, True), (out_grad, True),
         (gain, True),
         (coefs, False)],
        [(full, True), (states, True), (payload, True)],
        pair_flops // 2,
        scalars=doc_ids,
    )
    half = head_count // 2

    def query_grads(heads, into):
        return per_head_call(
            functools.partial(query_grad_kernel, block_len),
            [(queries, True), (keys, True), (values, True), (d_attn, True),
             (preceding_states, True)],
            [(full, True), (wide, True), (wide, True)],
            5 * pair_flops,
            heads=heads,
            into=into,
        )

    following, (query_gradient, key_intra, value_intra) = carry(
        qd_payload,
        "ctx",
        True,
        reach,
        (
            lambda: query_grads((0, half), ()),
            lambda done: query_grads((half, head_count - half), tuple(done)),
        ),
    )
    key_gradient, value_gradient = per_head_call(
        functools.partial(key_value_grad_kernel, block_len),
        [(key_intra, True), (value_intra, True), (keys, True), (values, True),
         (local_suffix, True), (following[0], True), (following[1], True)],
        [(full, True), (full, True)],
        pair_flops,
        scalars=doc_ids,
    )
    return query_gradient, key_gradient, value_gradient


def solution(mesh):
    return jax.shard_map(
        on_device,
        mesh=mesh,
        in_specs=(
            P(("sub", "head"), ("groups", "ctx"), None),
            P(("sub", "head"), ("groups", "ctx"), None),
            P(("sub", "head"), ("groups", "ctx"), None),
            P(("sub", "head"), ("groups", "ctx"), None),
            P(("sub", "head"), None),
            P(("groups", "ctx")),
        ),
        out_specs=(
            P(("sub", "head"), ("groups", "ctx"), None),
            P(("sub", "head"), ("groups", "ctx"), None),
            P(("sub", "head"), ("groups", "ctx"), None),
        ),
        check_vma=False,
    )
```

```python
import functools
import math

import jax
import jax.numpy as jnp
from jax import lax
from jax.experimental import pallas as pl
from jax.experimental.pallas import tpu as pltpu
from jax.sharding import PartitionSpec as P

_ROWS_MINOR = (((1,), (1,)), ((), ()))
_ROWS_MAJOR = (((0,), (0,)), ((), ()))


def _causal(block_len):
    row_ids = lax.broadcasted_iota(jnp.int32, (block_len, block_len), 0)
    col_ids = lax.broadcasted_iota(jnp.int32, (block_len, block_len), 1)
    return row_ids >= col_ids


def _doc_sum(doc_ref, parts, keep):
    total = jnp.zeros_like(parts[0])
    for c in range(len(parts)):
        total = total + jnp.where(keep(c), parts[c], 0.0)
    return total


def _doc_row(doc_ref, n, shape):
    return jnp.full(shape, doc_ref[n].astype(jnp.float32) + 1.0, jnp.float32)


def _carried(state_ref, doc_ref, n, near_ref, far_ref, j):
    width = near_ref.shape[2]
    near_doc = near_ref[j, width : width + 1, :]
    carried = near_ref[j, :width, :] + jnp.where(
        near_doc == far_ref[j, width : width + 1, :], far_ref[j, :width, :], 0.0
    )
    joined = near_doc == doc_ref[n].astype(jnp.float32) + 1.0
    total = state_ref[j, n] + jnp.where(joined, carried, 0.0)
    return total.astype(jnp.bfloat16)


def state_kernel(block_len, doc_ref, k_ref, v_ref, prefix_ref, pay_ref):
    for j in range(k_ref.shape[0]):
        count = k_ref.shape[1] // block_len
        width = k_ref.shape[2]
        parts = []
        for n in range(count):
            rows = pl.ds(n * block_len, block_len)
            parts.append(
                lax.dot_general(
                    k_ref[j, rows, :], v_ref[j, rows, :], _ROWS_MAJOR,
                    preferred_element_type=jnp.float32,
                )
            )
        for b in range(count):
            prefix_ref[j, b] = _doc_sum(
                doc_ref, parts, lambda c: jnp.logical_and(c < b, doc_ref[c] == doc_ref[b])
            )
        pay_ref[j, :width, :] = _doc_sum(doc_ref, parts, lambda c: doc_ref[c] == doc_ref[count - 1])
        pay_ref[j, width:, :] = _doc_row(doc_ref, count - 1, (8, width))


def combine_kernel(near_ref, far_ref, o_ref):
    width = near_ref.shape[2]
    for h in range(near_ref.shape[0]):
        joined = near_ref[h, width : width + 1, :] == far_ref[h, width : width + 1, :]
        o_ref[h, :width, :] = near_ref[h, :width, :] + jnp.where(
            joined, far_ref[h, :width, :], 0.0
        )
        o_ref[h, width:, :] = near_ref[h, width:, :]


def intra_kernel(block_len, q_ref, k_ref, v_ref, o_ref):
    for j in range(q_ref.shape[0]):
        causal = _causal(block_len)
        for n in range(q_ref.shape[1] // block_len):
            rows = pl.ds(n * block_len, block_len)
            q, k, v = q_ref[j, rows, :], k_ref[j, rows, :], v_ref[j, rows, :]
            scores = lax.dot_general(q, k, _ROWS_MINOR, preferred_element_type=jnp.float32)
            probs = jnp.where(causal, scores, 0.0).astype(jnp.bfloat16)
            o_ref[j, rows, :] = jnp.dot(probs, v, preferred_element_type=jnp.float32)


def forward_kernel(
    block_len, doc_ref, i_ref, q_ref, g_ref, n_ref, prefix_ref, near_ref, far_ref, o_ref, s_ref
):
    @pl.when(pl.program_id(0) == 0)
    def _():
        o_ref[...] = jnp.zeros_like(o_ref)

    for j in range(q_ref.shape[0]):
        for n in range(q_ref.shape[1] // block_len):
            rows = pl.ds(n * block_len, block_len)
            state = _carried(prefix_ref, doc_ref, n, near_ref, far_ref, j)
            s_ref[j, n] = state
            raw = i_ref[j, rows, :] + jnp.dot(
                q_ref[j, rows, :], state, preferred_element_type=jnp.float32
            )
            scaled = n_ref[j] * g_ref[j, rows, :].astype(jnp.float32)
            o_ref[rows, 0:1] += jnp.sum(raw * raw, axis=1, keepdims=True)
            o_ref[rows, 1:2] += jnp.sum(scaled * raw, axis=1, keepdims=True)


def grad_kernel(
    block_len, doc_ref, q_ref, i_ref, s_ref, g_ref, n_ref, c_ref, d_ref, suffix_ref, pay_ref
):
    for j in range(q_ref.shape[0]):
        count = q_ref.shape[1] // block_len
        width = q_ref.shape[2]
        parts = []
        for n in range(count):
            rows = pl.ds(n * block_len, block_len)
            q = q_ref[j, rows, :]
            raw = i_ref[j, rows, :] + jnp.dot(q, s_ref[j, n], preferred_element_type=jnp.float32)
            scaled = n_ref[j] * g_ref[j, rows, :].astype(jnp.float32)
            root_mean = c_ref[rows, 0:1]
            factor = c_ref[rows, 1:2]
            inverse = 1.0 / root_mean
            d = ((scaled - raw * factor) * inverse).astype(jnp.bfloat16)
            d_ref[j, rows, :] = d
            parts.append(lax.dot_general(q, d, _ROWS_MAJOR, preferred_element_type=jnp.float32))
        for b in range(count):
            suffix_ref[j, b] = _doc_sum(
                doc_ref, parts, lambda c: jnp.logical_and(c > b, doc_ref[c] == doc_ref[b])
            )
        pay_ref[j, :width, :] = _doc_sum(doc_ref, parts, lambda c: doc_ref[c] == doc_ref[0])
        pay_ref[j, width:, :] = _doc_row(doc_ref, 0, (8, width))


def query_grad_kernel(block_len, q_ref, k_ref, v_ref, d_ref, s_ref, dq_ref, dk_ref, dv_ref):
    for j in range(q_ref.shape[0]):
        causal = _causal(block_len)
        for n in range(k_ref.shape[1] // block_len):
            rows = pl.ds(n * block_len, block_len)
            q, k, v = q_ref[j, rows, :], k_ref[j, rows, :], v_ref[j, rows, :]
            d = d_ref[j, rows, :]
            scores = lax.dot_general(q, k, _ROWS_MINOR, preferred_element_type=jnp.float32)
            probs = jnp.where(causal, scores, 0.0).astype(jnp.bfloat16)
            grad_scores = lax.dot_general(d, v, _ROWS_MINOR, preferred_element_type=jnp.float32)
            grad_probs = jnp.where(causal, grad_scores, 0.0).astype(jnp.bfloat16)
            dq = jnp.dot(grad_probs, k, preferred_element_type=jnp.float32)
            dq = dq + lax.dot_general(d, s_ref[j, n], _ROWS_MINOR, preferred_element_type=jnp.float32)
            dq_ref[j, rows, :] = dq.astype(dq_ref.dtype)
            dk_ref[j, rows, :] = lax.dot_general(
                grad_probs, q, _ROWS_MAJOR, preferred_element_type=jnp.float32
            )
            dv_ref[j, rows, :] = lax.dot_general(
                probs, d, _ROWS_MAJOR, preferred_element_type=jnp.float32
            )


def key_value_grad_kernel(
    block_len, doc_ref, ik_ref, iv_ref, k_ref, v_ref, suffix_ref, near_ref, far_ref, dk_ref,
    dv_ref,
):
    for j in range(ik_ref.shape[0]):
        for n in range(k_ref.shape[1] // block_len):
            rows = pl.ds(n * block_len, block_len)
            state = _carried(suffix_ref, doc_ref, n, near_ref, far_ref, j)
            dk = ik_ref[j, rows, :] + lax.dot_general(
                v_ref[j, rows, :], state, _ROWS_MINOR, preferred_element_type=jnp.float32
            )
            dv = iv_ref[j, rows, :] + jnp.dot(
                k_ref[j, rows, :], state, preferred_element_type=jnp.float32
            )
            dk_ref[j, rows, :] = dk.astype(dk_ref.dtype)
            dv_ref[j, rows, :] = dv.astype(dv_ref.dtype)


def per_head_call(
    kernel, inputs, outputs, flops, heads=None, into=(), scalars=None, per_step=2
):
    head_count = inputs[0][0].shape[0]
    first, count = heads if heads is not None else (0, head_count)
    group = math.gcd(math.gcd(first, count), per_step)

    def spec(shape, per_head, first):
        if per_head:
            return pl.BlockSpec(
                (group,) + shape[1:],
                lambda h, *_: (h + first // group,) + (0,) * (len(shape) - 1),
            )
        return pl.BlockSpec(shape, lambda h, *_: (0,) * len(shape))

    share = count / head_count
    in_bytes = sum(x.size * x.dtype.itemsize for x, _ in inputs) * share
    out_bytes = sum(math.prod(o.shape) * o.dtype.itemsize for o, _ in outputs) * share
    lead = 0 if scalars is None else 1
    skip = lead + len(inputs)

    def body(*refs):
        kernel(*refs[:skip], *refs[skip + len(into):])

    grid_spec = pltpu.PrefetchScalarGridSpec(
        num_scalar_prefetch=lead,
        grid=(count // group,),
        in_specs=[spec(x.shape, h, first) for x, h in inputs]
        + [pl.BlockSpec(memory_space=pl.ANY) for _ in into],
        out_specs=[spec(o.shape, h, first) for o, h in outputs],
    )
    return pl.pallas_call(
        body,
        grid_spec=grid_spec,
        out_shape=[o for o, _ in outputs],
        input_output_aliases={skip + i: i for i in range(len(into))},
        cost_estimate=pl.CostEstimate(
            flops=int(flops * share), transcendentals=0,
            bytes_accessed=int(in_bytes + out_bytes),
        ),
    )(*([] if scalars is None else [scalars]), *[x for x, _ in inputs], *into)


def combine(near, far):
    return pl.pallas_call(
        combine_kernel,
        out_shape=jax.ShapeDtypeStruct(near.shape, near.dtype),
        cost_estimate=pl.CostEstimate(
            flops=2 * near.size, transcendentals=0, bytes_accessed=3 * near.size * 4
        ),
    )(near, far)


def carry(payload, axis, reverse, reach, cover):
    peers = lax.axis_size(axis)
    reach = min(reach, peers - 1)

    def shift(value, step):
        if reverse:
            pairs = [(j, j - step) for j in range(step, peers)]
        else:
            pairs = [(j, j + step) for j in range(peers - step)]
        return lax.ppermute(value, axis, pairs)

    first_cover, second_cover = cover
    none = jnp.zeros_like(payload)
    if reach < 1:
        return (none, none), second_cover(first_cover())
    got = shift(payload, 1)
    covered_value = first_cover()
    got, covered_value = lax.optimization_barrier((got, covered_value))
    if reach <= 2:
        if reach == 2:
            beyond = shift(got, 1)
            covered_value = second_cover(covered_value)
            beyond, covered_value = lax.optimization_barrier((beyond, covered_value))
            return (got, beyond), covered_value
        return (got, none), second_cover(covered_value)
    earlier, inclusive = got, combine(payload, got)
    covered = 1
    while covered < reach:
        step = covered + 1
        got = shift(inclusive, step)
        earlier = combine(earlier, got)
        covered = covered + step
        if covered < reach:
            inclusive = combine(inclusive, got)
    return (earlier, none), second_cover(covered_value)


def on_device(queries, keys, values, out_grad, norm_gain, doc_ids):
    head_count, tok_count, head_width = queries.shape
    block_count = doc_ids.shape[0]
    block_len = tok_count // block_count
    gain = norm_gain.reshape(head_count, 1, head_width)
    pair_flops = 2 * head_count * block_count * block_len * block_len * head_width
    full = jax.ShapeDtypeStruct(queries.shape, jnp.bfloat16)
    wide = jax.ShapeDtypeStruct(queries.shape, jnp.float32)
    states = jax.ShapeDtypeStruct((head_count, block_count, head_width, head_width), jnp.float32)
    payload = jax.ShapeDtypeStruct((head_count, head_width + 8, head_width), jnp.float32)
    ctx_size = lax.axis_size("ctx")
    longest_doc = ctx_size * block_count // 2
    reach = (longest_doc - 2) // block_count + 1

    local_prefix, kv_payload = per_head_call(
        functools.partial(state_kernel, block_len),
        [(keys, True), (values, True)],
        [(states, True), (payload, True)],
        pair_flops // 2,
        scalars=doc_ids,
        per_step=4,
    )
    prior, intra_part = carry(
        kv_payload,
        "ctx",
        False,
        reach,
        (
            lambda: per_head_call(
                functools.partial(intra_kernel, block_len),
                [(queries, True), (keys, True), (values, True)],
                [(wide, True)],
                2 * pair_flops,
                per_step=4,
            )[0],
            lambda intra: intra,
        ),
    )
    local_sums, preceding_states = per_head_call(
        functools.partial(forward_kernel, block_len),
        [(intra_part, True), (queries, True), (out_grad, True), (gain, True),
         (local_prefix, True), (prior[0], True), (prior[1], True)],
        [(jax.ShapeDtypeStruct((tok_count, 2), jnp.float32), False),
         (jax.ShapeDtypeStruct(states.shape, jnp.bfloat16), True)],
        pair_flops // 2,
        scalars=doc_ids,
        per_step=4,
    )
    feature_count = head_count * head_width * lax.axis_size(("sub", "head"))
    total_sums = local_sums.T.reshape(2 * tok_count)
    if lax.axis_size("head") == 2 and lax.axis_size("sub") == 2:
        partners = [
            lax.ppermute(total_sums, ("sub", "head"), [(k, k ^ flip) for k in range(4)])
            for flip in (1, 2, 3)
        ]
        total_sums = (total_sums + partners[0]) + (partners[1] + partners[2])
    else:
        total_sums = lax.psum(total_sums, ("sub", "head"))
    root_mean = jnp.sqrt(total_sums[:tok_count] / feature_count + 1e-06)
    inner_mean = total_sums[tok_count:] / feature_count
    factor = inner_mean / (root_mean * root_mean)
    coefs = jnp.stack([root_mean, factor], axis=1)
    d_attn, local_suffix, qd_payload = per_head_call(
        functools.partial(grad_kernel, block_len),
        [(queries, True), (intra_part, True), (preceding_states, True), (out_grad, True),
         (gain, True),
         (coefs, False)],
        [(full, True), (states, True), (payload, True)],
        pair_flops // 2,
        scalars=doc_ids,
    )
    half = head_count // 2

    def query_grads(heads, into):
        return per_head_call(
            functools.partial(query_grad_kernel, block_len),
            [(queries, True), (keys, True), (values, True), (d_attn, True),
             (preceding_states, True)],
            [(full, True), (wide, True), (wide, True)],
            5 * pair_flops,
            heads=heads,
            into=into,
        )

    following, (query_gradient, key_intra, value_intra) = carry(
        qd_payload,
        "ctx",
        True,
        reach,
        (
            lambda: query_grads((0, half), ()),
            lambda done: query_grads((half, head_count - half), tuple(done)),
        ),
    )
    key_gradient, value_gradient = per_head_call(
        functools.partial(key_value_grad_kernel, block_len),
        [(key_intra, True), (value_intra, True), (keys, True), (values, True),
         (local_suffix, True), (following[0], True), (following[1], True)],
        [(full, True), (full, True)],
        pair_flops,
        scalars=doc_ids,
    )
    return query_gradient, key_gradient, value_gradient


def solution(mesh):
    return jax.shard_map(
        on_device,
        mesh=mesh,
        in_specs=(
            P(("sub", "head"), ("groups", "ctx"), None),
            P(("sub", "head"), ("groups", "ctx"), None),
            P(("sub", "head"), ("groups", "ctx"), None),
            P(("sub", "head"), ("groups", "ctx"), None),
            P(("sub", "head"), None),
            P(("groups", "ctx")),
        ),
        out_specs=(
            P(("sub", "head"), ("groups", "ctx"), None),
            P(("sub", "head"), ("groups", "ctx"), None),
            P(("sub", "head"), ("groups", "ctx"), None),
        ),
        check_vma=False,
    )
```

```python
import functools
import math

import jax
import jax.numpy as jnp
from jax import lax
from jax.experimental import pallas as pl
from jax.experimental.pallas import tpu as pltpu
from jax.sharding import PartitionSpec as P

_ROWS_MINOR = (((1,), (1,)), ((), ()))
_ROWS_MAJOR = (((0,), (0,)), ((), ()))


def _causal(block_len):
    row_ids = lax.broadcasted_iota(jnp.int32, (block_len, block_len), 0)
    col_ids = lax.broadcasted_iota(jnp.int32, (block_len, block_len), 1)
    return row_ids >= col_ids


def _doc_sum(doc_ref, parts, keep):
    total = jnp.zeros_like(parts[0])
    for c in range(len(parts)):
        total = total + jnp.where(keep(c), parts[c], 0.0)
    return total


def _doc_row(doc_ref, n, shape):
    return jnp.full(shape, doc_ref[n].astype(jnp.float32) + 1.0, jnp.float32)


def _carried(state_ref, doc_ref, n, near_ref, far_ref, j):
    width = near_ref.shape[2]
    near_doc = near_ref[j, width : width + 1, :]
    carried = near_ref[j, :width, :] + jnp.where(
        near_doc == far_ref[j, width : width + 1, :], far_ref[j, :width, :], 0.0
    )
    joined = near_doc == doc_ref[n].astype(jnp.float32) + 1.0
    total = state_ref[j, n] + jnp.where(joined, carried, 0.0)
    return total.astype(jnp.bfloat16)


def state_kernel(block_len, doc_ref, k_ref, v_ref, prefix_ref, pay_ref):
    for j in range(k_ref.shape[0]):
        count = k_ref.shape[1] // block_len
        width = k_ref.shape[2]
        parts = []
        for n in range(count):
            rows = pl.ds(n * block_len, block_len)
            parts.append(
                lax.dot_general(
                    k_ref[j, rows, :], v_ref[j, rows, :], _ROWS_MAJOR,
                    preferred_element_type=jnp.float32,
                )
            )
        for b in range(count):
            prefix_ref[j, b] = _doc_sum(
                doc_ref, parts, lambda c: jnp.logical_and(c < b, doc_ref[c] == doc_ref[b])
            )
        pay_ref[j, :width, :] = _doc_sum(doc_ref, parts, lambda c: doc_ref[c] == doc_ref[count - 1])
        pay_ref[j, width:, :] = _doc_row(doc_ref, count - 1, (8, width))


def combine_kernel(near_ref, far_ref, o_ref):
    width = near_ref.shape[2]
    for h in range(near_ref.shape[0]):
        joined = near_ref[h, width : width + 1, :] == far_ref[h, width : width + 1, :]
        o_ref[h, :width, :] = near_ref[h, :width, :] + jnp.where(
            joined, far_ref[h, :width, :], 0.0
        )
        o_ref[h, width:, :] = near_ref[h, width:, :]


def intra_kernel(block_len, q_ref, k_ref, v_ref, o_ref):
    for j in range(q_ref.shape[0]):
        causal = _causal(block_len)
        for n in range(q_ref.shape[1] // block_len):
            rows = pl.ds(n * block_len, block_len)
            q, k, v = q_ref[j, rows, :], k_ref[j, rows, :], v_ref[j, rows, :]
            scores = lax.dot_general(q, k, _ROWS_MINOR, preferred_element_type=jnp.float32)
            probs = jnp.where(causal, scores, 0.0).astype(jnp.bfloat16)
            o_ref[j, rows, :] = jnp.dot(probs, v, preferred_element_type=jnp.float32)


def forward_kernel(
    block_len, doc_ref, i_ref, q_ref, g_ref, n_ref, prefix_ref, near_ref, far_ref, o_ref, s_ref
):
    @pl.when(pl.program_id(0) == 0)
    def _():
        o_ref[...] = jnp.zeros_like(o_ref)

    for j in range(q_ref.shape[0]):
        for n in range(q_ref.shape[1] // block_len):
            rows = pl.ds(n * block_len, block_len)
            state = _carried(prefix_ref, doc_ref, n, near_ref, far_ref, j)
            s_ref[j, n] = state
            raw = i_ref[j, rows, :] + jnp.dot(
                q_ref[j, rows, :], state, preferred_element_type=jnp.float32
            )
            scaled = n_ref[j] * g_ref[j, rows, :].astype(jnp.float32)
            o_ref[rows, 0:1] += jnp.sum(raw * raw, axis=1, keepdims=True)
            o_ref[rows, 1:2] += jnp.sum(scaled * raw, axis=1, keepdims=True)


def grad_kernel(
    block_len, doc_ref, q_ref, i_ref, s_ref, g_ref, n_ref, c_ref, d_ref, suffix_ref, pay_ref
):
    for j in range(q_ref.shape[0]):
        count = q_ref.shape[1] // block_len
        width = q_ref.shape[2]
        parts = []
        for n in range(count):
            rows = pl.ds(n * block_len, block_len)
            q = q_ref[j, rows, :]
            raw = i_ref[j, rows, :] + jnp.dot(q, s_ref[j, n], preferred_element_type=jnp.float32)
            scaled = n_ref[j] * g_ref[j, rows, :].astype(jnp.float32)
            root_mean = c_ref[rows, 0:1]
            factor = c_ref[rows, 1:2]
            d = ((scaled - raw * factor) / root_mean).astype(jnp.bfloat16)
            d_ref[j, rows, :] = d
            parts.append(lax.dot_general(q, d, _ROWS_MAJOR, preferred_element_type=jnp.float32))
        for b in range(count):
            suffix_ref[j, b] = _doc_sum(
                doc_ref, parts, lambda c: jnp.logical_and(c > b, doc_ref[c] == doc_ref[b])
            )
        pay_ref[j, :width, :] = _doc_sum(doc_ref, parts, lambda c: doc_ref[c] == doc_ref[0])
        pay_ref[j, width:, :] = _doc_row(doc_ref, 0, (8, width))


def query_grad_kernel(block_len, q_ref, k_ref, v_ref, d_ref, s_ref, dq_ref, dk_ref, dv_ref):
    for j in range(q_ref.shape[0]):
        causal = _causal(block_len)
        for n in range(k_ref.shape[1] // block_len):
            rows = pl.ds(n * block_len, block_len)
            q, k, v = q_ref[j, rows, :], k_ref[j, rows, :], v_ref[j, rows, :]
            d = d_ref[j, rows, :]
            scores = lax.dot_general(q, k, _ROWS_MINOR, preferred_element_type=jnp.float32)
            probs = jnp.where(causal, scores, 0.0).astype(jnp.bfloat16)
            grad_scores = lax.dot_general(d, v, _ROWS_MINOR, preferred_element_type=jnp.float32)
            grad_probs = jnp.where(causal, grad_scores, 0.0).astype(jnp.bfloat16)
            dq = jnp.dot(grad_probs, k, preferred_element_type=jnp.float32)
            dq = dq + lax.dot_general(d, s_ref[j, n], _ROWS_MINOR, preferred_element_type=jnp.float32)
            dq_ref[j, rows, :] = dq.astype(dq_ref.dtype)
            dk_ref[j, rows, :] = lax.dot_general(
                grad_probs, q, _ROWS_MAJOR, preferred_element_type=jnp.float32
            )
            dv_ref[j, rows, :] = lax.dot_general(
                probs, d, _ROWS_MAJOR, preferred_element_type=jnp.float32
            )


def key_value_grad_kernel(
    block_len, doc_ref, ik_ref, iv_ref, k_ref, v_ref, suffix_ref, near_ref, far_ref, dk_ref,
    dv_ref,
):
    for j in range(ik_ref.shape[0]):
        for n in range(k_ref.shape[1] // block_len):
            rows = pl.ds(n * block_len, block_len)
            state = _carried(suffix_ref, doc_ref, n, near_ref, far_ref, j)
            dk = ik_ref[j, rows, :] + lax.dot_general(
                v_ref[j, rows, :], state, _ROWS_MINOR, preferred_element_type=jnp.float32
            )
            dv = iv_ref[j, rows, :] + jnp.dot(
                k_ref[j, rows, :], state, preferred_element_type=jnp.float32
            )
            dk_ref[j, rows, :] = dk.astype(dk_ref.dtype)
            dv_ref[j, rows, :] = dv.astype(dv_ref.dtype)


def per_head_call(
    kernel, inputs, outputs, flops, heads=None, into=(), scalars=None, per_step=2
):
    head_count = inputs[0][0].shape[0]
    first, count = heads if heads is not None else (0, head_count)
    group = math.gcd(math.gcd(first, count), per_step)

    def spec(shape, per_head, first):
        if per_head:
            return pl.BlockSpec(
                (group,) + shape[1:],
                lambda h, *_: (h + first // group,) + (0,) * (len(shape) - 1),
            )
        return pl.BlockSpec(shape, lambda h, *_: (0,) * len(shape))

    share = count / head_count
    in_bytes = sum(x.size * x.dtype.itemsize for x, _ in inputs) * share
    out_bytes = sum(math.prod(o.shape) * o.dtype.itemsize for o, _ in outputs) * share
    lead = 0 if scalars is None else 1
    skip = lead + len(inputs)

    def body(*refs):
        kernel(*refs[:skip], *refs[skip + len(into):])

    grid_spec = pltpu.PrefetchScalarGridSpec(
        num_scalar_prefetch=lead,
        grid=(count // group,),
        in_specs=[spec(x.shape, h, first) for x, h in inputs]
        + [pl.BlockSpec(memory_space=pl.ANY) for _ in into],
        out_specs=[spec(o.shape, h, first) for o, h in outputs],
    )
    return pl.pallas_call(
        body,
        grid_spec=grid_spec,
        out_shape=[o for o, _ in outputs],
        input_output_aliases={skip + i: i for i in range(len(into))},
        cost_estimate=pl.CostEstimate(
            flops=int(flops * share), transcendentals=0,
            bytes_accessed=int(in_bytes + out_bytes),
        ),
    )(*([] if scalars is None else [scalars]), *[x for x, _ in inputs], *into)


def combine(near, far):
    return pl.pallas_call(
        combine_kernel,
        out_shape=jax.ShapeDtypeStruct(near.shape, near.dtype),
        cost_estimate=pl.CostEstimate(
            flops=2 * near.size, transcendentals=0, bytes_accessed=3 * near.size * 4
        ),
    )(near, far)


def carry(payload, axis, reverse, reach, cover):
    peers = lax.axis_size(axis)
    reach = min(reach, peers - 1)

    def shift(value, step):
        if reverse:
            pairs = [(j, j - step) for j in range(step, peers)]
        else:
            pairs = [(j, j + step) for j in range(peers - step)]
        return lax.ppermute(value, axis, pairs)

    first_cover, second_cover = cover
    none = jnp.zeros_like(payload)
    if reach < 1:
        return (none, none), second_cover(first_cover())
    got = shift(payload, 1)
    covered_value = first_cover()
    got, covered_value = lax.optimization_barrier((got, covered_value))
    if reach <= 2:
        if reach == 2:
            beyond = shift(got, 1)
            covered_value = second_cover(covered_value)
            beyond, covered_value = lax.optimization_barrier((beyond, covered_value))
            return (got, beyond), covered_value
        return (got, none), second_cover(covered_value)
    earlier, inclusive = got, combine(payload, got)
    covered = 1
    while covered < reach:
        step = covered + 1
        got = shift(inclusive, step)
        earlier = combine(earlier, got)
        covered = covered + step
        if covered < reach:
            inclusive = combine(inclusive, got)
    return (earlier, none), second_cover(covered_value)


def on_device(queries, keys, values, out_grad, norm_gain, doc_ids):
    head_count, tok_count, head_width = queries.shape
    block_count = doc_ids.shape[0]
    block_len = tok_count // block_count
    gain = norm_gain.reshape(head_count, 1, head_width)
    pair_flops = 2 * head_count * block_count * block_len * block_len * head_width
    full = jax.ShapeDtypeStruct(queries.shape, jnp.bfloat16)
    wide = jax.ShapeDtypeStruct(queries.shape, jnp.float32)
    states = jax.ShapeDtypeStruct((head_count, block_count, head_width, head_width), jnp.float32)
    payload = jax.ShapeDtypeStruct((head_count, head_width + 8, head_width), jnp.float32)
    ctx_size = lax.axis_size("ctx")
    longest_doc = ctx_size * block_count // 2
    reach = (longest_doc - 2) // block_count + 1

    local_prefix, kv_payload = per_head_call(
        functools.partial(state_kernel, block_len),
        [(keys, True), (values, True)],
        [(states, True), (payload, True)],
        pair_flops // 2,
        scalars=doc_ids,
        per_step=8,
    )
    prior, intra_part = carry(
        kv_payload,
        "ctx",
        False,
        reach,
        (
            lambda: per_head_call(
                functools.partial(intra_kernel, block_len),
                [(queries, True), (keys, True), (values, True)],
                [(wide, True)],
                2 * pair_flops,
                per_step=4,
            )[0],
            lambda intra: intra,
        ),
    )
    local_sums, preceding_states = per_head_call(
        functools.partial(forward_kernel, block_len),
        [(intra_part, True), (queries, True), (out_grad, True), (gain, True),
         (local_prefix, True), (prior[0], True), (prior[1], True)],
        [(jax.ShapeDtypeStruct((tok_count, 2), jnp.float32), False),
         (jax.ShapeDtypeStruct(states.shape, jnp.bfloat16), True)],
        pair_flops // 2,
        scalars=doc_ids,
        per_step=4,
    )
    feature_count = head_count * head_width * lax.axis_size(("sub", "head"))
    total_sums = local_sums.T.reshape(2 * tok_count)
    if lax.axis_size("head") == 2 and lax.axis_size("sub") == 2:
        partners = [
            lax.ppermute(total_sums, ("sub", "head"), [(k, k ^ flip) for k in range(4)])
            for flip in (1, 2, 3)
        ]
        total_sums = (total_sums + partners[0]) + (partners[1] + partners[2])
    else:
        total_sums = lax.psum(total_sums, ("sub", "head"))
    root_mean = jnp.sqrt(total_sums[:tok_count] / feature_count + 1e-06)
    inner_mean = total_sums[tok_count:] / feature_count
    factor = inner_mean / (root_mean * root_mean)
    coefs = jnp.stack([root_mean, factor], axis=1)
    d_attn, local_suffix, qd_payload = per_head_call(
        functools.partial(grad_kernel, block_len),
        [(queries, True), (intra_part, True), (preceding_states, True), (out_grad, True),
         (gain, True),
         (coefs, False)],
        [(full, True), (states, True), (payload, True)],
        pair_flops // 2,
        scalars=doc_ids,
    )
    half = head_count // 2

    def query_grads(heads, into):
        return per_head_call(
            functools.partial(query_grad_kernel, block_len),
            [(queries, True), (keys, True), (values, True), (d_attn, True),
             (preceding_states, True)],
            [(full, True), (wide, True), (wide, True)],
            5 * pair_flops,
            heads=heads,
            into=into,
        )

    following, (query_gradient, key_intra, value_intra) = carry(
        qd_payload,
        "ctx",
        True,
        reach,
        (
            lambda: query_grads((0, half), ()),
            lambda done: query_grads((half, head_count - half), tuple(done)),
        ),
    )
    key_gradient, value_gradient = per_head_call(
        functools.partial(key_value_grad_kernel, block_len),
        [(key_intra, True), (value_intra, True), (keys, True), (values, True),
         (local_suffix, True), (following[0], True), (following[1], True)],
        [(full, True), (full, True)],
        pair_flops,
        scalars=doc_ids,
    )
    return query_gradient, key_gradient, value_gradient


def solution(mesh):
    return jax.shard_map(
        on_device,
        mesh=mesh,
        in_specs=(
            P(("sub", "head"), ("groups", "ctx"), None),
            P(("sub", "head"), ("groups", "ctx"), None),
            P(("sub", "head"), ("groups", "ctx"), None),
            P(("sub", "head"), ("groups", "ctx"), None),
            P(("sub", "head"), None),
            P(("groups", "ctx")),
        ),
        out_specs=(
            P(("sub", "head"), ("groups", "ctx"), None),
            P(("sub", "head"), ("groups", "ctx"), None),
            P(("sub", "head"), ("groups", "ctx"), None),
        ),
        check_vma=False,
    )
```
